32 devices in a mesh: groups: 2 (over y), ctx: 4 (over z), head: 2 (over x), rep: 2 (over core).
Axes of the slice: x: 2, y: 2, z: 4, core: 2. Of those that a mesh axis runs over, the one named last changes fastest.
Arguments:
- queries: bfloat16 [2048, 8192], P(('groups', 'rep'), 'head'), parts along dimension 0, may hold values from -6 to 6
- cached_keys: bfloat16 [32768, 1024], P(('groups', 'ctx'), 'head'), parts along dimension 0, may hold values from -6 to 6
- cached_values: bfloat16 [32768, 1024], P(('groups', 'ctx'), 'head'), parts along dimension 0, may hold values from -6 to 6
- pattern: int32 [16, 16], P(('groups', 'rep')), parts along dimension 0, may hold values from 0 to 127, as said below
- out_weight: bfloat16 [8192, 8192], P('head', 'ctx'), may hold values from -1.1953125 to 1.1953125
Outputs:
- projected: bfloat16 [2048, 8192], P(('groups', 'rep'), ('ctx', 'head')), parts along dimension 0
The draws below stay inside these ranges and needn't reach their ends.
There are 2 independent parts, one for each index of `groups`. The reference program is written for one: setup_inputs(seed, part) draws one part's arguments, and reference() takes and returns one part's arrays. A program takes and returns all parts, laid end to end along the dimension named above; an argument that names none is the same for every part. Nothing has to cross between parts.
Inputs may be any that keep to these rules, and one draw needn't show every extreme that they name: Each row of pattern names 16 different key blocks; no row names more than 8 blocks among blocks k * 32 to (k + 1) * 32 - 1 for any k, and every row names exactly 8 in some such range.
All inputs are finite; a program needn't handle non-finite values.
Results may differ from the reference program's by a relative error of at most 0.0055.
Values may be sent and summed in bfloat16 or wider, within the bound.
No kernel may reach another device: no remote copies, remote signals or barrier semaphores. Data moves between devices by JAX's collectives and lax.ppermute only.
A program may use at most 128 MiB of HBM per device.

```python
import jax
import jax.numpy as jnp
from jax import lax

D = 8192
HEADS = 64
KV_HEADS = 8
HEAD_DIM = 128
BLOCK = 128
KB_DEV = 32
QB = 8
Q_TOK = 1024
KBLOCKS = 128
TOPK = 16
CAP = 8
N_CTX = 4


def draw_queries(key, part):
    first_key = jax.random.fold_in(jax.random.fold_in(key, 3), 0)
    base = jnp.clip(5.0 * jax.random.normal(first_key, (Q_TOK, HEADS, HEAD_DIM), jnp.float32), -6.0, 6.0)
    return base.reshape(Q_TOK, HEADS * HEAD_DIM).astype(jnp.bfloat16)


def draw_cached_keys(key, part):
    total_rows = KBLOCKS * BLOCK
    first_key = jax.random.fold_in(jax.random.fold_in(key, 5), 0)
    base = jnp.clip(0.3 * jax.random.normal(first_key, (total_rows, KV_HEADS, HEAD_DIM), jnp.float32), -6.0, 6.0)
    return base.reshape(total_rows, KV_HEADS * HEAD_DIM).astype(jnp.bfloat16)


def draw_pattern(key, part):
    hot_key, slot_key, order_key = jax.random.split(jax.random.fold_in(key, 9), 3)
    hot_shard = jax.random.randint(hot_key, (QB, 1, 1), 0, N_CTX)
    shard_ids = jnp.arange(N_CTX, dtype=jnp.int32)[None, :, None]
    block_scores = jax.random.randint(order_key, (QB, N_CTX, KB_DEV), 0, 1 << 20) * KB_DEV + jnp.arange(KB_DEV, dtype=jnp.int32)[None, None, :]
    shuffled = jnp.argsort(block_scores, axis=-1).astype(jnp.int32)[:, :, :CAP]
    block_ids = shard_ids * KB_DEV + shuffled
    slot_draws = jax.random.randint(slot_key, (QB, N_CTX, CAP), 0, 1 << 16) + 1
    slot_rank = jnp.where(shard_ids == hot_shard, 0, slot_draws) * (N_CTX * CAP)
    slot_rank = slot_rank + jnp.arange(N_CTX * CAP, dtype=jnp.int32).reshape(1, N_CTX, CAP)
    picked = jnp.argsort(slot_rank.reshape(QB, N_CTX * CAP), axis=-1).astype(jnp.int32)[:, :TOPK]
    return jnp.take_along_axis(block_ids.reshape(QB, N_CTX * CAP), picked, axis=1).astype(jnp.int32)


def levels(key, extent, pieces, smallest, high):
    def one(dim, shards_of):
        heights = jax.random.uniform(jax.random.fold_in(jax.random.fold_in(key, 6), dim), (shards_of,), jnp.float32, smallest / len(pieces), high / len(pieces))
        return jnp.repeat(jnp.exp(heights), extent[dim] // shards_of).reshape((-1,) + (1,) * (len(extent) - dim - 1))

    loudness = one(*pieces[0])
    for cut in pieces[1:]:
        loudness = loudness * one(*cut)
    return loudness


def gaussian(rng, shape, spread, bound, cuts=(), kind=jnp.bfloat16):
    values = jax.random.normal(rng, shape, jnp.float32) * spread
    if len(cuts) > 0:
        values = levels(rng, shape, cuts, -0.22, 0.18) * values
    return jnp.clip(values, min=-bound, max=bound).astype(kind)


def setup_inputs(seed: int = 0, part: int = 0) -> dict:
    seeds = jax.random.split(jax.random.key(seed), 6)
    part_splits = jax.random.split(jax.random.fold_in(seeds[5], part), 6)
    queries = draw_queries(jax.random.fold_in(jax.random.fold_in(seeds[5], part), 71), part)
    cached_keys = draw_cached_keys(jax.random.fold_in(jax.random.fold_in(seeds[5], part), 71), part)
    cached_values = gaussian(part_splits[2], (KBLOCKS * BLOCK, KV_HEADS * HEAD_DIM), 1.0, 6.0, ((0, 4), (1, 2)))
    pattern = draw_pattern(jax.random.fold_in(jax.random.fold_in(seeds[5], part), 71), part)
    out_weight = gaussian(seeds[4], (HEADS * HEAD_DIM, D), 0.2, 1.1953125, ((0, 2), (1, 4)))
    return {"queries": queries, "cached_keys": cached_keys, "cached_values": cached_values, "pattern": pattern, "out_weight": out_weight}


def reference(queries, cached_keys, cached_values, pattern, out_weight):
    group_size = HEADS // KV_HEADS
    score_scale = HEAD_DIM ** -0.5
    key_blocks = cached_keys.reshape(KBLOCKS, BLOCK, KV_HEADS, HEAD_DIM)
    value_blocks = cached_values.reshape(KBLOCKS, BLOCK, KV_HEADS, HEAD_DIM)
    query_blocks = queries.reshape(QB, BLOCK, KV_HEADS, group_size, HEAD_DIM)
    segment_ids = jnp.arange(N_CTX, dtype=jnp.int32)

    def attend(inputs):
        query_block, chosen = inputs
        keys_sel = key_blocks[chosen].astype(jnp.float32)
        values_sel = value_blocks[chosen].astype(jnp.float32)
        scores = jnp.einsum('rkgd,tskd->kgrts', query_block.astype(jnp.float32), keys_sel) * score_scale
        block_top = scores.max(axis=-1)
        segment = (chosen // KB_DEV).astype(jnp.int32)
        member = segment[:, None] == segment_ids[None, :]
        seg_max = jnp.max(jnp.where(member, block_top[..., None], jnp.float32(-1e30)), axis=-2)
        key_max = jnp.take(seg_max, segment, axis=-1)
        shifted = jnp.exp(scores - key_max[..., None])
        probs = shifted.astype(jnp.bfloat16)
        block_total = shifted.sum(axis=-1)
        block_out = jnp.einsum('kgrts,tskd->kgrtd', probs.astype(jnp.float32), values_sel)
        row_max = seg_max.max(axis=-1)
        rescale = jnp.exp(key_max - row_max[..., None])
        numer = jnp.sum(block_out * rescale[..., None], axis=3)
        denom = jnp.sum(block_total * rescale, axis=3)
        result = numer / denom[..., None]
        return result.transpose(2, 0, 1, 3).reshape(BLOCK, HEADS * HEAD_DIM).astype(jnp.bfloat16)

    attended = lax.map(attend, (query_blocks, pattern)).reshape(Q_TOK, HEADS * HEAD_DIM)
    return jnp.dot(attended, out_weight, preferred_element_type=jnp.float32).astype(jnp.bfloat16)
```

```python
import jax
import jax.numpy as jnp
from jax import lax
from jax.sharding import PartitionSpec as P

HEADS = 64
KV_HEADS = 8
HEAD_DIM = 128
BLOCK = 128
CAP = 8


def shards(queries, cached_keys, cached_values, pattern, out_weight):
    shard_index = lax.axis_index("ctx")
    head_index = lax.axis_index("head")
    query_count, query_width = queries.shape
    cache_rows, cache_width = cached_keys.shape
    heads_kv = cache_width // HEAD_DIM
    group_size = HEADS // KV_HEADS
    heads_here = heads_kv * group_size
    local_blocks = cache_rows // BLOCK
    score_scale = HEAD_DIM ** (-0.5)
    key_blocks = cached_keys.reshape(local_blocks, BLOCK, cache_width)
    value_blocks = cached_values.reshape(local_blocks, BLOCK, cache_width)
    query_blocks = queries.reshape(query_count // BLOCK, BLOCK, heads_kv, group_size, HEAD_DIM)
    slot_ids = jnp.arange(CAP, dtype=jnp.int32)

    def attend(inputs):
        query_block, chosen_list = inputs
        local_block = chosen_list - shard_index * local_blocks
        in_shard = (local_block >= 0) & (local_block < local_blocks)
        slot_rank = jnp.cumsum(in_shard.astype(jnp.int32)) - 1
        picked = in_shard[:, None] & (slot_rank[:, None] == slot_ids[None, :])
        chosen = jnp.sum(jnp.where(picked, local_block[:, None], 0), axis=0)
        slot_live = jnp.any(picked, axis=0)
        key_block = key_blocks[chosen].reshape(CAP * BLOCK, heads_kv, HEAD_DIM)
        value_block = value_blocks[chosen].reshape(CAP * BLOCK, heads_kv, HEAD_DIM)
        scores = (
            jnp.einsum("rkgd,skd->kgrs", query_block, key_block, preferred_element_type=jnp.float32)
            * score_scale
        )
        key_live = jnp.repeat(slot_live, BLOCK)
        masked = jnp.where(key_live, scores, jnp.float32(-1e30))
        row_top = masked.max(axis=-1)
        weights = jnp.where(key_live, jnp.exp(masked - row_top[..., None]), 0.0)
        row_total = weights.sum(axis=-1)
        mixed = jnp.einsum(
            "kgrs,skd->rkgd",
            weights.astype(jnp.bfloat16),
            value_block,
            preferred_element_type=jnp.float32,
        )
        return (
            mixed.reshape(BLOCK, heads_here, HEAD_DIM),
            row_top.transpose(2, 0, 1).reshape(BLOCK, heads_here),
            row_total.transpose(2, 0, 1).reshape(BLOCK, heads_here),
        )

    mixed_all, top_all, total_all = lax.map(attend, (query_blocks, pattern))
    mixed_all = mixed_all.reshape(query_count, heads_here, HEAD_DIM)
    top_all = top_all.reshape(query_count, heads_here)
    total_all = total_all.reshape(query_count, heads_here)
    row_peak = lax.pmax(top_all, "ctx")
    rescale = jnp.exp(top_all - row_peak)
    scaled = (mixed_all * rescale[..., None]).reshape(query_count, query_width)
    summed = lax.psum_scatter(scaled, "ctx", scatter_dimension=0, tiled=True)
    row_norm = lax.psum_scatter(total_all * rescale, "ctx", scatter_dimension=0, tiled=True)
    rows_here = summed.shape[0]
    attended = (
        summed.reshape(rows_here, heads_here, HEAD_DIM) / row_norm[:, :, None]
    ).reshape(rows_here, query_width).astype(jnp.bfloat16)
    partial_out = jnp.dot(
        lax.all_gather(attended, "ctx", axis=0, tiled=True),
        out_weight,
        preferred_element_type=jnp.float32,
    )
    heads_n = lax.axis_size("head")
    share = partial_out.shape[1] // heads_n
    if heads_n == 2:
        kept = lax.dynamic_slice_in_dim(partial_out, head_index * share, share, axis=1)
        sent = lax.dynamic_slice_in_dim(partial_out, (1 - head_index) * share, share, axis=1)
        got = lax.ppermute(sent.astype(jnp.bfloat16), "head", perm=[(0, 1), (1, 0)])
        return (kept + got.astype(jnp.float32)).astype(jnp.bfloat16)
    pieces = partial_out.reshape(query_count, heads_n, share).transpose(1, 0, 2)
    got = lax.all_to_all(pieces.astype(jnp.bfloat16), "head", 0, 0, tiled=True)
    return got.astype(jnp.float32).sum(axis=0).astype(jnp.bfloat16)

def solution(mesh):
    return jax.shard_map(
        shards,
        mesh=mesh,
        in_specs=(
            P(("groups", "rep"), "head"),
            P(("groups", "ctx"), "head"),
            P(("groups", "ctx"), "head"),
            P(("groups", "rep"), None),
            P("head", "ctx"),
        ),
        out_specs=P(("groups", "rep"), ("ctx", "head")),
        check_vma=False,
    )
```

```python
import jax
import jax.numpy as jnp
from jax import lax
from jax.sharding import PartitionSpec as P

HEADS = 64
KV_HEADS = 8
HEAD_DIM = 128
BLOCK = 128
CAP = 8


def shards(queries, cached_keys, cached_values, pattern, out_weight):
    shard_index = lax.axis_index("ctx")
    head_index = lax.axis_index("head")
    query_count, query_width = queries.shape
    cache_rows, cache_width = cached_keys.shape
    heads_kv = cache_width // HEAD_DIM
    group_size = HEADS // KV_HEADS
    heads_here = heads_kv * group_size
    local_blocks = cache_rows // BLOCK
    score_scale = HEAD_DIM ** (-0.5)
    key_blocks = cached_keys.reshape(local_blocks, BLOCK, cache_width)
    value_blocks = cached_values.reshape(local_blocks, BLOCK, cache_width)
    query_blocks = queries.reshape(query_count // BLOCK, BLOCK, heads_kv, group_size, HEAD_DIM)
    slot_ids = jnp.arange(CAP, dtype=jnp.int32)

    def attend(inputs):
        query_block, chosen_list = inputs
        local_block = chosen_list - shard_index * local_blocks
        in_shard = (local_block >= 0) & (local_block < local_blocks)
        slot_rank = jnp.cumsum(in_shard.astype(jnp.int32)) - 1
        picked = in_shard[:, None] & (slot_rank[:, None] == slot_ids[None, :])
        chosen = jnp.sum(jnp.where(picked, local_block[:, None], 0), axis=0)
        slot_live = jnp.any(picked, axis=0)
        key_block = key_blocks[chosen].reshape(CAP * BLOCK, heads_kv, HEAD_DIM)
        value_block = value_blocks[chosen].reshape(CAP * BLOCK, heads_kv, HEAD_DIM)
        scores = (
            jnp.einsum("rkgd,skd->kgrs", query_block, key_block, preferred_element_type=jnp.float32)
            * score_scale
        )
        key_live = jnp.repeat(slot_live, BLOCK)
        masked = jnp.where(key_live, scores, jnp.float32(-1e30))
        row_top = masked.max(axis=-1)
        weights = jnp.where(key_live, jnp.exp(masked - row_top[..., None]), 0.0)
        row_total = weights.sum(axis=-1)
        mixed = jnp.einsum(
            "kgrs,skd->rkgd",
            weights.astype(jnp.bfloat16),
            value_block,
            preferred_element_type=jnp.float32,
        )
        return (
            mixed.reshape(BLOCK, heads_here, HEAD_DIM),
            row_top.transpose(2, 0, 1).reshape(BLOCK, heads_here),
            row_total.transpose(2, 0, 1).reshape(BLOCK, heads_here),
        )

    mixed_all, top_all, total_all = lax.map(attend, (query_blocks, pattern))
    mixed_all = mixed_all.reshape(query_count, heads_here, HEAD_DIM)
    top_all = top_all.reshape(query_count, heads_here)
    total_all = total_all.reshape(query_count, heads_here)
    ctx_n = lax.axis_size("ctx")
    row_peak = top_all
    if ctx_n & (ctx_n - 1) == 0:
        step = 1
        while step < ctx_n:
            pairs = [(src, src ^ step) for src in range(ctx_n)]
            row_peak = jnp.maximum(row_peak, lax.ppermute(row_peak, "ctx", perm=pairs))
            step *= 2
    else:
        row_peak = lax.pmax(top_all, "ctx")
    rescale = jnp.exp(top_all - row_peak)
    scaled = (mixed_all * rescale[..., None]).astype(jnp.bfloat16).reshape(query_count, query_width)
    summed = lax.psum_scatter(scaled, "ctx", scatter_dimension=0, tiled=True)
    row_norm = lax.psum_scatter(total_all * rescale, "ctx", scatter_dimension=0, tiled=True)
    rows_here = summed.shape[0]
    attended = (
        summed.astype(jnp.float32).reshape(rows_here, heads_here, HEAD_DIM) / row_norm[:, :, None]
    ).reshape(rows_here, query_width).astype(jnp.bfloat16)
    partial_out = jnp.dot(
        lax.all_gather(attended, "ctx", axis=0, tiled=True),
        out_weight,
        preferred_element_type=jnp.float32,
    )
    heads_n = lax.axis_size("head")
    share = partial_out.shape[1] // heads_n
    if heads_n == 2:
        kept = lax.dynamic_slice_in_dim(partial_out, head_index * share, share, axis=1)
        sent = lax.dynamic_slice_in_dim(partial_out, (1 - head_index) * share, share, axis=1)
        got = lax.ppermute(sent.astype(jnp.bfloat16), "head", perm=[(0, 1), (1, 0)])
        return (kept + got.astype(jnp.float32)).astype(jnp.bfloat16)
    pieces = partial_out.reshape(query_count, heads_n, share).transpose(1, 0, 2)
    got = lax.all_to_all(pieces.astype(jnp.bfloat16), "head", 0, 0, tiled=True)
    return got.astype(jnp.float32).sum(axis=0).astype(jnp.bfloat16)

def solution(mesh):
    return jax.shard_map(
        shards,
        mesh=mesh,
        in_specs=(
            P(("groups", "rep"), "head"),
            P(("groups", "ctx"), "head"),
            P(("groups", "ctx"), "head"),
            P(("groups", "rep"), None),
            P("head", "ctx"),
        ),
        out_specs=P(("groups", "rep"), ("ctx", "head")),
        check_vma=False,
    )
```

```python
import jax
import jax.numpy as jnp
from jax import lax
from jax.sharding import PartitionSpec as P

HEADS = 64
KV_HEADS = 8
HEAD_DIM = 128
BLOCK = 128
CAP = 8


def shards(queries, cached_keys, cached_values, pattern, out_weight):
    shard_index = lax.axis_index("ctx")
    head_index = lax.axis_index("head")
    query_count, query_width = queries.shape
    cache_rows, cache_width = cached_keys.shape
    heads_kv = cache_width // HEAD_DIM
    group_size = HEADS // KV_HEADS
    heads_here = heads_kv * group_size
    local_blocks = cache_rows // BLOCK
    score_scale = HEAD_DIM ** (-0.5)
    key_blocks = cached_keys.reshape(local_blocks, BLOCK, cache_width)
    value_blocks = cached_values.reshape(local_blocks, BLOCK, cache_width)
    query_blocks = queries.reshape(query_count // BLOCK, BLOCK, heads_kv, group_size, HEAD_DIM)
    slot_ids = jnp.arange(CAP, dtype=jnp.int32)

    def attend(inputs):
        query_block, chosen_list = inputs
        local_block = chosen_list - shard_index * local_blocks
        in_shard = (local_block >= 0) & (local_block < local_blocks)
        slot_rank = jnp.cumsum(in_shard.astype(jnp.int32)) - 1
        picked = in_shard[:, None] & (slot_rank[:, None] == slot_ids[None, :])
        chosen = jnp.sum(jnp.where(picked, local_block[:, None], 0), axis=0)
        slot_live = jnp.any(picked, axis=0)
        key_block = key_blocks[chosen].reshape(CAP * BLOCK, heads_kv, HEAD_DIM)
        value_block = value_blocks[chosen].reshape(CAP * BLOCK, heads_kv, HEAD_DIM)
        scores = (
            jnp.einsum("rkgd,skd->kgrs", query_block, key_block, preferred_element_type=jnp.float32)
            * score_scale
        )
        key_live = jnp.repeat(slot_live, BLOCK)
        masked = jnp.where(key_live, scores, jnp.float32(-1e30))
        row_top = masked.max(axis=-1)
        weights = jnp.where(key_live, jnp.exp(masked - row_top[..., None]), 0.0)
        row_total = weights.sum(axis=-1)
        mixed = jnp.einsum(
            "kgrs,skd->rkgd",
            weights.astype(jnp.bfloat16),
            value_block,
            preferred_element_type=jnp.float32,
        )
        return (
            mixed.reshape(BLOCK, heads_here, HEAD_DIM),
            row_top.transpose(2, 0, 1).reshape(BLOCK, heads_here),
            row_total.transpose(2, 0, 1).reshape(BLOCK, heads_here),
        )

    mixed_all, top_all, total_all = lax.map(attend, (query_blocks, pattern))
    mixed_all = mixed_all.reshape(query_count, heads_here, HEAD_DIM)
    top_all = top_all.reshape(query_count, heads_here)
    total_all = total_all.reshape(query_count, heads_here)
    ctx_n = lax.axis_size("ctx")
    row_peak = top_all
    if ctx_n & (ctx_n - 1) == 0:
        step = 1
        while step < ctx_n:
            pairs = [(src, src ^ step) for src in range(ctx_n)]
            row_peak = jnp.maximum(row_peak, lax.ppermute(row_peak, "ctx", perm=pairs))
            step *= 2
    else:
        row_peak = lax.pmax(top_all, "ctx")
    rescale = jnp.exp(top_all - row_peak)
    scaled = (mixed_all * rescale[..., None]).astype(jnp.bfloat16).reshape(query_count, query_width)
    got_parts = lax.all_to_all(scaled, "ctx", split_axis=0, concat_axis=0, tiled=True)
    summed = got_parts.reshape(ctx_n, -1, query_width).astype(jnp.float32).sum(axis=0)
    row_norm = lax.psum_scatter(total_all * rescale, "ctx", scatter_dimension=0, tiled=True)
    rows_here = summed.shape[0]
    attended = (
        summed.reshape(rows_here, heads_here, HEAD_DIM) / row_norm[:, :, None]
    ).reshape(rows_here, query_width).astype(jnp.bfloat16)
    partial_out = jnp.dot(
        lax.all_gather(attended, "ctx", axis=0, tiled=True),
        out_weight,
        preferred_element_type=jnp.float32,
    )
    heads_n = lax.axis_size("head")
    share = partial_out.shape[1] // heads_n
    if heads_n == 2:
        kept = lax.dynamic_slice_in_dim(partial_out, head_index * share, share, axis=1)
        sent = lax.dynamic_slice_in_dim(partial_out, (1 - head_index) * share, share, axis=1)
        got = lax.ppermute(sent.astype(jnp.bfloat16), "head", perm=[(0, 1), (1, 0)])
        return (kept + got.astype(jnp.float32)).astype(jnp.bfloat16)
    pieces = partial_out.reshape(query_count, heads_n, share).transpose(1, 0, 2)
    got = lax.all_to_all(pieces.astype(jnp.bfloat16), "head", 0, 0, tiled=True)
    return got.astype(jnp.float32).sum(axis=0).astype(jnp.bfloat16)

def solution(mesh):
    return jax.shard_map(
        shards,
        mesh=mesh,
        in_specs=(
            P(("groups", "rep"), "head"),
            P(("groups", "ctx"), "head"),
            P(("groups", "ctx"), "head"),
            P(("groups", "rep"), None),
            P("head", "ctx"),
        ),
        out_specs=P(("groups", "rep"), ("ctx", "head")),
        check_vma=False,
    )
```

```python
import jax
import jax.numpy as jnp
from jax import lax
from jax.experimental import pallas as pl
from jax.experimental.pallas import tpu as pltpu
from jax.sharding import PartitionSpec as P

HEADS = 64
KV_HEADS = 8
HEAD_DIM = 128
BLOCK = 128
CAP = 8


def attend_kernel(chosen_ref, live_ref, q_ref, k_hbm, v_hbm, o_ref, m_ref, l_ref, kbuf, vbuf, sem):
    b = pl.program_id(0)
    kv = pl.program_id(1)
    group_size = q_ref.shape[1] // HEAD_DIM
    copies = []
    for j in range(CAP):
        rows = pl.ds(pl.multiple_of(chosen_ref[b, j] * BLOCK, BLOCK), BLOCK)
        cols = pl.ds(pl.multiple_of(kv * HEAD_DIM, HEAD_DIM), HEAD_DIM)
        dst = pl.ds(j * BLOCK, BLOCK)
        copies.append(pltpu.make_async_copy(k_hbm.at[rows, cols], kbuf.at[dst], sem.at[0, j]))
        copies.append(pltpu.make_async_copy(v_hbm.at[rows, cols], vbuf.at[dst], sem.at[1, j]))
    for c in copies:
        c.start()
    q = q_ref[...]
    stacked = jnp.concatenate([q[:, g * HEAD_DIM:(g + 1) * HEAD_DIM] for g in range(group_size)], axis=0)
    for c in copies[0::2]:
        c.wait()
    scores = lax.dot_general(
        stacked, kbuf[...], (((1,), (1,)), ((), ())), preferred_element_type=jnp.float32
    ) * (HEAD_DIM ** (-0.5))
    key_slot = lax.broadcasted_iota(jnp.int32, (1, CAP * BLOCK), 1) // BLOCK
    live_keys = key_slot < 0
    for j in range(CAP):
        live_keys = live_keys | ((key_slot == j) & (live_ref[b, j] > 0))
    scores = jnp.where(live_keys, scores, jnp.float32(-1e30))
    top = jnp.max(scores, axis=1, keepdims=True)
    weights = jnp.exp(scores - top)
    total = jnp.sum(weights, axis=1, keepdims=True)
    for c in copies[1::2]:
        c.wait()
    mixed = jnp.dot(weights.astype(jnp.bfloat16), vbuf[...], preferred_element_type=jnp.float32)
    for g in range(group_size):
        o_ref[:, g * HEAD_DIM:(g + 1) * HEAD_DIM] = mixed[g * BLOCK:(g + 1) * BLOCK].astype(o_ref.dtype)
    m_ref[0, 0] = jnp.transpose(jnp.broadcast_to(top, (top.shape[0], 128)))[0:1]
    l_ref[0, 0] = jnp.transpose(jnp.broadcast_to(total, (total.shape[0], 128)))[0:1]


def local_attention(queries, cached_keys, chosen, live, cached_values):
    query_count, query_width = queries.shape
    heads_kv = cached_keys.shape[1] // HEAD_DIM
    group_size = query_width // (heads_kv * HEAD_DIM)
    qblocks = query_count // BLOCK
    width = group_size * HEAD_DIM
    stat_shape = jax.ShapeDtypeStruct((qblocks, heads_kv, 1, group_size * BLOCK), jnp.float32)
    stat_spec = pl.BlockSpec((1, 1, 1, group_size * BLOCK), lambda b, k, c, v: (b, k, 0, 0))
    flops = 4 * query_count * heads_kv * group_size * CAP * BLOCK * HEAD_DIM
    return pl.pallas_call(
        attend_kernel,
        out_shape=(jax.ShapeDtypeStruct((query_count, query_width), jnp.bfloat16), stat_shape, stat_shape),
        grid_spec=pltpu.PrefetchScalarGridSpec(
            num_scalar_prefetch=2,
            grid=(qblocks, heads_kv),
            in_specs=[
                pl.BlockSpec((BLOCK, width), lambda b, k, c, v: (b, k)),
                pl.BlockSpec(memory_space=pl.ANY),
                pl.BlockSpec(memory_space=pl.ANY),
            ],
            out_specs=[pl.BlockSpec((BLOCK, width), lambda b, k, c, v: (b, k)), stat_spec, stat_spec],
            scratch_shapes=[
                pltpu.VMEM((CAP * BLOCK, HEAD_DIM), jnp.bfloat16),
                pltpu.VMEM((CAP * BLOCK, HEAD_DIM), jnp.bfloat16),
                pltpu.SemaphoreType.DMA((2, CAP)),
            ],
        ),
        cost_estimate=pl.CostEstimate(
            flops=flops,
            transcendentals=query_count * heads_kv * group_size * CAP * BLOCK,
            bytes_accessed=4 * queries.size + 4 * qblocks * heads_kv * CAP * BLOCK * HEAD_DIM,
        ),
    )(chosen, live, queries, cached_keys, cached_values)


def shards(queries, cached_keys, cached_values, pattern, out_weight):
    shard_index = lax.axis_index("ctx")
    head_index = lax.axis_index("head")
    ctx_n = lax.axis_size("ctx")
    query_count, query_width = queries.shape
    cache_rows, cache_width = cached_keys.shape
    heads_kv = cache_width // HEAD_DIM
    group_size = HEADS // KV_HEADS
    heads_here = heads_kv * group_size
    local_blocks = cache_rows // BLOCK
    qblocks = query_count // BLOCK

    local_block = pattern - shard_index * local_blocks
    in_shard = (local_block >= 0) & (local_block < local_blocks)
    slot_rank = jnp.cumsum(in_shard.astype(jnp.int32), axis=1) - 1
    slot_ids = jnp.arange(CAP, dtype=jnp.int32)
    picked = in_shard[:, :, None] & (slot_rank[:, :, None] == slot_ids[None, None, :])
    chosen = jnp.sum(jnp.where(picked, local_block[:, :, None], 0), axis=1).astype(jnp.int32)
    live = jnp.any(picked, axis=1).astype(jnp.int32)

    mixed, top, total = local_attention(queries, cached_keys, chosen, live, cached_values)

    def by_row(stat):
        stat = stat.reshape(qblocks, heads_kv, group_size, BLOCK).transpose(0, 3, 1, 2)
        return stat.reshape(query_count, heads_here)

    stats = jnp.concatenate([by_row(top), by_row(total)], axis=1)
    got_stats = lax.all_to_all(stats, "ctx", split_axis=0, concat_axis=0, tiled=True)
    got_stats = got_stats.reshape(ctx_n, -1, 2, heads_here)
    got_top, got_total = got_stats[:, :, 0], got_stats[:, :, 1]
    row_peak = got_top.max(axis=0)
    rescale = jnp.exp(got_top - row_peak[None])
    got_mixed = lax.all_to_all(mixed, "ctx", split_axis=0, concat_axis=0, tiled=True)
    got_mixed = got_mixed.reshape(ctx_n, -1, heads_here, HEAD_DIM).astype(jnp.float32)
    summed = jnp.sum(got_mixed * rescale[..., None], axis=0)
    row_norm = jnp.sum(got_total * rescale, axis=0)
    rows_here = summed.shape[0]
    attended = (summed / row_norm[:, :, None]).reshape(rows_here, query_width).astype(jnp.bfloat16)
    partial_out = jnp.dot(
        lax.all_gather(attended, "ctx", axis=0, tiled=True),
        out_weight,
        preferred_element_type=jnp.float32,
    )
    heads_n = lax.axis_size("head")
    share = partial_out.shape[1] // heads_n
    if heads_n == 2:
        kept = lax.dynamic_slice_in_dim(partial_out, head_index * share, share, axis=1)
        sent = lax.dynamic_slice_in_dim(partial_out, (1 - head_index) * share, share, axis=1)
        got = lax.ppermute(sent.astype(jnp.bfloat16), "head", perm=[(0, 1), (1, 0)])
        return (kept + got.astype(jnp.float32)).astype(jnp.bfloat16)
    pieces = partial_out.reshape(query_count, heads_n, share).transpose(1, 0, 2)
    got = lax.all_to_all(pieces.astype(jnp.bfloat16), "head", 0, 0, tiled=True)
    return got.astype(jnp.float32).sum(axis=0).astype(jnp.bfloat16)


def solution(mesh):
    return jax.shard_map(
        shards,
        mesh=mesh,
        in_specs=(
            P(("groups", "rep"), "head"),
            P(("groups", "ctx"), "head"),
            P(("groups", "ctx"), "head"),
            P(("groups", "rep"), None),
            P("head", "ctx"),
        ),
        out_specs=P(("groups", "rep"), ("ctx", "head")),
        check_vma=False,
    )
```

```python
import jax
import jax.numpy as jnp
from jax import lax
from jax.experimental import pallas as pl
from jax.experimental.pallas import tpu as pltpu
from jax.sharding import PartitionSpec as P

HEADS = 64
KV_HEADS = 8
HEAD_DIM = 128
BLOCK = 128
CAP = 8


def attend_kernel(chosen_ref, live_ref, q_ref, k_hbm, v_hbm, o_ref, m_ref, l_ref, kbuf, vbuf, sem):
    b = pl.program_id(0)
    steps = pl.num_programs(0)
    heads_kv = k_hbm.shape[1] // HEAD_DIM
    group_size = q_ref.shape[1] // (heads_kv * HEAD_DIM)

    def block_copies(step, slot):
        copies = []
        for j in range(CAP):
            rows = pl.ds(pl.multiple_of(chosen_ref[step, j] * BLOCK, BLOCK), BLOCK)
            dst = pl.ds(j * BLOCK, BLOCK)
            copies.append(pltpu.make_async_copy(k_hbm.at[rows], kbuf.at[slot, dst], sem.at[slot, 0, j]))
            copies.append(pltpu.make_async_copy(v_hbm.at[rows], vbuf.at[slot, dst], sem.at[slot, 1, j]))
        return copies

    slot = b % 2

    @pl.when(b == 0)
    def _():
        for c in block_copies(b, slot):
            c.start()

    @pl.when(b + 1 < steps)
    def _():
        for c in block_copies(b + 1, 1 - slot):
            c.start()

    for c in block_copies(b, slot):
        c.wait()

    key_slot = lax.broadcasted_iota(jnp.int32, (1, CAP * BLOCK), 1) // BLOCK
    live_keys = key_slot < 0
    for j in range(CAP):
        live_keys = live_keys | ((key_slot == j) & (live_ref[b, j] > 0))
    for kv in range(heads_kv):
        base = kv * group_size * HEAD_DIM
        stacked = jnp.concatenate(
            [q_ref[:, base + g * HEAD_DIM:base + (g + 1) * HEAD_DIM] for g in range(group_size)], axis=0
        )
        keys = kbuf[slot, :, kv * HEAD_DIM:(kv + 1) * HEAD_DIM]
        scores = lax.dot_general(
            stacked, keys, (((1,), (1,)), ((), ())), preferred_element_type=jnp.float32
        ) * (HEAD_DIM ** (-0.5))
        scores = jnp.where(live_keys, scores, jnp.float32(-1e30))
        top = jnp.max(scores, axis=1, keepdims=True)
        weights = jnp.exp(scores - top)
        total = jnp.sum(weights, axis=1, keepdims=True)
        values = vbuf[slot, :, kv * HEAD_DIM:(kv + 1) * HEAD_DIM]
        mixed = jnp.dot(weights.astype(jnp.bfloat16), values, preferred_element_type=jnp.float32)
        for g in range(group_size):
            o_ref[:, base + g * HEAD_DIM:base + (g + 1) * HEAD_DIM] = (
                mixed[g * BLOCK:(g + 1) * BLOCK].astype(o_ref.dtype)
            )
        m_ref[0, kv] = jnp.transpose(jnp.broadcast_to(top, (top.shape[0], 128)))[0:1]
        l_ref[0, kv] = jnp.transpose(jnp.broadcast_to(total, (total.shape[0], 128)))[0:1]


def local_attention(queries, cached_keys, chosen, live, cached_values):
    query_count, query_width = queries.shape
    cache_width = cached_keys.shape[1]
    heads_kv = cache_width // HEAD_DIM
    group_size = query_width // (heads_kv * HEAD_DIM)
    qblocks = query_count // BLOCK
    stat_shape = jax.ShapeDtypeStruct((qblocks, heads_kv, 1, group_size * BLOCK), jnp.float32)
    stat_spec = pl.BlockSpec((1, heads_kv, 1, group_size * BLOCK), lambda b, c, v: (b, 0, 0, 0))
    flops = 4 * query_count * heads_kv * group_size * CAP * BLOCK * HEAD_DIM
    return pl.pallas_call(
        attend_kernel,
        out_shape=(jax.ShapeDtypeStruct((query_count, query_width), jnp.bfloat16), stat_shape, stat_shape),
        grid_spec=pltpu.PrefetchScalarGridSpec(
            num_scalar_prefetch=2,
            grid=(qblocks,),
            in_specs=[
                pl.BlockSpec((BLOCK, query_width), lambda b, c, v: (b, 0)),
                pl.BlockSpec(memory_space=pl.ANY),
                pl.BlockSpec(memory_space=pl.ANY),
            ],
            out_specs=[pl.BlockSpec((BLOCK, query_width), lambda b, c, v: (b, 0)), stat_spec, stat_spec],
            scratch_shapes=[
                pltpu.VMEM((2, CAP * BLOCK, cache_width), jnp.bfloat16),
                pltpu.VMEM((2, CAP * BLOCK, cache_width), jnp.bfloat16),
                pltpu.SemaphoreType.DMA((2, 2, CAP)),
            ],
        ),
        compiler_params=pltpu.CompilerParams(dimension_semantics=("arbitrary",)),
        cost_estimate=pl.CostEstimate(
            flops=flops,
            transcendentals=query_count * heads_kv * group_size * CAP * BLOCK,
            bytes_accessed=4 * queries.size + 4 * qblocks * CAP * BLOCK * cache_width,
        ),
    )(chosen, live, queries, cached_keys, cached_values)


def shards(queries, cached_keys, cached_values, pattern, out_weight):
    shard_index = lax.axis_index("ctx")
    head_index = lax.axis_index("head")
    ctx_n = lax.axis_size("ctx")
    query_count, query_width = queries.shape
    cache_rows, cache_width = cached_keys.shape
    heads_kv = cache_width // HEAD_DIM
    group_size = HEADS // KV_HEADS
    heads_here = heads_kv * group_size
    local_blocks = cache_rows // BLOCK
    qblocks = query_count // BLOCK

    local_block = pattern - shard_index * local_blocks
    in_shard = (local_block >= 0) & (local_block < local_blocks)
    slot_rank = jnp.cumsum(in_shard.astype(jnp.int32), axis=1) - 1
    slot_ids = jnp.arange(CAP, dtype=jnp.int32)
    picked = in_shard[:, :, None] & (slot_rank[:, :, None] == slot_ids[None, None, :])
    chosen = jnp.sum(jnp.where(picked, local_block[:, :, None], 0), axis=1).astype(jnp.int32)
    live = jnp.any(picked, axis=1).astype(jnp.int32)

    mixed, top, total = local_attention(queries, cached_keys, chosen, live, cached_values)

    def by_row(stat):
        stat = stat.reshape(qblocks, heads_kv, group_size, BLOCK).transpose(0, 3, 1, 2)
        return stat.reshape(query_count, heads_here)

    stats = jnp.concatenate([by_row(top), by_row(total)], axis=1)
    got_stats = lax.all_to_all(stats, "ctx", split_axis=0, concat_axis=0, tiled=True)
    got_stats = got_stats.reshape(ctx_n, -1, 2, heads_here)
    got_top, got_total = got_stats[:, :, 0], got_stats[:, :, 1]
    row_peak = got_top.max(axis=0)
    rescale = jnp.exp(got_top - row_peak[None])
    got_mixed = lax.all_to_all(mixed, "ctx", split_axis=0, concat_axis=0, tiled=True)
    got_mixed = got_mixed.reshape(ctx_n, -1, heads_here, HEAD_DIM).astype(jnp.float32)
    summed = jnp.sum(got_mixed * rescale[..., None], axis=0)
    row_norm = jnp.sum(got_total * rescale, axis=0)
    rows_here = summed.shape[0]
    attended = (summed / row_norm[:, :, None]).reshape(rows_here, query_width).astype(jnp.bfloat16)
    partial_out = jnp.dot(
        lax.all_gather(attended, "ctx", axis=0, tiled=True),
        out_weight,
        preferred_element_type=jnp.float32,
    )
    heads_n = lax.axis_size("head")
    share = partial_out.shape[1] // heads_n
    if heads_n == 2:
        kept = lax.dynamic_slice_in_dim(partial_out, head_index * share, share, axis=1)
        sent = lax.dynamic_slice_in_dim(partial_out, (1 - head_index) * share, share, axis=1)
        got = lax.ppermute(sent.astype(jnp.bfloat16), "head", perm=[(0, 1), (1, 0)])
        return (kept + got.astype(jnp.float32)).astype(jnp.bfloat16)
    pieces = partial_out.reshape(query_count, heads_n, share).transpose(1, 0, 2)
    got = lax.all_to_all(pieces.astype(jnp.bfloat16), "head", 0, 0, tiled=True)
    return got.astype(jnp.float32).sum(axis=0).astype(jnp.bfloat16)


def solution(mesh):
    return jax.shard_map(
        shards,
        mesh=mesh,
        in_specs=(
            P(("groups", "rep"), "head"),
            P(("groups", "ctx"), "head"),
            P(("groups", "ctx"), "head"),
            P(("groups", "rep"), None),
            P("head", "ctx"),
        ),
        out_specs=P(("groups", "rep"), ("ctx", "head")),
        check_vma=False,
    )
```

```python
import jax
import jax.numpy as jnp
from jax import lax
from jax.experimental import pallas as pl
from jax.experimental.pallas import tpu as pltpu
from jax.sharding import PartitionSpec as P

HEADS = 64
KV_HEADS = 8
HEAD_DIM = 128
BLOCK = 128
CAP = 8


def attend_kernel(chosen_ref, live_ref, q_ref, k_hbm, v_hbm, o0_ref, o1_ref, m_ref, l_ref, kbuf, vbuf, sem):
    b = pl.program_id(0)
    steps = pl.num_programs(0)
    heads_kv = k_hbm.shape[1] // HEAD_DIM
    group_size = q_ref.shape[1] // (heads_kv * HEAD_DIM)

    def block_copies(step, slot):
        copies = []
        for j in range(CAP):
            rows = pl.ds(pl.multiple_of(chosen_ref[step, j] * BLOCK, BLOCK), BLOCK)
            dst = pl.ds(j * BLOCK, BLOCK)
            copies.append(pltpu.make_async_copy(k_hbm.at[rows], kbuf.at[slot, dst], sem.at[slot, 0, j]))
            copies.append(pltpu.make_async_copy(v_hbm.at[rows], vbuf.at[slot, dst], sem.at[slot, 1, j]))
        return copies

    slot = b % 2

    @pl.when(b == 0)
    def _():
        for c in block_copies(b, slot):
            c.start()

    @pl.when(b + 1 < steps)
    def _():
        for c in block_copies(b + 1, 1 - slot):
            c.start()

    for c in block_copies(b, slot):
        c.wait()

    key_slot = lax.broadcasted_iota(jnp.int32, (1, CAP * BLOCK), 1) // BLOCK
    live_keys = key_slot < 0
    for j in range(CAP):
        live_keys = live_keys | ((key_slot == j) & (live_ref[b, j] > 0))
    for kv in range(heads_kv):
        base = kv * group_size * HEAD_DIM
        stacked = jnp.concatenate(
            [q_ref[:, base + g * HEAD_DIM:base + (g + 1) * HEAD_DIM] for g in range(group_size)], axis=0
        )
        keys = kbuf[slot, :, kv * HEAD_DIM:(kv + 1) * HEAD_DIM]
        scores = lax.dot_general(
            stacked, keys, (((1,), (1,)), ((), ())), preferred_element_type=jnp.float32
        ) * (HEAD_DIM ** (-0.5))
        scores = jnp.where(live_keys, scores, jnp.float32(-1e30))
        top = jnp.max(scores, axis=1, keepdims=True)
        weights = jnp.exp(scores - top)
        total = jnp.sum(weights, axis=1, keepdims=True)
        values = vbuf[slot, :, kv * HEAD_DIM:(kv + 1) * HEAD_DIM]
        mixed = jnp.dot(weights.astype(jnp.bfloat16), values, preferred_element_type=jnp.float32)
        half_width = o0_ref.shape[1]
        for g in range(group_size):
            column = base + g * HEAD_DIM
            o_ref = o0_ref if column < half_width else o1_ref
            column = column % half_width
            o_ref[:, column:column + HEAD_DIM] = mixed[g * BLOCK:(g + 1) * BLOCK].astype(o_ref.dtype)
        m_ref[0, kv] = jnp.transpose(jnp.broadcast_to(top, (top.shape[0], 128)))[0:1]
        l_ref[0, kv] = jnp.transpose(jnp.broadcast_to(total, (total.shape[0], 128)))[0:1]


def local_attention(queries, cached_keys, chosen, live, cached_values):
    query_count, query_width = queries.shape
    cache_width = cached_keys.shape[1]
    heads_kv = cache_width // HEAD_DIM
    group_size = query_width // (heads_kv * HEAD_DIM)
    qblocks = query_count // BLOCK
    stat_shape = jax.ShapeDtypeStruct((qblocks, heads_kv, 1, group_size * BLOCK), jnp.float32)
    stat_spec = pl.BlockSpec((1, heads_kv, 1, group_size * BLOCK), lambda b, c, v: (b, 0, 0, 0))
    half_shape = jax.ShapeDtypeStruct((query_count, query_width // 2), jnp.bfloat16)
    half_spec = pl.BlockSpec((BLOCK, query_width // 2), lambda b, c, v: (b, 0))
    flops = 4 * query_count * heads_kv * group_size * CAP * BLOCK * HEAD_DIM
    return pl.pallas_call(
        attend_kernel,
        out_shape=(half_shape, half_shape, stat_shape, stat_shape),
        grid_spec=pltpu.PrefetchScalarGridSpec(
            num_scalar_prefetch=2,
            grid=(qblocks,),
            in_specs=[
                pl.BlockSpec((BLOCK, query_width), lambda b, c, v: (b, 0)),
                pl.BlockSpec(memory_space=pl.ANY),
                pl.BlockSpec(memory_space=pl.ANY),
            ],
            out_specs=[half_spec, half_spec, stat_spec, stat_spec],
            scratch_shapes=[
                pltpu.VMEM((2, CAP * BLOCK, cache_width), jnp.bfloat16),
                pltpu.VMEM((2, CAP * BLOCK, cache_width), jnp.bfloat16),
                pltpu.SemaphoreType.DMA((2, 2, CAP)),
            ],
        ),
        compiler_params=pltpu.CompilerParams(dimension_semantics=("arbitrary",)),
        cost_estimate=pl.CostEstimate(
            flops=flops,
            transcendentals=query_count * heads_kv * group_size * CAP * BLOCK,
            bytes_accessed=4 * queries.size + 4 * qblocks * CAP * BLOCK * cache_width,
        ),
    )(chosen, live, queries, cached_keys, cached_values)


def shards(queries, cached_keys, cached_values, pattern, out_weight):
    shard_index = lax.axis_index("ctx")
    head_index = lax.axis_index("head")
    ctx_n = lax.axis_size("ctx")
    query_count, query_width = queries.shape
    cache_rows, cache_width = cached_keys.shape
    heads_kv = cache_width // HEAD_DIM
    group_size = HEADS // KV_HEADS
    heads_here = heads_kv * group_size
    local_blocks = cache_rows // BLOCK
    qblocks = query_count // BLOCK

    local_block = pattern - shard_index * local_blocks
    in_shard = (local_block >= 0) & (local_block < local_blocks)
    slot_rank = jnp.cumsum(in_shard.astype(jnp.int32), axis=1) - 1
    slot_ids = jnp.arange(CAP, dtype=jnp.int32)
    picked = in_shard[:, :, None] & (slot_rank[:, :, None] == slot_ids[None, None, :])
    chosen = jnp.sum(jnp.where(picked, local_block[:, :, None], 0), axis=1).astype(jnp.int32)
    live = jnp.any(picked, axis=1).astype(jnp.int32)

    mixed0, mixed1, top, total = local_attention(queries, cached_keys, chosen, live, cached_values)

    def by_row(stat):
        stat = stat.reshape(qblocks, heads_kv, group_size, BLOCK).transpose(0, 3, 1, 2)
        return stat.reshape(query_count, heads_here)

    stats = jnp.concatenate([by_row(top), by_row(total)], axis=1)
    got_stats = lax.all_to_all(stats, "ctx", split_axis=0, concat_axis=0, tiled=True)
    got_stats = got_stats.reshape(ctx_n, -1, 2, heads_here)
    got_top, got_total = got_stats[:, :, 0], got_stats[:, :, 1]
    row_peak = got_top.max(axis=0)
    rescale = jnp.exp(got_top - row_peak[None])
    row_norm = jnp.sum(got_total * rescale, axis=0)
    half_heads = heads_here // 2
    half_width = query_width // 2
    partial_out = None
    for part, mixed in enumerate((mixed0, mixed1)):
        heads = slice(part * half_heads, (part + 1) * half_heads)
        got_mixed = lax.all_to_all(mixed, "ctx", split_axis=0, concat_axis=0, tiled=True)
        got_mixed = got_mixed.reshape(ctx_n, -1, half_heads, HEAD_DIM).astype(jnp.float32)
        summed = jnp.sum(got_mixed * rescale[:, :, heads, None], axis=0)
        rows_here = summed.shape[0]
        attended = (summed / row_norm[:, heads, None]).reshape(rows_here, half_width).astype(jnp.bfloat16)
        term = jnp.dot(
            lax.all_gather(attended, "ctx", axis=0, tiled=True),
            out_weight[part * half_width:(part + 1) * half_width],
            preferred_element_type=jnp.float32,
        )
        partial_out = term if partial_out is None else partial_out + term
    heads_n = lax.axis_size("head")
    share = partial_out.shape[1] // heads_n
    if heads_n == 2:
        kept = lax.dynamic_slice_in_dim(partial_out, head_index * share, share, axis=1)
        sent = lax.dynamic_slice_in_dim(partial_out, (1 - head_index) * share, share, axis=1)
        got = lax.ppermute(sent.astype(jnp.bfloat16), "head", perm=[(0, 1), (1, 0)])
        return (kept + got.astype(jnp.float32)).astype(jnp.bfloat16)
    pieces = partial_out.reshape(query_count, heads_n, share).transpose(1, 0, 2)
    got = lax.all_to_all(pieces.astype(jnp.bfloat16), "head", 0, 0, tiled=True)
    return got.astype(jnp.float32).sum(axis=0).astype(jnp.bfloat16)


def solution(mesh):
    return jax.shard_map(
        shards,
        mesh=mesh,
        in_specs=(
            P(("groups", "rep"), "head"),
            P(("groups", "ctx"), "head"),
            P(("groups", "ctx"), "head"),
            P(("groups", "rep"), None),
            P("head", "ctx"),
        ),
        out_specs=P(("groups", "rep"), ("ctx", "head")),
        check_vma=False,
    )
```

```python
import functools

import jax
import jax.numpy as jnp
from jax import lax
from jax.experimental import pallas as pl
from jax.experimental.pallas import tpu as pltpu
from jax.sharding import PartitionSpec as P

HEADS = 64
KV_HEADS = 8
HEAD_DIM = 128
BLOCK = 128
CAP = 8


def attend_kernel(kv_first, chosen_ref, live_ref, q_ref, k_hbm, v_hbm, o_ref, m_ref, l_ref, kbuf, vbuf, sem):
    b = pl.program_id(0)
    steps = pl.num_programs(0)
    heads_kv = m_ref.shape[1]
    group_size = q_ref.shape[1] // (heads_kv * HEAD_DIM)

    def block_copies(step, slot):
        copies = []
        for j in range(CAP):
            rows = pl.ds(pl.multiple_of(chosen_ref[step, j] * BLOCK, BLOCK), BLOCK)
            dst = pl.ds(j * BLOCK, BLOCK)
            copies.append(pltpu.make_async_copy(k_hbm.at[rows], kbuf.at[slot, dst], sem.at[slot, 0, j]))
            copies.append(pltpu.make_async_copy(v_hbm.at[rows], vbuf.at[slot, dst], sem.at[slot, 1, j]))
        return copies

    slot = b % 2

    @pl.when(b == 0)
    def _():
        for c in block_copies(b, slot):
            c.start()

    @pl.when(b + 1 < steps)
    def _():
        for c in block_copies(b + 1, 1 - slot):
            c.start()

    for c in block_copies(b, slot):
        c.wait()

    key_slot = lax.broadcasted_iota(jnp.int32, (1, CAP * BLOCK), 1) // BLOCK
    live_keys = key_slot < 0
    for j in range(CAP):
        live_keys = live_keys | ((key_slot == j) & (live_ref[b, j] > 0))
    for kv in range(heads_kv):
        base = kv * group_size * HEAD_DIM
        stacked = jnp.concatenate(
            [q_ref[:, base + g * HEAD_DIM:base + (g + 1) * HEAD_DIM] for g in range(group_size)], axis=0
        )
        column = (kv_first + kv) * HEAD_DIM
        keys = kbuf[slot, :, column:column + HEAD_DIM]
        scores = lax.dot_general(
            stacked, keys, (((1,), (1,)), ((), ())), preferred_element_type=jnp.float32
        ) * (HEAD_DIM ** (-0.5))
        scores = jnp.where(live_keys, scores, jnp.float32(-1e30))
        top = jnp.max(scores, axis=1, keepdims=True)
        weights = jnp.exp(scores - top)
        total = jnp.sum(weights, axis=1, keepdims=True)
        values = vbuf[slot, :, column:column + HEAD_DIM]
        mixed = jnp.dot(weights.astype(jnp.bfloat16), values, preferred_element_type=jnp.float32)
        for g in range(group_size):
            o_ref[:, base + g * HEAD_DIM:base + (g + 1) * HEAD_DIM] = (
                mixed[g * BLOCK:(g + 1) * BLOCK].astype(o_ref.dtype)
            )
        m_ref[0, kv] = jnp.transpose(jnp.broadcast_to(top, (top.shape[0], 128)))[0:1]
        l_ref[0, kv] = jnp.transpose(jnp.broadcast_to(total, (total.shape[0], 128)))[0:1]


def local_attention(queries, cached_keys, chosen, live, cached_values, kv_first, heads_kv):
    query_count = queries.shape[0]
    cache_width = cached_keys.shape[1]
    group_size = HEADS // KV_HEADS
    query_width = heads_kv * group_size * HEAD_DIM
    part = kv_first // heads_kv
    qblocks = query_count // BLOCK
    stat_shape = jax.ShapeDtypeStruct((qblocks, heads_kv, 1, group_size * BLOCK), jnp.float32)
    stat_spec = pl.BlockSpec((1, heads_kv, 1, group_size * BLOCK), lambda b, c, v: (b, 0, 0, 0))
    flops = 4 * query_count * heads_kv * group_size * CAP * BLOCK * HEAD_DIM
    return pl.pallas_call(
        functools.partial(attend_kernel, kv_first),
        out_shape=(jax.ShapeDtypeStruct((query_count, query_width), jnp.bfloat16), stat_shape, stat_shape),
        grid_spec=pltpu.PrefetchScalarGridSpec(
            num_scalar_prefetch=2,
            grid=(qblocks,),
            in_specs=[
                pl.BlockSpec((BLOCK, query_width), lambda b, c, v: (b, part)),
                pl.BlockSpec(memory_space=pl.ANY),
                pl.BlockSpec(memory_space=pl.ANY),
            ],
            out_specs=[pl.BlockSpec((BLOCK, query_width), lambda b, c, v: (b, 0)), stat_spec, stat_spec],
            scratch_shapes=[
                pltpu.VMEM((2, CAP * BLOCK, cache_width), jnp.bfloat16),
                pltpu.VMEM((2, CAP * BLOCK, cache_width), jnp.bfloat16),
                pltpu.SemaphoreType.DMA((2, 2, CAP)),
            ],
        ),
        compiler_params=pltpu.CompilerParams(dimension_semantics=("arbitrary",)),
        cost_estimate=pl.CostEstimate(
            flops=flops,
            transcendentals=query_count * heads_kv * group_size * CAP * BLOCK,
            bytes_accessed=2 * query_count * query_width + 4 * qblocks * CAP * BLOCK * cache_width,
        ),
    )(chosen, live, queries, cached_keys, cached_values)


def shards(queries, cached_keys, cached_values, pattern, out_weight):
    shard_index = lax.axis_index("ctx")
    head_index = lax.axis_index("head")
    ctx_n = lax.axis_size("ctx")
    query_count, query_width = queries.shape
    cache_rows, cache_width = cached_keys.shape
    heads_kv = cache_width // HEAD_DIM
    group_size = HEADS // KV_HEADS
    heads_here = heads_kv * group_size
    local_blocks = cache_rows // BLOCK
    qblocks = query_count // BLOCK

    local_block = pattern - shard_index * local_blocks
    in_shard = (local_block >= 0) & (local_block < local_blocks)
    slot_rank = jnp.cumsum(in_shard.astype(jnp.int32), axis=1) - 1
    slot_ids = jnp.arange(CAP, dtype=jnp.int32)
    picked = in_shard[:, :, None] & (slot_rank[:, :, None] == slot_ids[None, None, :])
    chosen = jnp.sum(jnp.where(picked, local_block[:, :, None], 0), axis=1).astype(jnp.int32)
    live = jnp.any(picked, axis=1).astype(jnp.int32)

    parts = 2 if heads_kv % 2 == 0 else 1
    part_kv = heads_kv // parts
    part_heads = part_kv * group_size
    part_width = part_heads * HEAD_DIM
    heads_n = lax.axis_size("head")
    share = out_weight.shape[1] // heads_n

    def by_row(stat):
        stat = stat.reshape(qblocks, part_kv, group_size, BLOCK).transpose(0, 3, 1, 2)
        return stat.reshape(query_count, part_heads)

    terms = []
    for part in range(parts):
        mixed, top, total = local_attention(
            queries, cached_keys, chosen, live, cached_values, part * part_kv, part_kv
        )
        stats = jnp.concatenate([by_row(top), by_row(total)], axis=1)
        got_stats = lax.all_to_all(stats, "ctx", split_axis=0, concat_axis=0, tiled=True)
        got_stats = got_stats.reshape(ctx_n, -1, 2, part_heads)
        got_top, got_total = got_stats[:, :, 0], got_stats[:, :, 1]
        row_peak = got_top.max(axis=0)
        rescale = jnp.exp(got_top - row_peak[None])
        row_norm = jnp.sum(got_total * rescale, axis=0)
        got_mixed = lax.all_to_all(mixed, "ctx", split_axis=0, concat_axis=0, tiled=True)
        got_mixed = got_mixed.reshape(ctx_n, -1, part_heads, HEAD_DIM).astype(jnp.float32)
        summed = jnp.sum(got_mixed * rescale[..., None], axis=0)
        rows_here = summed.shape[0]
        attended = (summed / row_norm[:, :, None]).reshape(rows_here, part_width).astype(jnp.bfloat16)
        terms.append((lax.all_gather(attended, "ctx", axis=0, tiled=True),
                      out_weight[part * part_width:(part + 1) * part_width]))

    def project(columns):
        total_out = None
        for rows, weight in terms:
            term = jnp.dot(rows, columns(weight), preferred_element_type=jnp.float32)
            total_out = term if total_out is None else total_out + term
        return total_out

    if heads_n == 2:
        sent = project(lambda w: lax.dynamic_slice_in_dim(w, (1 - head_index) * share, share, axis=1))
        got = lax.ppermute(sent.astype(jnp.bfloat16), "head", perm=[(0, 1), (1, 0)])
        kept = project(lambda w: lax.dynamic_slice_in_dim(w, head_index * share, share, axis=1))
        return (kept + got.astype(jnp.float32)).astype(jnp.bfloat16)
    partial_out = project(lambda w: w)
    pieces = partial_out.reshape(query_count, heads_n, share).transpose(1, 0, 2)
    got = lax.all_to_all(pieces.astype(jnp.bfloat16), "head", 0, 0, tiled=True)
    return got.astype(jnp.float32).sum(axis=0).astype(jnp.bfloat16)


def solution(mesh):
    return jax.shard_map(
        shards,
        mesh=mesh,
        in_specs=(
            P(("groups", "rep"), "head"),
            P(("groups", "ctx"), "head"),
            P(("groups", "ctx"), "head"),
            P(("groups", "rep"), None),
            P("head", "ctx"),
        ),
        out_specs=P(("groups", "rep"), ("ctx", "head")),
        check_vma=False,
    )
```

```python
import jax
import jax.numpy as jnp
from jax import lax
from jax.experimental import pallas as pl
from jax.experimental.pallas import tpu as pltpu
from jax.sharding import PartitionSpec as P

HEADS = 64
KV_HEADS = 8
HEAD_DIM = 128
BLOCK = 128
CAP = 8


def attend_kernel(chosen_ref, live_ref, q_ref, k_hbm, v_hbm, o0_ref, o1_ref, m_ref, l_ref, kbuf, vbuf, sem,
                  score_ref, top_ref, total_ref, acc_ref):
    b = pl.program_id(0)
    steps = pl.num_programs(0)
    heads_kv = k_hbm.shape[1] // HEAD_DIM
    group_size = q_ref.shape[1] // (heads_kv * HEAD_DIM)

    def block_copies(step, slot):
        copies = []
        for j in range(CAP):
            rows = pl.ds(pl.multiple_of(chosen_ref[step, j] * BLOCK, BLOCK), BLOCK)
            dst = pl.ds(j * BLOCK, BLOCK)
            copies.append(pltpu.make_async_copy(k_hbm.at[rows], kbuf.at[slot, dst], sem.at[slot, 0, j]))
            copies.append(pltpu.make_async_copy(v_hbm.at[rows], vbuf.at[slot, dst], sem.at[slot, 1, j]))
        return copies

    slot = b % 2

    @pl.when(b == 0)
    def _():
        for c in block_copies(b, slot):
            c.start()

    @pl.when(b + 1 < steps)
    def _():
        for c in block_copies(b + 1, 1 - slot):
            c.start()

    for c in block_copies(b, slot):
        c.wait()

    for kv in range(heads_kv):
        base = kv * group_size * HEAD_DIM
        column = kv * HEAD_DIM
        stacked = jnp.concatenate(
            [q_ref[:, base + g * HEAD_DIM:base + (g + 1) * HEAD_DIM] for g in range(group_size)], axis=0
        )
        top_ref[...] = jnp.full(top_ref.shape, -1e30, jnp.float32)
        total_ref[...] = jnp.zeros(total_ref.shape, jnp.float32)
        acc_ref[...] = jnp.zeros(acc_ref.shape, jnp.float32)
        def score_slot(j, carry):
            @pl.when(live_ref[b, j] > 0)
            def _():
                rows = pl.ds(pl.multiple_of(j * BLOCK, BLOCK), BLOCK)
                keys = kbuf[slot, rows, column:column + HEAD_DIM]
                scores = lax.dot_general(
                    stacked, keys, (((1,), (1,)), ((), ())), preferred_element_type=jnp.float32
                ) * (HEAD_DIM ** (-0.5))
                score_ref[j] = scores
                top_ref[...] = jnp.maximum(top_ref[...], jnp.max(scores, axis=1, keepdims=True))
            return carry

        def mix_slot(j, carry):
            @pl.when(live_ref[b, j] > 0)
            def _():
                rows = pl.ds(pl.multiple_of(j * BLOCK, BLOCK), BLOCK)
                weights = jnp.exp(score_ref[j] - top_ref[...])
                total_ref[...] += jnp.sum(weights, axis=1, keepdims=True)
                values = vbuf[slot, rows, column:column + HEAD_DIM]
                acc_ref[...] += jnp.dot(weights.astype(jnp.bfloat16), values, preferred_element_type=jnp.float32)
            return carry

        lax.fori_loop(0, CAP, score_slot, 0)
        lax.fori_loop(0, CAP, mix_slot, 0)
        mixed = acc_ref[...]
        top = top_ref[...]
        total = total_ref[...]
        half_width = o0_ref.shape[1]
        for g in range(group_size):
            column = base + g * HEAD_DIM
            o_ref = o0_ref if column < half_width else o1_ref
            column = column % half_width
            o_ref[:, column:column + HEAD_DIM] = mixed[g * BLOCK:(g + 1) * BLOCK].astype(o_ref.dtype)
        m_ref[0, kv] = jnp.transpose(jnp.broadcast_to(top, (top.shape[0], 128)))[0:1]
        l_ref[0, kv] = jnp.transpose(jnp.broadcast_to(total, (total.shape[0], 128)))[0:1]


def local_attention(queries, cached_keys, chosen, live, cached_values):
    query_count, query_width = queries.shape
    cache_width = cached_keys.shape[1]
    heads_kv = cache_width // HEAD_DIM
    group_size = query_width // (heads_kv * HEAD_DIM)
    qblocks = query_count // BLOCK
    stat_shape = jax.ShapeDtypeStruct((qblocks, heads_kv, 1, group_size * BLOCK), jnp.float32)
    stat_spec = pl.BlockSpec((1, heads_kv, 1, group_size * BLOCK), lambda b, c, v: (b, 0, 0, 0))
    half_shape = jax.ShapeDtypeStruct((query_count, query_width // 2), jnp.bfloat16)
    half_spec = pl.BlockSpec((BLOCK, query_width // 2), lambda b, c, v: (b, 0))
    flops = 4 * query_count * heads_kv * group_size * CAP * BLOCK * HEAD_DIM
    return pl.pallas_call(
        attend_kernel,
        out_shape=(half_shape, half_shape, stat_shape, stat_shape),
        grid_spec=pltpu.PrefetchScalarGridSpec(
            num_scalar_prefetch=2,
            grid=(qblocks,),
            in_specs=[
                pl.BlockSpec((BLOCK, query_width), lambda b, c, v: (b, 0)),
                pl.BlockSpec(memory_space=pl.ANY),
                pl.BlockSpec(memory_space=pl.ANY),
            ],
            out_specs=[half_spec, half_spec, stat_spec, stat_spec],
            scratch_shapes=[
                pltpu.VMEM((2, CAP * BLOCK, cache_width), jnp.bfloat16),
                pltpu.VMEM((2, CAP * BLOCK, cache_width), jnp.bfloat16),
                pltpu.SemaphoreType.DMA((2, 2, CAP)),
                pltpu.VMEM((CAP, group_size * BLOCK, BLOCK), jnp.float32),
                pltpu.VMEM((group_size * BLOCK, 1), jnp.float32),
                pltpu.VMEM((group_size * BLOCK, 1), jnp.float32),
                pltpu.VMEM((group_size * BLOCK, HEAD_DIM), jnp.float32),
            ],
        ),
        compiler_params=pltpu.CompilerParams(dimension_semantics=("arbitrary",)),
        cost_estimate=pl.CostEstimate(
            flops=flops,
            transcendentals=query_count * heads_kv * group_size * CAP * BLOCK,
            bytes_accessed=4 * queries.size + 4 * qblocks * CAP * BLOCK * cache_width,
        ),
    )(chosen, live, queries, cached_keys, cached_values)


def shards(queries, cached_keys, cached_values, pattern, out_weight):
    shard_index = lax.axis_index("ctx")
    head_index = lax.axis_index("head")
    ctx_n = lax.axis_size("ctx")
    query_count, query_width = queries.shape
    cache_rows, cache_width = cached_keys.shape
    heads_kv = cache_width // HEAD_DIM
    group_size = HEADS // KV_HEADS
    heads_here = heads_kv * group_size
    local_blocks = cache_rows // BLOCK
    qblocks = query_count // BLOCK

    local_block = pattern - shard_index * local_blocks
    in_shard = (local_block >= 0) & (local_block < local_blocks)
    slot_rank = jnp.cumsum(in_shard.astype(jnp.int32), axis=1) - 1
    slot_ids = jnp.arange(CAP, dtype=jnp.int32)
    picked = in_shard[:, :, None] & (slot_rank[:, :, None] == slot_ids[None, None, :])
    chosen = jnp.sum(jnp.where(picked, local_block[:, :, None], 0), axis=1).astype(jnp.int32)
    live = jnp.any(picked, axis=1).astype(jnp.int32)

    mixed0, mixed1, top, total = local_attention(queries, cached_keys, chosen, live, cached_values)

    def by_row(stat):
        stat = stat.reshape(qblocks, heads_kv, group_size, BLOCK).transpose(0, 3, 1, 2)
        return stat.reshape(query_count, heads_here)

    stats = jnp.concatenate([by_row(top), by_row(total)], axis=1)
    got_stats = lax.all_to_all(stats, "ctx", split_axis=0, concat_axis=0, tiled=True)
    got_stats = got_stats.reshape(ctx_n, -1, 2, heads_here)
    got_top, got_total = got_stats[:, :, 0], got_stats[:, :, 1]
    row_peak = got_top.max(axis=0)
    rescale = jnp.exp(got_top - row_peak[None])
    row_norm = jnp.sum(got_total * rescale, axis=0)
    half_heads = heads_here // 2
    half_width = query_width // 2
    partial_out = None
    for part, mixed in enumerate((mixed0, mixed1)):
        heads = slice(part * half_heads, (part + 1) * half_heads)
        got_mixed = lax.all_to_all(mixed, "ctx", split_axis=0, concat_axis=0, tiled=True)
        got_mixed = got_mixed.reshape(ctx_n, -1, half_heads, HEAD_DIM).astype(jnp.float32)
        summed = jnp.sum(got_mixed * rescale[:, :, heads, None], axis=0)
        rows_here = summed.shape[0]
        attended = (summed / row_norm[:, heads, None]).reshape(rows_here, half_width).astype(jnp.bfloat16)
        term = jnp.dot(
            lax.all_gather(attended, "ctx", axis=0, tiled=True),
            out_weight[part * half_width:(part + 1) * half_width],
            preferred_element_type=jnp.float32,
        )
        partial_out = term if partial_out is None else partial_out + term
    heads_n = lax.axis_size("head")
    share = partial_out.shape[1] // heads_n
    if heads_n == 2:
        kept = lax.dynamic_slice_in_dim(partial_out, head_index * share, share, axis=1)
        sent = lax.dynamic_slice_in_dim(partial_out, (1 - head_index) * share, share, axis=1)
        got = lax.ppermute(sent.astype(jnp.bfloat16), "head", perm=[(0, 1), (1, 0)])
        return (kept + got.astype(jnp.float32)).astype(jnp.bfloat16)
    pieces = partial_out.reshape(query_count, heads_n, share).transpose(1, 0, 2)
    got = lax.all_to_all(pieces.astype(jnp.bfloat16), "head", 0, 0, tiled=True)
    return got.astype(jnp.float32).sum(axis=0).astype(jnp.bfloat16)


def solution(mesh):
    return jax.shard_map(
        shards,
        mesh=mesh,
        in_specs=(
            P(("groups", "rep"), "head"),
            P(("groups", "ctx"), "head"),
            P(("groups", "ctx"), "head"),
            P(("groups", "rep"), None),
            P("head", "ctx"),
        ),
        out_specs=P(("groups", "rep"), ("ctx", "head")),
        check_vma=False,
    )
```

```python
import jax
import jax.numpy as jnp
from jax import lax
from jax.experimental import pallas as pl
from jax.experimental.pallas import tpu as pltpu
from jax.sharding import PartitionSpec as P

HEADS = 64
KV_HEADS = 8
HEAD_DIM = 128
BLOCK = 128
CAP = 8


def attend_kernel(chosen_ref, live_ref, q_ref, k_hbm, v_hbm, o0_ref, o1_ref, m_ref, l_ref, kbuf, vbuf, sem):
    b = pl.program_id(0)
    steps = pl.num_programs(0)
    heads_kv = k_hbm.shape[1] // HEAD_DIM
    group_size = q_ref.shape[1] // (heads_kv * HEAD_DIM)

    def block_copies(step, slot):
        copies = []
        for j in range(CAP):
            rows = pl.ds(pl.multiple_of(chosen_ref[step, j] * BLOCK, BLOCK), BLOCK)
            dst = pl.ds(j * BLOCK, BLOCK)
            copies.append(pltpu.make_async_copy(k_hbm.at[rows], kbuf.at[slot, dst], sem.at[slot, 0, j]))
            copies.append(pltpu.make_async_copy(v_hbm.at[rows], vbuf.at[slot, dst], sem.at[slot, 1, j]))
        return copies

    slot = b % 2

    @pl.when(b == 0)
    def _():
        for c in block_copies(b, slot):
            c.start()

    @pl.when(b + 1 < steps)
    def _():
        for c in block_copies(b + 1, 1 - slot):
            c.start()

    for c in block_copies(b, slot):
        c.wait()

    key_slot = lax.broadcasted_iota(jnp.int32, (1, CAP * BLOCK), 1) // BLOCK
    live_keys = key_slot < 0
    for j in range(CAP):
        live_keys = live_keys | ((key_slot == j) & (live_ref[b, j] > 0))
    for kv in range(heads_kv):
        base = kv * group_size * HEAD_DIM
        stacked = jnp.concatenate(
            [q_ref[:, base + g * HEAD_DIM:base + (g + 1) * HEAD_DIM] for g in range(group_size)], axis=0
        )
        keys = kbuf[slot, :, kv * HEAD_DIM:(kv + 1) * HEAD_DIM]
        scores = lax.dot_general(
            stacked, keys, (((1,), (1,)), ((), ())), preferred_element_type=jnp.float32
        ) * (HEAD_DIM ** (-0.5))
        scores = jnp.where(live_keys, scores, jnp.float32(-1e30))
        top = jnp.max(scores, axis=1, keepdims=True)
        weights = jnp.exp(scores - top)
        total = jnp.sum(weights, axis=1, keepdims=True)
        values = vbuf[slot, :, kv * HEAD_DIM:(kv + 1) * HEAD_DIM]
        mixed = jnp.dot(weights.astype(jnp.bfloat16), values, preferred_element_type=jnp.float32)
        half_width = o0_ref.shape[1]
        for g in range(group_size):
            column = base + g * HEAD_DIM
            o_ref = o0_ref if column < half_width else o1_ref
            column = column % half_width
            o_ref[:, column:column + HEAD_DIM] = mixed[g * BLOCK:(g + 1) * BLOCK].astype(o_ref.dtype)
        m_ref[0, kv] = jnp.transpose(jnp.broadcast_to(top, (top.shape[0], 128)))[0:1]
        l_ref[0, kv] = jnp.transpose(jnp.broadcast_to(total, (total.shape[0], 128)))[0:1]


def local_attention(queries, cached_keys, chosen, live, cached_values):
    query_count, query_width = queries.shape
    cache_width = cached_keys.shape[1]
    heads_kv = cache_width // HEAD_DIM
    group_size = query_width // (heads_kv * HEAD_DIM)
    qblocks = query_count // BLOCK
    stat_shape = jax.ShapeDtypeStruct((qblocks, heads_kv, 1, group_size * BLOCK), jnp.float32)
    stat_spec = pl.BlockSpec((1, heads_kv, 1, group_size * BLOCK), lambda b, c, v: (b, 0, 0, 0))
    half_shape = jax.ShapeDtypeStruct((query_count, query_width // 2), jnp.bfloat16)
    half_spec = pl.BlockSpec((BLOCK, query_width // 2), lambda b, c, v: (b, 0))
    flops = 4 * query_count * heads_kv * group_size * CAP * BLOCK * HEAD_DIM
    return pl.pallas_call(
        attend_kernel,
        out_shape=(half_shape, half_shape, stat_shape, stat_shape),
        grid_spec=pltpu.PrefetchScalarGridSpec(
            num_scalar_prefetch=2,
            grid=(qblocks,),
            in_specs=[
                pl.BlockSpec((BLOCK, query_width), lambda b, c, v: (b, 0)),
                pl.BlockSpec(memory_space=pl.ANY),
                pl.BlockSpec(memory_space=pl.ANY),
            ],
            out_specs=[half_spec, half_spec, stat_spec, stat_spec],
            scratch_shapes=[
                pltpu.VMEM((2, CAP * BLOCK, cache_width), jnp.bfloat16),
                pltpu.VMEM((2, CAP * BLOCK, cache_width), jnp.bfloat16),
                pltpu.SemaphoreType.DMA((2, 2, CAP)),
            ],
        ),
        compiler_params=pltpu.CompilerParams(dimension_semantics=("arbitrary",)),
        cost_estimate=pl.CostEstimate(
            flops=flops,
            transcendentals=query_count * heads_kv * group_size * CAP * BLOCK,
            bytes_accessed=4 * queries.size + 4 * qblocks * CAP * BLOCK * cache_width,
        ),
    )(chosen, live, queries, cached_keys, cached_values)


def shards(queries, cached_keys, cached_values, pattern, out_weight):
    shard_index = lax.axis_index("ctx")
    head_index = lax.axis_index("head")
    ctx_n = lax.axis_size("ctx")
    query_count, query_width = queries.shape
    cache_rows, cache_width = cached_keys.shape
    heads_kv = cache_width // HEAD_DIM
    group_size = HEADS // KV_HEADS
    heads_here = heads_kv * group_size
    local_blocks = cache_rows // BLOCK
    qblocks = query_count // BLOCK

    local_block = pattern - shard_index * local_blocks
    in_shard = (local_block >= 0) & (local_block < local_blocks)
    slot_rank = jnp.cumsum(in_shard.astype(jnp.int32), axis=1) - 1
    slot_ids = jnp.arange(CAP, dtype=jnp.int32)
    picked = in_shard[:, :, None] & (slot_rank[:, :, None] == slot_ids[None, None, :])
    chosen = jnp.sum(jnp.where(picked, local_block[:, :, None], 0), axis=1).astype(jnp.int32)
    live = jnp.any(picked, axis=1).astype(jnp.int32)

    mixed0, mixed1, top, total = local_attention(queries, cached_keys, chosen, live, cached_values)

    def by_row(stat):
        stat = stat.reshape(qblocks, heads_kv, group_size, BLOCK).transpose(0, 3, 1, 2)
        return stat.reshape(query_count, heads_here)

    stats = jnp.concatenate([by_row(top), by_row(total)], axis=1)
    rows_here = query_count // ctx_n
    got_stats = lax.dynamic_slice_in_dim(
        lax.all_gather(stats, "ctx"), shard_index * rows_here, rows_here, axis=1
    )
    got_stats = got_stats.reshape(ctx_n, rows_here, 2, heads_here)
    got_top, got_total = got_stats[:, :, 0], got_stats[:, :, 1]
    row_peak = got_top.max(axis=0)
    rescale = jnp.exp(got_top - row_peak[None])
    row_norm = jnp.sum(got_total * rescale, axis=0)
    half_heads = heads_here // 2
    half_width = query_width // 2
    terms = []
    for part, mixed in enumerate((mixed0, mixed1)):
        heads = slice(part * half_heads, (part + 1) * half_heads)
        got_mixed = lax.all_to_all(mixed, "ctx", split_axis=0, concat_axis=0, tiled=True)
        got_mixed = got_mixed.reshape(ctx_n, -1, half_heads, HEAD_DIM).astype(jnp.float32)
        summed = jnp.sum(got_mixed * rescale[:, :, heads, None], axis=0)
        attended = (summed / row_norm[:, heads, None]).reshape(rows_here, half_width).astype(jnp.bfloat16)
        terms.append((lax.all_gather(attended, "ctx", axis=0, tiled=True),
                      out_weight[part * half_width:(part + 1) * half_width]))

    def project(columns):
        total_out = None
        for rows, weight in terms:
            term = jnp.dot(rows, columns(weight), preferred_element_type=jnp.float32)
            total_out = term if total_out is None else total_out + term
        return total_out

    heads_n = lax.axis_size("head")
    share = out_weight.shape[1] // heads_n
    if heads_n == 2:
        sent = project(lambda w: lax.dynamic_slice_in_dim(w, (1 - head_index) * share, share, axis=1))
        got = lax.ppermute(sent.astype(jnp.bfloat16), "head", perm=[(0, 1), (1, 0)])
        kept = project(lambda w: lax.dynamic_slice_in_dim(w, head_index * share, share, axis=1))
        return (kept + got.astype(jnp.float32)).astype(jnp.bfloat16)
    partial_out = project(lambda w: w)
    pieces = partial_out.reshape(query_count, heads_n, share).transpose(1, 0, 2)
    got = lax.all_to_all(pieces.astype(jnp.bfloat16), "head", 0, 0, tiled=True)
    return got.astype(jnp.float32).sum(axis=0).astype(jnp.bfloat16)


def solution(mesh):
    return jax.shard_map(
        shards,
        mesh=mesh,
        in_specs=(
            P(("groups", "rep"), "head"),
            P(("groups", "ctx"), "head"),
            P(("groups", "ctx"), "head"),
            P(("groups", "rep"), None),
            P("head", "ctx"),
        ),
        out_specs=P(("groups", "rep"), ("ctx", "head")),
        check_vma=False,
    )
```

```python
import jax
import jax.numpy as jnp
from jax import lax
from jax.experimental import pallas as pl
from jax.experimental.pallas import tpu as pltpu
from jax.sharding import PartitionSpec as P

HEADS = 64
KV_HEADS = 8
HEAD_DIM = 128
BLOCK = 128
CAP = 8


def attend_kernel(chosen_ref, live_ref, q_ref, k_hbm, v_hbm, o0_ref, o1_ref, m_ref, l_ref, kbuf, vbuf, sem):
    b = pl.program_id(0)
    steps = pl.num_programs(0)
    heads_kv = k_hbm.shape[1] // HEAD_DIM
    group_size = q_ref.shape[1] // (heads_kv * HEAD_DIM)

    def block_copies(step, slot):
        copies = []
        for j in range(CAP):
            rows = pl.ds(pl.multiple_of(chosen_ref[step, j] * BLOCK, BLOCK), BLOCK)
            dst = pl.ds(j * BLOCK, BLOCK)
            copies.append(pltpu.make_async_copy(k_hbm.at[rows], kbuf.at[slot, dst], sem.at[slot, 0, j]))
            copies.append(pltpu.make_async_copy(v_hbm.at[rows], vbuf.at[slot, dst], sem.at[slot, 1, j]))
        return copies

    slot = b % 2

    @pl.when(b == 0)
    def _():
        for c in block_copies(b, slot):
            c.start()

    @pl.when(b + 1 < steps)
    def _():
        for c in block_copies(b + 1, 1 - slot):
            c.start()

    for c in block_copies(b, slot):
        c.wait()

    key_slot = lax.broadcasted_iota(jnp.int32, (1, CAP * BLOCK), 1) // BLOCK
    live_keys = key_slot < 0
    for j in range(CAP):
        live_keys = live_keys | ((key_slot == j) & (live_ref[b, j] > 0))
    for kv in range(heads_kv):
        base = kv * group_size * HEAD_DIM
        stacked = jnp.concatenate(
            [q_ref[:, base + g * HEAD_DIM:base + (g + 1) * HEAD_DIM] for g in range(group_size)], axis=0
        )
        keys = kbuf[slot, :, kv * HEAD_DIM:(kv + 1) * HEAD_DIM]
        scores = lax.dot_general(
            stacked, keys, (((1,), (1,)), ((), ())), preferred_element_type=jnp.float32
        ) * (HEAD_DIM ** (-0.5))
        scores = jnp.where(live_keys, scores, jnp.float32(-1e30))
        top = jnp.max(scores, axis=1, keepdims=True)
        weights = jnp.exp(scores - top)
        total = jnp.sum(weights, axis=1, keepdims=True)
        values = vbuf[slot, :, kv * HEAD_DIM:(kv + 1) * HEAD_DIM]
        mixed = jnp.dot(weights.astype(jnp.bfloat16), values, preferred_element_type=jnp.float32)
        half_width = o0_ref.shape[1]
        for g in range(group_size):
            column = base + g * HEAD_DIM
            o_ref = o0_ref if column < half_width else o1_ref
            column = column % half_width
            o_ref[:, column:column + HEAD_DIM] = mixed[g * BLOCK:(g + 1) * BLOCK].astype(o_ref.dtype)
        m_ref[0, kv] = jnp.transpose(jnp.broadcast_to(top, (top.shape[0], 128)))[0:1]
        l_ref[0, kv] = jnp.transpose(jnp.broadcast_to(total, (total.shape[0], 128)))[0:1]


def local_attention(queries, cached_keys, chosen, live, cached_values):
    query_count, query_width = queries.shape
    cache_width = cached_keys.shape[1]
    heads_kv = cache_width // HEAD_DIM
    group_size = query_width // (heads_kv * HEAD_DIM)
    qblocks = query_count // BLOCK
    stat_shape = jax.ShapeDtypeStruct((qblocks, heads_kv, 1, group_size * BLOCK), jnp.float32)
    stat_spec = pl.BlockSpec((1, heads_kv, 1, group_size * BLOCK), lambda b, c, v: (b, 0, 0, 0))
    half_shape = jax.ShapeDtypeStruct((query_count, query_width // 2), jnp.bfloat16)
    half_spec = pl.BlockSpec((BLOCK, query_width // 2), lambda b, c, v: (b, 0))
    flops = 4 * query_count * heads_kv * group_size * CAP * BLOCK * HEAD_DIM
    return pl.pallas_call(
        attend_kernel,
        out_shape=(half_shape, half_shape, stat_shape, stat_shape),
        grid_spec=pltpu.PrefetchScalarGridSpec(
            num_scalar_prefetch=2,
            grid=(qblocks,),
            in_specs=[
                pl.BlockSpec((BLOCK, query_width), lambda b, c, v: (b, 0)),
                pl.BlockSpec(memory_space=pl.ANY),
                pl.BlockSpec(memory_space=pl.ANY),
            ],
            out_specs=[half_spec, half_spec, stat_spec, stat_spec],
            scratch_shapes=[
                pltpu.VMEM((2, CAP * BLOCK, cache_width), jnp.bfloat16),
                pltpu.VMEM((2, CAP * BLOCK, cache_width), jnp.bfloat16),
                pltpu.SemaphoreType.DMA((2, 2, CAP)),
            ],
        ),
        compiler_params=pltpu.CompilerParams(dimension_semantics=("arbitrary",)),
        cost_estimate=pl.CostEstimate(
            flops=flops,
            transcendentals=query_count * heads_kv * group_size * CAP * BLOCK,
            bytes_accessed=4 * queries.size + 4 * qblocks * CAP * BLOCK * cache_width,
        ),
    )(chosen, live, queries, cached_keys, cached_values)


def shards(queries, cached_keys, cached_values, pattern, out_weight):
    shard_index = lax.axis_index("ctx")
    head_index = lax.axis_index("head")
    ctx_n = lax.axis_size("ctx")
    query_count, query_width = queries.shape
    cache_rows, cache_width = cached_keys.shape
    heads_kv = cache_width // HEAD_DIM
    group_size = HEADS // KV_HEADS
    heads_here = heads_kv * group_size
    local_blocks = cache_rows // BLOCK
    qblocks = query_count // BLOCK

    local_block = pattern - shard_index * local_blocks
    in_shard = (local_block >= 0) & (local_block < local_blocks)
    slot_rank = jnp.cumsum(in_shard.astype(jnp.int32), axis=1) - 1
    slot_ids = jnp.arange(CAP, dtype=jnp.int32)
    picked = in_shard[:, :, None] & (slot_rank[:, :, None] == slot_ids[None, None, :])
    chosen = jnp.sum(jnp.where(picked, local_block[:, :, None], 0), axis=1).astype(jnp.int32)
    live = jnp.any(picked, axis=1).astype(jnp.int32)

    mixed0, mixed1, top, total = local_attention(queries, cached_keys, chosen, live, cached_values)

    def by_row(stat):
        stat = stat.reshape(qblocks, heads_kv, group_size, BLOCK).transpose(0, 3, 1, 2)
        return stat.reshape(query_count, heads_here)

    stats = jnp.concatenate([by_row(top), by_row(total)], axis=1)
    rows_here = query_count // ctx_n
    got_stats = lax.all_to_all(stats, "ctx", split_axis=0, concat_axis=0, tiled=True)
    got_stats = got_stats.reshape(ctx_n, rows_here, 2, heads_here)
    got_top, got_total = got_stats[:, :, 0], got_stats[:, :, 1]
    row_peak = got_top.max(axis=0)
    rescale = jnp.exp(got_top - row_peak[None])
    row_norm = jnp.sum(got_total * rescale, axis=0)
    half_heads = heads_here // 2
    half_width = query_width // 2
    terms = []
    for part, mixed in enumerate((mixed0, mixed1)):
        heads = slice(part * half_heads, (part + 1) * half_heads)
        got_mixed = lax.all_to_all(mixed, "ctx", split_axis=0, concat_axis=0, tiled=True)
        got_mixed = got_mixed.reshape(ctx_n, -1, half_heads, HEAD_DIM).astype(jnp.float32)
        summed = jnp.sum(got_mixed * rescale[:, :, heads, None], axis=0)
        attended = (summed / row_norm[:, heads, None]).reshape(rows_here, half_width).astype(jnp.bfloat16)
        terms.append((lax.all_gather(attended, "ctx", axis=0, tiled=True),
                      out_weight[part * half_width:(part + 1) * half_width]))

    def project(columns):
        total_out = None
        for rows, weight in terms:
            term = jnp.dot(rows, columns(weight), preferred_element_type=jnp.float32)
            total_out = term if total_out is None else total_out + term
        return total_out

    heads_n = lax.axis_size("head")
    share = out_weight.shape[1] // heads_n
    if heads_n == 2:
        sent = project(lambda w: lax.dynamic_slice_in_dim(w, (1 - head_index) * share, share, axis=1))
        got = lax.ppermute(sent.astype(jnp.bfloat16), "head", perm=[(0, 1), (1, 0)])
        kept = project(lambda w: lax.dynamic_slice_in_dim(w, head_index * share, share, axis=1))
        return (kept + got.astype(jnp.float32)).astype(jnp.bfloat16)
    partial_out = project(lambda w: w)
    pieces = partial_out.reshape(query_count, heads_n, share).transpose(1, 0, 2)
    got = lax.all_to_all(pieces.astype(jnp.bfloat16), "head", 0, 0, tiled=True)
    return got.astype(jnp.float32).sum(axis=0).astype(jnp.bfloat16)


def solution(mesh):
    return jax.shard_map(
        shards,
        mesh=mesh,
        in_specs=(
            P(("groups", "rep"), "head"),
            P(("groups", "ctx"), "head"),
            P(("groups", "ctx"), "head"),
            P(("groups", "rep"), None),
            P("head", "ctx"),
        ),
        out_specs=P(("groups", "rep"), ("ctx", "head")),
        check_vma=False,
    )
```

```python
import functools

import jax
import jax.numpy as jnp
from jax import lax
from jax.experimental import pallas as pl
from jax.experimental.pallas import tpu as pltpu
from jax.sharding import PartitionSpec as P

HEADS = 64
KV_HEADS = 8
HEAD_DIM = 128
BLOCK = 128
CAP = 8


def attend_kernel(parts, chosen_ref, live_ref, q_ref, k_hbm, v_hbm, *refs):
    o_refs = refs[:parts]
    m_ref, l_ref, kbuf, vbuf, sem = refs[parts:]
    b = pl.program_id(0)
    steps = pl.num_programs(0)
    heads_kv = k_hbm.shape[1] // HEAD_DIM
    group_size = q_ref.shape[1] // (heads_kv * HEAD_DIM)

    def block_copies(step, slot):
        copies = []
        for j in range(CAP):
            rows = pl.ds(pl.multiple_of(chosen_ref[step, j] * BLOCK, BLOCK), BLOCK)
            dst = pl.ds(j * BLOCK, BLOCK)
            copies.append(pltpu.make_async_copy(k_hbm.at[rows], kbuf.at[slot, dst], sem.at[slot, 0, j]))
            copies.append(pltpu.make_async_copy(v_hbm.at[rows], vbuf.at[slot, dst], sem.at[slot, 1, j]))
        return copies

    slot = b % 2

    @pl.when(b == 0)
    def _():
        for c in block_copies(b, slot):
            c.start()

    @pl.when(b + 1 < steps)
    def _():
        for c in block_copies(b + 1, 1 - slot):
            c.start()

    for c in block_copies(b, slot):
        c.wait()

    key_slot = lax.broadcasted_iota(jnp.int32, (1, CAP * BLOCK), 1) // BLOCK
    live_keys = key_slot < 0
    for j in range(CAP):
        live_keys = live_keys | ((key_slot == j) & (live_ref[b, j] > 0))
    for kv in range(heads_kv):
        base = kv * group_size * HEAD_DIM
        stacked = jnp.concatenate(
            [q_ref[:, base + g * HEAD_DIM:base + (g + 1) * HEAD_DIM] for g in range(group_size)], axis=0
        )
        keys = kbuf[slot, :, kv * HEAD_DIM:(kv + 1) * HEAD_DIM]
        scores = lax.dot_general(
            stacked, keys, (((1,), (1,)), ((), ())), preferred_element_type=jnp.float32
        ) * (HEAD_DIM ** (-0.5))
        scores = jnp.where(live_keys, scores, jnp.float32(-1e30))
        top = jnp.max(scores, axis=1, keepdims=True)
        weights = jnp.exp(scores - top)
        total = jnp.sum(weights, axis=1, keepdims=True)
        values = vbuf[slot, :, kv * HEAD_DIM:(kv + 1) * HEAD_DIM]
        mixed = jnp.dot(weights.astype(jnp.bfloat16), values, preferred_element_type=jnp.float32)
        part_width = o_refs[0].shape[1]
        for g in range(group_size):
            column = base + g * HEAD_DIM
            o_ref = o_refs[column // part_width]
            column = column % part_width
            o_ref[:, column:column + HEAD_DIM] = mixed[g * BLOCK:(g + 1) * BLOCK].astype(o_ref.dtype)
        m_ref[0, kv] = jnp.transpose(jnp.broadcast_to(top, (top.shape[0], 128)))[0:1]
        l_ref[0, kv] = jnp.transpose(jnp.broadcast_to(total, (total.shape[0], 128)))[0:1]


def local_attention(queries, cached_keys, chosen, live, cached_values, parts):
    query_count, query_width = queries.shape
    cache_width = cached_keys.shape[1]
    heads_kv = cache_width // HEAD_DIM
    group_size = query_width // (heads_kv * HEAD_DIM)
    qblocks = query_count // BLOCK
    stat_shape = jax.ShapeDtypeStruct((qblocks, heads_kv, 1, group_size * BLOCK), jnp.float32)
    stat_spec = pl.BlockSpec((1, heads_kv, 1, group_size * BLOCK), lambda b, c, v: (b, 0, 0, 0))
    part_shape = jax.ShapeDtypeStruct((query_count, query_width // parts), jnp.bfloat16)
    part_spec = pl.BlockSpec((BLOCK, query_width // parts), lambda b, c, v: (b, 0))
    flops = 4 * query_count * heads_kv * group_size * CAP * BLOCK * HEAD_DIM
    return pl.pallas_call(
        functools.partial(attend_kernel, parts),
        out_shape=(part_shape,) * parts + (stat_shape, stat_shape),
        grid_spec=pltpu.PrefetchScalarGridSpec(
            num_scalar_prefetch=2,
            grid=(qblocks,),
            in_specs=[
                pl.BlockSpec((BLOCK, query_width), lambda b, c, v: (b, 0)),
                pl.BlockSpec(memory_space=pl.ANY),
                pl.BlockSpec(memory_space=pl.ANY),
            ],
            out_specs=[part_spec] * parts + [stat_spec, stat_spec],
            scratch_shapes=[
                pltpu.VMEM((2, CAP * BLOCK, cache_width), jnp.bfloat16),
                pltpu.VMEM((2, CAP * BLOCK, cache_width), jnp.bfloat16),
                pltpu.SemaphoreType.DMA((2, 2, CAP)),
            ],
        ),
        compiler_params=pltpu.CompilerParams(dimension_semantics=("arbitrary",)),
        cost_estimate=pl.CostEstimate(
            flops=flops,
            transcendentals=query_count * heads_kv * group_size * CAP * BLOCK,
            bytes_accessed=4 * queries.size + 4 * qblocks * CAP * BLOCK * cache_width,
        ),
    )(chosen, live, queries, cached_keys, cached_values)


def shards(queries, cached_keys, cached_values, pattern, out_weight):
    shard_index = lax.axis_index("ctx")
    head_index = lax.axis_index("head")
    ctx_n = lax.axis_size("ctx")
    query_count, query_width = queries.shape
    cache_rows, cache_width = cached_keys.shape
    heads_kv = cache_width // HEAD_DIM
    group_size = HEADS // KV_HEADS
    heads_here = heads_kv * group_size
    local_blocks = cache_rows // BLOCK
    qblocks = query_count // BLOCK

    local_block = pattern - shard_index * local_blocks
    in_shard = (local_block >= 0) & (local_block < local_blocks)
    slot_rank = jnp.cumsum(in_shard.astype(jnp.int32), axis=1) - 1
    slot_ids = jnp.arange(CAP, dtype=jnp.int32)
    picked = in_shard[:, :, None] & (slot_rank[:, :, None] == slot_ids[None, None, :])
    chosen = jnp.sum(jnp.where(picked, local_block[:, :, None], 0), axis=1).astype(jnp.int32)
    live = jnp.any(picked, axis=1).astype(jnp.int32)

    parts = heads_kv
    outs = local_attention(queries, cached_keys, chosen, live, cached_values, parts)
    mixed_parts, top, total = outs[:parts], outs[parts], outs[parts + 1]

    def by_row(stat):
        stat = stat.reshape(qblocks, heads_kv, group_size, BLOCK).transpose(0, 3, 1, 2)
        return stat.reshape(query_count, heads_here)

    stats = jnp.concatenate([by_row(top), by_row(total)], axis=1)
    rows_here = query_count // ctx_n
    got_stats = lax.all_to_all(stats, "ctx", split_axis=0, concat_axis=0, tiled=True)
    got_stats = got_stats.reshape(ctx_n, rows_here, 2, heads_here)
    got_top, got_total = got_stats[:, :, 0], got_stats[:, :, 1]
    row_peak = got_top.max(axis=0)
    rescale = jnp.exp(got_top - row_peak[None])
    row_norm = jnp.sum(got_total * rescale, axis=0)
    half_heads = heads_here // parts
    half_width = query_width // parts
    terms = []
    for part, mixed in enumerate(mixed_parts):
        heads = slice(part * half_heads, (part + 1) * half_heads)
        got_mixed = lax.all_to_all(mixed, "ctx", split_axis=0, concat_axis=0, tiled=True)
        got_mixed = got_mixed.reshape(ctx_n, -1, half_heads, HEAD_DIM).astype(jnp.float32)
        summed = jnp.sum(got_mixed * rescale[:, :, heads, None], axis=0)
        attended = (summed / row_norm[:, heads, None]).reshape(rows_here, half_width).astype(jnp.bfloat16)
        terms.append((lax.all_gather(attended, "ctx", axis=0, tiled=True),
                      out_weight[part * half_width:(part + 1) * half_width]))

    def project(columns):
        total_out = None
        for rows, weight in terms:
            term = jnp.dot(rows, columns(weight), preferred_element_type=jnp.float32)
            total_out = term if total_out is None else total_out + term
        return total_out

    heads_n = lax.axis_size("head")
    share = out_weight.shape[1] // heads_n
    if heads_n == 2:
        sent = project(lambda w: lax.dynamic_slice_in_dim(w, (1 - head_index) * share, share, axis=1))
        got = lax.ppermute(sent.astype(jnp.bfloat16), "head", perm=[(0, 1), (1, 0)])
        kept = project(lambda w: lax.dynamic_slice_in_dim(w, head_index * share, share, axis=1))
        return (kept + got.astype(jnp.float32)).astype(jnp.bfloat16)
    partial_out = project(lambda w: w)
    pieces = partial_out.reshape(query_count, heads_n, share).transpose(1, 0, 2)
    got = lax.all_to_all(pieces.astype(jnp.bfloat16), "head", 0, 0, tiled=True)
    return got.astype(jnp.float32).sum(axis=0).astype(jnp.bfloat16)


def solution(mesh):
    return jax.shard_map(
        shards,
        mesh=mesh,
        in_specs=(
            P(("groups", "rep"), "head"),
            P(("groups", "ctx"), "head"),
            P(("groups", "ctx"), "head"),
            P(("groups", "rep"), None),
            P("head", "ctx"),
        ),
        out_specs=P(("groups", "rep"), ("ctx", "head")),
        check_vma=False,
    )
```

```python
import functools

import jax
import jax.numpy as jnp
from jax import lax
from jax.experimental import pallas as pl
from jax.experimental.pallas import tpu as pltpu
from jax.sharding import PartitionSpec as P

HEADS = 64
KV_HEADS = 8
HEAD_DIM = 128
BLOCK = 128
CAP = 8


def attend_kernel(kv_first, chosen_ref, live_ref, q_ref, k_hbm, v_hbm, o_ref, m_ref, l_ref, kbuf, vbuf, sem):
    b = pl.program_id(0)
    steps = pl.num_programs(0)
    heads_kv = m_ref.shape[1]
    group_size = q_ref.shape[1] // (heads_kv * HEAD_DIM)

    def block_copies(step, slot):
        copies = []
        for j in range(CAP):
            rows = pl.ds(pl.multiple_of(chosen_ref[step, j] * BLOCK, BLOCK), BLOCK)
            dst = pl.ds(j * BLOCK, BLOCK)
            copies.append(pltpu.make_async_copy(k_hbm.at[rows], kbuf.at[slot, dst], sem.at[slot, 0, j]))
            copies.append(pltpu.make_async_copy(v_hbm.at[rows], vbuf.at[slot, dst], sem.at[slot, 1, j]))
        return copies

    slot = b % 2

    @pl.when(b == 0)
    def _():
        for c in block_copies(b, slot):
            c.start()

    @pl.when(b + 1 < steps)
    def _():
        for c in block_copies(b + 1, 1 - slot):
            c.start()

    for c in block_copies(b, slot):
        c.wait()

    key_slot = lax.broadcasted_iota(jnp.int32, (1, CAP * BLOCK), 1) // BLOCK
    live_keys = key_slot < 0
    for j in range(CAP):
        live_keys = live_keys | ((key_slot == j) & (live_ref[b, j] > 0))
    for kv in range(heads_kv):
        base = kv * group_size * HEAD_DIM
        stacked = jnp.concatenate(
            [q_ref[:, base + g * HEAD_DIM:base + (g + 1) * HEAD_DIM] for g in range(group_size)], axis=0
        )
        column = (kv_first + kv) * HEAD_DIM
        keys = kbuf[slot, :, column:column + HEAD_DIM]
        scores = lax.dot_general(
            stacked, keys, (((1,), (1,)), ((), ())), preferred_element_type=jnp.float32
        ) * (HEAD_DIM ** (-0.5))
        scores = jnp.where(live_keys, scores, jnp.float32(-1e30))
        top = jnp.max(scores, axis=1, keepdims=True)
        weights = jnp.exp(scores - top)
        total = jnp.sum(weights, axis=1, keepdims=True)
        values = vbuf[slot, :, column:column + HEAD_DIM]
        mixed = jnp.dot(weights.astype(jnp.bfloat16), values, preferred_element_type=jnp.float32)
        for g in range(group_size):
            o_ref[:, base + g * HEAD_DIM:base + (g + 1) * HEAD_DIM] = (
                mixed[g * BLOCK:(g + 1) * BLOCK].astype(o_ref.dtype)
            )
        m_ref[0, kv] = jnp.transpose(jnp.broadcast_to(top, (top.shape[0], 128)))[0:1]
        l_ref[0, kv] = jnp.transpose(jnp.broadcast_to(total, (total.shape[0], 128)))[0:1]


def local_attention(queries, cached_keys, chosen, live, cached_values, kv_first, heads_kv):
    query_count = queries.shape[0]
    cache_width = cached_keys.shape[1]
    group_size = HEADS // KV_HEADS
    query_width = heads_kv * group_size * HEAD_DIM
    part = kv_first // heads_kv
    qblocks = query_count // BLOCK
    stat_shape = jax.ShapeDtypeStruct((qblocks, heads_kv, 1, group_size * BLOCK), jnp.float32)
    stat_spec = pl.BlockSpec((1, heads_kv, 1, group_size * BLOCK), lambda b, c, v: (b, 0, 0, 0))
    flops = 4 * query_count * heads_kv * group_size * CAP * BLOCK * HEAD_DIM
    return pl.pallas_call(
        functools.partial(attend_kernel, kv_first),
        out_shape=(jax.ShapeDtypeStruct((query_count, query_width), jnp.bfloat16), stat_shape, stat_shape),
        grid_spec=pltpu.PrefetchScalarGridSpec(
            num_scalar_prefetch=2,
            grid=(qblocks,),
            in_specs=[
                pl.BlockSpec((BLOCK, query_width), lambda b, c, v: (b, part)),
                pl.BlockSpec(memory_space=pl.ANY),
                pl.BlockSpec(memory_space=pl.ANY),
            ],
            out_specs=[pl.BlockSpec((BLOCK, query_width), lambda b, c, v: (b, 0)), stat_spec, stat_spec],
            scratch_shapes=[
                pltpu.VMEM((2, CAP * BLOCK, cache_width), jnp.bfloat16),
                pltpu.VMEM((2, CAP * BLOCK, cache_width), jnp.bfloat16),
                pltpu.SemaphoreType.DMA((2, 2, CAP)),
            ],
        ),
        compiler_params=pltpu.CompilerParams(dimension_semantics=("arbitrary",)),
        cost_estimate=pl.CostEstimate(
            flops=flops,
            transcendentals=query_count * heads_kv * group_size * CAP * BLOCK,
            bytes_accessed=2 * query_count * query_width + 4 * qblocks * CAP * BLOCK * cache_width,
        ),
    )(chosen, live, queries, cached_keys, cached_values)


def shards(queries, cached_keys, cached_values, pattern, out_weight):
    shard_index = lax.axis_index("ctx")
    head_index = lax.axis_index("head")
    ctx_n = lax.axis_size("ctx")
    query_count, query_width = queries.shape
    cache_rows, cache_width = cached_keys.shape
    heads_kv = cache_width // HEAD_DIM
    group_size = HEADS // KV_HEADS
    heads_here = heads_kv * group_size
    local_blocks = cache_rows // BLOCK
    qblocks = query_count // BLOCK

    local_block = pattern - shard_index * local_blocks
    in_shard = (local_block >= 0) & (local_block < local_blocks)
    slot_rank = jnp.cumsum(in_shard.astype(jnp.int32), axis=1) - 1
    slot_ids = jnp.arange(CAP, dtype=jnp.int32)
    picked = in_shard[:, :, None] & (slot_rank[:, :, None] == slot_ids[None, None, :])
    chosen = jnp.sum(jnp.where(picked, local_block[:, :, None], 0), axis=1).astype(jnp.int32)
    live = jnp.any(picked, axis=1).astype(jnp.int32)

    parts = heads_kv
    outs = [
        local_attention(queries, cached_keys, chosen, live, cached_values, part, 1)
        for part in range(parts)
    ]
    mixed_parts = [out[0] for out in outs]
    top = jnp.concatenate([out[1] for out in outs], axis=1)
    total = jnp.concatenate([out[2] for out in outs], axis=1)

    def by_row(stat):
        stat = stat.reshape(qblocks, heads_kv, group_size, BLOCK).transpose(0, 3, 1, 2)
        return stat.reshape(query_count, heads_here)

    stats = jnp.concatenate([by_row(top), by_row(total)], axis=1)
    rows_here = query_count // ctx_n
    own = lax.dynamic_slice_in_dim(stats, shard_index * rows_here, rows_here, axis=0)
    by_shift = [own]
    for shift in range(1, ctx_n):
        target = lax.rem(shard_index + shift, ctx_n)
        chunk = lax.dynamic_slice_in_dim(stats, target * rows_here, rows_here, axis=0)
        pairs = [(src, (src + shift) % ctx_n) for src in range(ctx_n)]
        by_shift.append(lax.ppermute(chunk, "ctx", perm=pairs))
    sources = lax.rem(shard_index - jnp.arange(ctx_n, dtype=jnp.int32) + ctx_n, ctx_n)
    got_stats = jnp.take(jnp.stack(by_shift), sources, axis=0)
    got_stats = got_stats.reshape(ctx_n, rows_here, 2, heads_here)
    got_top, got_total = got_stats[:, :, 0], got_stats[:, :, 1]
    row_peak = got_top.max(axis=0)
    rescale = jnp.exp(got_top - row_peak[None])
    row_norm = jnp.sum(got_total * rescale, axis=0)
    half_heads = heads_here // parts
    half_width = query_width // parts
    terms = []
    for part, mixed in enumerate(mixed_parts):
        heads = slice(part * half_heads, (part + 1) * half_heads)
        got_mixed = lax.all_to_all(mixed, "ctx", split_axis=0, concat_axis=0, tiled=True)
        got_mixed = got_mixed.reshape(ctx_n, -1, half_heads, HEAD_DIM).astype(jnp.float32)
        summed = jnp.sum(got_mixed * rescale[:, :, heads, None], axis=0)
        attended = (summed / row_norm[:, heads, None]).reshape(rows_here, half_width).astype(jnp.bfloat16)
        terms.append((lax.all_gather(attended, "ctx", axis=0, tiled=True),
                      out_weight[part * half_width:(part + 1) * half_width]))

    def project(columns):
        total_out = None
        for rows, weight in terms:
            term = jnp.dot(rows, columns(weight), preferred_element_type=jnp.float32)
            total_out = term if total_out is None else total_out + term
        return total_out

    heads_n = lax.axis_size("head")
    share = out_weight.shape[1] // heads_n
    if heads_n == 2:
        sent = project(lambda w: lax.dynamic_slice_in_dim(w, (1 - head_index) * share, share, axis=1))
        got = lax.ppermute(sent.astype(jnp.bfloat16), "head", perm=[(0, 1), (1, 0)])
        kept = project(lambda w: lax.dynamic_slice_in_dim(w, head_index * share, share, axis=1))
        return (kept + got.astype(jnp.float32)).astype(jnp.bfloat16)
    partial_out = project(lambda w: w)
    pieces = partial_out.reshape(query_count, heads_n, share).transpose(1, 0, 2)
    got = lax.all_to_all(pieces.astype(jnp.bfloat16), "head", 0, 0, tiled=True)
    return got.astype(jnp.float32).sum(axis=0).astype(jnp.bfloat16)


def solution(mesh):
    return jax.shard_map(
        shards,
        mesh=mesh,
        in_specs=(
            P(("groups", "rep"), "head"),
            P(("groups", "ctx"), "head"),
            P(("groups", "ctx"), "head"),
            P(("groups", "rep"), None),
            P("head", "ctx"),
        ),
        out_specs=P(("groups", "rep"), ("ctx", "head")),
        check_vma=False,
    )
```

```python
import functools

import jax
import jax.numpy as jnp
from jax import lax
from jax.experimental import pallas as pl
from jax.experimental.pallas import tpu as pltpu
from jax.sharding import PartitionSpec as P

HEADS = 64
KV_HEADS = 8
HEAD_DIM = 128
BLOCK = 128
CAP = 8


def attend_kernel(kv_first, chosen_ref, live_ref, q_ref, k_hbm, v_hbm, o_ref, m_ref, l_ref, kbuf, vbuf, sem):
    b = pl.program_id(0)
    steps = pl.num_programs(0)
    heads_kv = m_ref.shape[1]
    group_size = q_ref.shape[1] // (heads_kv * HEAD_DIM)

    cols = pl.ds(kv_first * HEAD_DIM, heads_kv * HEAD_DIM)

    def block_copies(step, slot):
        copies = []
        for j in range(CAP):
            rows = pl.ds(pl.multiple_of(chosen_ref[step, j] * BLOCK, BLOCK), BLOCK)
            dst = pl.ds(j * BLOCK, BLOCK)
            copies.append(pltpu.make_async_copy(k_hbm.at[rows, cols], kbuf.at[slot, dst], sem.at[slot, 0, j]))
            copies.append(pltpu.make_async_copy(v_hbm.at[rows, cols], vbuf.at[slot, dst], sem.at[slot, 1, j]))
        return copies

    slot = b % 2

    @pl.when(b == 0)
    def _():
        for c in block_copies(b, slot):
            c.start()

    @pl.when(b + 1 < steps)
    def _():
        for c in block_copies(b + 1, 1 - slot):
            c.start()

    for c in block_copies(b, slot):
        c.wait()

    key_slot = lax.broadcasted_iota(jnp.int32, (1, CAP * BLOCK), 1) // BLOCK
    live_keys = key_slot < 0
    for j in range(CAP):
        live_keys = live_keys | ((key_slot == j) & (live_ref[b, j] > 0))
    for kv in range(heads_kv):
        base = kv * group_size * HEAD_DIM
        stacked = jnp.concatenate(
            [q_ref[:, base + g * HEAD_DIM:base + (g + 1) * HEAD_DIM] for g in range(group_size)], axis=0
        )
        column = kv * HEAD_DIM
        keys = kbuf[slot, :, column:column + HEAD_DIM]
        scores = lax.dot_general(
            stacked, keys, (((1,), (1,)), ((), ())), preferred_element_type=jnp.float32
        ) * (HEAD_DIM ** (-0.5))
        scores = jnp.where(live_keys, scores, jnp.float32(-1e30))
        top = jnp.max(scores, axis=1, keepdims=True)
        weights = jnp.exp(scores - top)
        total = jnp.sum(weights, axis=1, keepdims=True)
        values = vbuf[slot, :, column:column + HEAD_DIM]
        mixed = jnp.dot(weights.astype(jnp.bfloat16), values, preferred_element_type=jnp.float32)
        for g in range(group_size):
            o_ref[:, base + g * HEAD_DIM:base + (g + 1) * HEAD_DIM] = (
                mixed[g * BLOCK:(g + 1) * BLOCK].astype(o_ref.dtype)
            )
        m_ref[0, kv] = jnp.transpose(jnp.broadcast_to(top, (top.shape[0], 128)))[0:1]
        l_ref[0, kv] = jnp.transpose(jnp.broadcast_to(total, (total.shape[0], 128)))[0:1]


def local_attention(queries, cached_keys, chosen, live, cached_values, kv_first, heads_kv):
    query_count = queries.shape[0]
    cache_width = cached_keys.shape[1]
    group_size = HEADS // KV_HEADS
    query_width = heads_kv * group_size * HEAD_DIM
    part = kv_first // heads_kv
    qblocks = query_count // BLOCK
    stat_shape = jax.ShapeDtypeStruct((qblocks, heads_kv, 1, group_size * BLOCK), jnp.float32)
    stat_spec = pl.BlockSpec((1, heads_kv, 1, group_size * BLOCK), lambda b, c, v: (b, 0, 0, 0))
    flops = 4 * query_count * heads_kv * group_size * CAP * BLOCK * HEAD_DIM
    return pl.pallas_call(
        functools.partial(attend_kernel, kv_first),
        out_shape=(jax.ShapeDtypeStruct((query_count, query_width), jnp.bfloat16), stat_shape, stat_shape),
        grid_spec=pltpu.PrefetchScalarGridSpec(
            num_scalar_prefetch=2,
            grid=(qblocks,),
            in_specs=[
                pl.BlockSpec((BLOCK, query_width), lambda b, c, v: (b, part)),
                pl.BlockSpec(memory_space=pl.ANY),
                pl.BlockSpec(memory_space=pl.ANY),
            ],
            out_specs=[pl.BlockSpec((BLOCK, query_width), lambda b, c, v: (b, 0)), stat_spec, stat_spec],
            scratch_shapes=[
                pltpu.VMEM((2, CAP * BLOCK, heads_kv * HEAD_DIM), jnp.bfloat16),
                pltpu.VMEM((2, CAP * BLOCK, heads_kv * HEAD_DIM), jnp.bfloat16),
                pltpu.SemaphoreType.DMA((2, 2, CAP)),
            ],
        ),
        compiler_params=pltpu.CompilerParams(dimension_semantics=("arbitrary",)),
        cost_estimate=pl.CostEstimate(
            flops=flops,
            transcendentals=query_count * heads_kv * group_size * CAP * BLOCK,
            bytes_accessed=2 * query_count * query_width + 4 * qblocks * CAP * BLOCK * heads_kv * HEAD_DIM,
        ),
    )(chosen, live, queries, cached_keys, cached_values)


def shards(queries, cached_keys, cached_values, pattern, out_weight):
    shard_index = lax.axis_index("ctx")
    head_index = lax.axis_index("head")
    ctx_n = lax.axis_size("ctx")
    query_count, query_width = queries.shape
    cache_rows, cache_width = cached_keys.shape
    heads_kv = cache_width // HEAD_DIM
    group_size = HEADS // KV_HEADS
    heads_here = heads_kv * group_size
    local_blocks = cache_rows // BLOCK
    qblocks = query_count // BLOCK

    local_block = pattern - shard_index * local_blocks
    in_shard = (local_block >= 0) & (local_block < local_blocks)
    slot_rank = jnp.cumsum(in_shard.astype(jnp.int32), axis=1) - 1
    slot_ids = jnp.arange(CAP, dtype=jnp.int32)
    picked = in_shard[:, :, None] & (slot_rank[:, :, None] == slot_ids[None, None, :])
    chosen = jnp.sum(jnp.where(picked, local_block[:, :, None], 0), axis=1).astype(jnp.int32)
    live = jnp.any(picked, axis=1).astype(jnp.int32)

    parts = heads_kv
    outs = [
        local_attention(queries, cached_keys, chosen, live, cached_values, part, 1)
        for part in range(parts)
    ]
    mixed_parts = [out[0] for out in outs]
    top = jnp.concatenate([out[1] for out in outs], axis=1)
    total = jnp.concatenate([out[2] for out in outs], axis=1)

    def by_row(stat):
        stat = stat.reshape(qblocks, heads_kv, group_size, BLOCK).transpose(0, 3, 1, 2)
        return stat.reshape(query_count, heads_here)

    stats = jnp.concatenate([by_row(top), by_row(total)], axis=1)
    rows_here = query_count // ctx_n
    own = lax.dynamic_slice_in_dim(stats, shard_index * rows_here, rows_here, axis=0)
    by_shift = [own]
    for shift in range(1, ctx_n):
        target = lax.rem(shard_index + shift, ctx_n)
        chunk = lax.dynamic_slice_in_dim(stats, target * rows_here, rows_here, axis=0)
        pairs = [(src, (src + shift) % ctx_n) for src in range(ctx_n)]
        by_shift.append(lax.ppermute(chunk, "ctx", perm=pairs))
    sources = lax.rem(shard_index - jnp.arange(ctx_n, dtype=jnp.int32) + ctx_n, ctx_n)
    got_stats = jnp.take(jnp.stack(by_shift), sources, axis=0)
    got_stats = got_stats.reshape(ctx_n, rows_here, 2, heads_here)
    got_top, got_total = got_stats[:, :, 0], got_stats[:, :, 1]
    row_peak = got_top.max(axis=0)
    rescale = jnp.exp(got_top - row_peak[None])
    row_norm = jnp.sum(got_total * rescale, axis=0)
    half_heads = heads_here // parts
    half_width = query_width // parts
    terms = []
    for part, mixed in enumerate(mixed_parts):
        heads = slice(part * half_heads, (part + 1) * half_heads)
        got_mixed = lax.all_to_all(mixed, "ctx", split_axis=0, concat_axis=0, tiled=True)
        got_mixed = got_mixed.reshape(ctx_n, -1, half_heads, HEAD_DIM).astype(jnp.float32)
        summed = jnp.sum(got_mixed * rescale[:, :, heads, None], axis=0)
        attended = (summed / row_norm[:, heads, None]).reshape(rows_here, half_width).astype(jnp.bfloat16)
        terms.append((lax.all_gather(attended, "ctx", axis=0, tiled=True),
                      out_weight[part * half_width:(part + 1) * half_width]))

    def project(columns):
        total_out = None
        for rows, weight in terms:
            term = jnp.dot(rows, columns(weight), preferred_element_type=jnp.float32)
            total_out = term if total_out is None else total_out + term
        return total_out

    heads_n = lax.axis_size("head")
    share = out_weight.shape[1] // heads_n
    if heads_n == 2:
        sent = project(lambda w: lax.dynamic_slice_in_dim(w, (1 - head_index) * share, share, axis=1))
        got = lax.ppermute(sent.astype(jnp.bfloat16), "head", perm=[(0, 1), (1, 0)])
        kept = project(lambda w: lax.dynamic_slice_in_dim(w, head_index * share, share, axis=1))
        return (kept + got.astype(jnp.float32)).astype(jnp.bfloat16)
    partial_out = project(lambda w: w)
    pieces = partial_out.reshape(query_count, heads_n, share).transpose(1, 0, 2)
    got = lax.all_to_all(pieces.astype(jnp.bfloat16), "head", 0, 0, tiled=True)
    return got.astype(jnp.float32).sum(axis=0).astype(jnp.bfloat16)


def solution(mesh):
    return jax.shard_map(
        shards,
        mesh=mesh,
        in_specs=(
            P(("groups", "rep"), "head"),
            P(("groups", "ctx"), "head"),
            P(("groups", "ctx"), "head"),
            P(("groups", "rep"), None),
            P("head", "ctx"),
        ),
        out_specs=P(("groups", "rep"), ("ctx", "head")),
        check_vma=False,
    )
```

```python
import functools

import jax
import jax.numpy as jnp
from jax import lax
from jax.experimental import pallas as pl
from jax.experimental.pallas import tpu as pltpu
from jax.sharding import PartitionSpec as P

HEADS = 64
KV_HEADS = 8
HEAD_DIM = 128
BLOCK = 128
CAP = 8


def attend_kernel(kv_first, chosen_ref, live_ref, q_ref, k_hbm, v_hbm, o_ref, m_ref, l_ref, kbuf, vbuf, sem):
    b = pl.program_id(0)
    steps = pl.num_programs(0)
    heads_kv = m_ref.shape[1]
    group_size = q_ref.shape[1] // (heads_kv * HEAD_DIM)

    cols = pl.ds(kv_first * HEAD_DIM, heads_kv * HEAD_DIM)

    def block_copies(step, slot):
        copies = []
        for j in range(CAP):
            rows = pl.ds(pl.multiple_of(chosen_ref[step, j] * BLOCK, BLOCK), BLOCK)
            dst = pl.ds(j * BLOCK, BLOCK)
            copies.append(pltpu.make_async_copy(k_hbm.at[rows, cols], kbuf.at[slot, dst], sem.at[slot, 0, j]))
            copies.append(pltpu.make_async_copy(v_hbm.at[rows, cols], vbuf.at[slot, dst], sem.at[slot, 1, j]))
        return copies

    slot = b % 2

    @pl.when(b == 0)
    def _():
        for c in block_copies(b, slot):
            c.start()

    @pl.when(b + 1 < steps)
    def _():
        for c in block_copies(b + 1, 1 - slot):
            c.start()

    for c in block_copies(b, slot):
        c.wait()

    key_slot = lax.broadcasted_iota(jnp.int32, (1, CAP * BLOCK), 1) // BLOCK
    live_keys = key_slot < 0
    for j in range(CAP):
        live_keys = live_keys | ((key_slot == j) & (live_ref[b, j] > 0))
    for kv in range(heads_kv):
        base = kv * group_size * HEAD_DIM
        stacked = jnp.concatenate(
            [q_ref[:, base + g * HEAD_DIM:base + (g + 1) * HEAD_DIM] for g in range(group_size)], axis=0
        )
        column = kv * HEAD_DIM
        keys = kbuf[slot, :, column:column + HEAD_DIM]
        scores = lax.dot_general(
            stacked, keys, (((1,), (1,)), ((), ())), preferred_element_type=jnp.float32
        ) * (HEAD_DIM ** (-0.5))
        scores = jnp.where(live_keys, scores, jnp.float32(-1e30))
        top = jnp.max(scores, axis=1, keepdims=True)
        weights = jnp.exp(scores - top)
        total = jnp.sum(weights, axis=1, keepdims=True)
        values = vbuf[slot, :, column:column + HEAD_DIM]
        mixed = jnp.dot(weights.astype(jnp.bfloat16), values, preferred_element_type=jnp.float32)
        for g in range(group_size):
            o_ref[:, base + g * HEAD_DIM:base + (g + 1) * HEAD_DIM] = (
                mixed[g * BLOCK:(g + 1) * BLOCK].astype(o_ref.dtype)
            )
        m_ref[0, kv] = jnp.transpose(jnp.broadcast_to(top, (top.shape[0], 128)))[0:1]
        l_ref[0, kv] = jnp.transpose(jnp.broadcast_to(total, (total.shape[0], 128)))[0:1]


def local_attention(queries, cached_keys, chosen, live, cached_values, kv_first, heads_kv):
    query_count = queries.shape[0]
    cache_width = cached_keys.shape[1]
    group_size = HEADS // KV_HEADS
    query_width = heads_kv * group_size * HEAD_DIM
    part = kv_first // heads_kv
    qblocks = query_count // BLOCK
    stat_shape = jax.ShapeDtypeStruct((qblocks, heads_kv, 1, group_size * BLOCK), jnp.float32)
    stat_spec = pl.BlockSpec((1, heads_kv, 1, group_size * BLOCK), lambda b, c, v: (b, 0, 0, 0))
    flops = 4 * query_count * heads_kv * group_size * CAP * BLOCK * HEAD_DIM
    return pl.pallas_call(
        functools.partial(attend_kernel, kv_first),
        out_shape=(jax.ShapeDtypeStruct((query_count, query_width), jnp.bfloat16), stat_shape, stat_shape),
        grid_spec=pltpu.PrefetchScalarGridSpec(
            num_scalar_prefetch=2,
            grid=(qblocks,),
            in_specs=[
                pl.BlockSpec((BLOCK, query_width), lambda b, c, v: (b, part)),
                pl.BlockSpec(memory_space=pl.ANY),
                pl.BlockSpec(memory_space=pl.ANY),
            ],
            out_specs=[pl.BlockSpec((BLOCK, query_width), lambda b, c, v: (b, 0)), stat_spec, stat_spec],
            scratch_shapes=[
                pltpu.VMEM((2, CAP * BLOCK, heads_kv * HEAD_DIM), jnp.bfloat16),
                pltpu.VMEM((2, CAP * BLOCK, heads_kv * HEAD_DIM), jnp.bfloat16),
                pltpu.SemaphoreType.DMA((2, 2, CAP)),
            ],
        ),
        compiler_params=pltpu.CompilerParams(dimension_semantics=("arbitrary",)),
        cost_estimate=pl.CostEstimate(
            flops=flops,
            transcendentals=query_count * heads_kv * group_size * CAP * BLOCK,
            bytes_accessed=2 * query_count * query_width + 4 * qblocks * CAP * BLOCK * heads_kv * HEAD_DIM,
        ),
    )(chosen, live, queries, cached_keys, cached_values)


def shards(queries, cached_keys, cached_values, pattern, out_weight):
    shard_index = lax.axis_index("ctx")
    head_index = lax.axis_index("head")
    ctx_n = lax.axis_size("ctx")
    query_count, query_width = queries.shape
    cache_rows, cache_width = cached_keys.shape
    heads_kv = cache_width // HEAD_DIM
    group_size = HEADS // KV_HEADS
    heads_here = heads_kv * group_size
    local_blocks = cache_rows // BLOCK
    qblocks = query_count // BLOCK

    local_block = pattern - shard_index * local_blocks
    in_shard = (local_block >= 0) & (local_block < local_blocks)
    slot_rank = jnp.cumsum(in_shard.astype(jnp.int32), axis=1) - 1
    slot_ids = jnp.arange(CAP, dtype=jnp.int32)
    picked = in_shard[:, :, None] & (slot_rank[:, :, None] == slot_ids[None, None, :])
    chosen = jnp.sum(jnp.where(picked, local_block[:, :, None], 0), axis=1).astype(jnp.int32)
    live = jnp.any(picked, axis=1).astype(jnp.int32)

    parts = heads_kv
    outs = [
        local_attention(queries, cached_keys, chosen, live, cached_values, part, 1)
        for part in range(parts)
    ]
    part_heads = heads_here // parts
    part_width = query_width // parts
    rows_here = query_count // ctx_n
    sources = lax.rem(shard_index - jnp.arange(ctx_n, dtype=jnp.int32) + ctx_n, ctx_n)

    def by_row(stat):
        stat = stat.reshape(qblocks, 1, group_size, BLOCK).transpose(0, 3, 1, 2)
        return stat.reshape(query_count, part_heads)

    terms = []
    for part, (mixed, top, total) in enumerate(outs):
        stats = jnp.concatenate([by_row(top), by_row(total)], axis=1)
        by_shift = [lax.dynamic_slice_in_dim(stats, shard_index * rows_here, rows_here, axis=0)]
        for shift in range(1, ctx_n):
            target = lax.rem(shard_index + shift, ctx_n)
            chunk = lax.dynamic_slice_in_dim(stats, target * rows_here, rows_here, axis=0)
            pairs = [(src, (src + shift) % ctx_n) for src in range(ctx_n)]
            by_shift.append(lax.ppermute(chunk, "ctx", perm=pairs))
        got_stats = jnp.take(jnp.stack(by_shift), sources, axis=0)
        got_stats = got_stats.reshape(ctx_n, rows_here, 2, part_heads)
        got_top, got_total = got_stats[:, :, 0], got_stats[:, :, 1]
        row_peak = got_top.max(axis=0)
        rescale = jnp.exp(got_top - row_peak[None])
        row_norm = jnp.sum(got_total * rescale, axis=0)
        got_mixed = lax.all_to_all(mixed, "ctx", split_axis=0, concat_axis=0, tiled=True)
        got_mixed = got_mixed.reshape(ctx_n, -1, part_heads, HEAD_DIM).astype(jnp.float32)
        summed = jnp.sum(got_mixed * rescale[..., None], axis=0)
        attended = (summed / row_norm[:, :, None]).reshape(rows_here, part_width).astype(jnp.bfloat16)
        terms.append((lax.all_gather(attended, "ctx", axis=0, tiled=True),
                      out_weight[part * part_width:(part + 1) * part_width]))

    def project(columns):
        total_out = None
        for rows, weight in terms:
            term = jnp.dot(rows, columns(weight), preferred_element_type=jnp.float32)
            total_out = term if total_out is None else total_out + term
        return total_out

    heads_n = lax.axis_size("head")
    share = out_weight.shape[1] // heads_n
    if heads_n == 2:
        sent = project(lambda w: lax.dynamic_slice_in_dim(w, (1 - head_index) * share, share, axis=1))
        got = lax.ppermute(sent.astype(jnp.bfloat16), "head", perm=[(0, 1), (1, 0)])
        kept = project(lambda w: lax.dynamic_slice_in_dim(w, head_index * share, share, axis=1))
        return (kept + got.astype(jnp.float32)).astype(jnp.bfloat16)
    partial_out = project(lambda w: w)
    pieces = partial_out.reshape(query_count, heads_n, share).transpose(1, 0, 2)
    got = lax.all_to_all(pieces.astype(jnp.bfloat16), "head", 0, 0, tiled=True)
    return got.astype(jnp.float32).sum(axis=0).astype(jnp.bfloat16)


def solution(mesh):
    return jax.shard_map(
        shards,
        mesh=mesh,
        in_specs=(
            P(("groups", "rep"), "head"),
            P(("groups", "ctx"), "head"),
            P(("groups", "ctx"), "head"),
            P(("groups", "rep"), None),
            P("head", "ctx"),
        ),
        out_specs=P(("groups", "rep"), ("ctx", "head")),
        check_vma=False,
    )
```

```python
import functools

import jax
import jax.numpy as jnp
from jax import lax
from jax.experimental import pallas as pl
from jax.experimental.pallas import tpu as pltpu
from jax.sharding import PartitionSpec as P

HEADS = 64
KV_HEADS = 8
HEAD_DIM = 128
BLOCK = 128
CAP = 8


def attend_kernel(kv_first, chosen_ref, live_ref, q_ref, k_hbm, v_hbm, o_ref, m_ref, l_ref, kbuf, vbuf, sem):
    b = pl.program_id(0)
    steps = pl.num_programs(0)
    heads_kv = m_ref.shape[1]
    group_size = q_ref.shape[1] // (heads_kv * HEAD_DIM)

    cols = pl.ds(kv_first * HEAD_DIM, heads_kv * HEAD_DIM)

    def block_copies(step, slot):
        copies = []
        for j in range(CAP):
            rows = pl.ds(pl.multiple_of(chosen_ref[step, j] * BLOCK, BLOCK), BLOCK)
            dst = pl.ds(j * BLOCK, BLOCK)
            copies.append(pltpu.make_async_copy(k_hbm.at[rows, cols], kbuf.at[slot, dst], sem.at[slot, 0, j]))
            copies.append(pltpu.make_async_copy(v_hbm.at[rows, cols], vbuf.at[slot, dst], sem.at[slot, 1, j]))
        return copies

    slot = b % 2

    @pl.when(b == 0)
    def _():
        for c in block_copies(b, slot):
            c.start()

    @pl.when(b + 1 < steps)
    def _():
        for c in block_copies(b + 1, 1 - slot):
            c.start()

    for c in block_copies(b, slot):
        c.wait()

    key_slot = lax.broadcasted_iota(jnp.int32, (1, CAP * BLOCK), 1) // BLOCK
    live_keys = key_slot < 0
    for j in range(CAP):
        live_keys = live_keys | ((key_slot == j) & (live_ref[b, j] > 0))
    for kv in range(heads_kv):
        base = kv * group_size * HEAD_DIM
        stacked = jnp.concatenate(
            [q_ref[:, base + g * HEAD_DIM:base + (g + 1) * HEAD_DIM] for g in range(group_size)], axis=0
        )
        column = kv * HEAD_DIM
        keys = kbuf[slot, :, column:column + HEAD_DIM]
        scores = lax.dot_general(
            stacked, keys, (((1,), (1,)), ((), ())), preferred_element_type=jnp.float32
        ) * (HEAD_DIM ** (-0.5))
        scores = jnp.where(live_keys, scores, jnp.float32(-1e30))
        top = jnp.max(scores, axis=1, keepdims=True)
        weights = jnp.exp(scores - top)
        total = jnp.sum(weights, axis=1, keepdims=True)
        values = vbuf[slot, :, column:column + HEAD_DIM]
        mixed = jnp.dot(weights.astype(jnp.bfloat16), values, preferred_element_type=jnp.float32)
        for g in range(group_size):
            o_ref[:, base + g * HEAD_DIM:base + (g + 1) * HEAD_DIM] = (
                mixed[g * BLOCK:(g + 1) * BLOCK].astype(o_ref.dtype)
            )
        m_ref[0, kv] = jnp.transpose(jnp.broadcast_to(top, (top.shape[0], 128)))[0:1]
        l_ref[0, kv] = jnp.transpose(jnp.broadcast_to(total, (total.shape[0], 128)))[0:1]


def local_attention(queries, cached_keys, chosen, live, cached_values, kv_first, heads_kv):
    query_count = queries.shape[0]
    cache_width = cached_keys.shape[1]
    group_size = HEADS // KV_HEADS
    query_width = heads_kv * group_size * HEAD_DIM
    part = kv_first // heads_kv
    qblocks = query_count // BLOCK
    stat_shape = jax.ShapeDtypeStruct((qblocks, heads_kv, 1, group_size * BLOCK), jnp.float32)
    stat_spec = pl.BlockSpec((1, heads_kv, 1, group_size * BLOCK), lambda b, c, v: (b, 0, 0, 0))
    flops = 4 * query_count * heads_kv * group_size * CAP * BLOCK * HEAD_DIM
    return pl.pallas_call(
        functools.partial(attend_kernel, kv_first),
        out_shape=(jax.ShapeDtypeStruct((query_count, query_width), jnp.bfloat16), stat_shape, stat_shape),
        grid_spec=pltpu.PrefetchScalarGridSpec(
            num_scalar_prefetch=2,
            grid=(qblocks,),
            in_specs=[
                pl.BlockSpec((BLOCK, query_width), lambda b, c, v: (b, part)),
                pl.BlockSpec(memory_space=pl.ANY),
                pl.BlockSpec(memory_space=pl.ANY),
            ],
            out_specs=[pl.BlockSpec((BLOCK, query_width), lambda b, c, v: (b, 0)), stat_spec, stat_spec],
            scratch_shapes=[
                pltpu.VMEM((2, CAP * BLOCK, heads_kv * HEAD_DIM), jnp.bfloat16),
                pltpu.VMEM((2, CAP * BLOCK, heads_kv * HEAD_DIM), jnp.bfloat16),
                pltpu.SemaphoreType.DMA((2, 2, CAP)),
            ],
        ),
        compiler_params=pltpu.CompilerParams(dimension_semantics=("arbitrary",)),
        cost_estimate=pl.CostEstimate(
            flops=flops,
            transcendentals=query_count * heads_kv * group_size * CAP * BLOCK,
            bytes_accessed=2 * query_count * query_width + 4 * qblocks * CAP * BLOCK * heads_kv * HEAD_DIM,
        ),
    )(chosen, live, queries, cached_keys, cached_values)


def shards(queries, cached_keys, cached_values, pattern, out_weight):
    shard_index = lax.axis_index("ctx")
    head_index = lax.axis_index("head")
    ctx_n = lax.axis_size("ctx")
    query_count, query_width = queries.shape
    cache_rows, cache_width = cached_keys.shape
    heads_kv = cache_width // HEAD_DIM
    group_size = HEADS // KV_HEADS
    heads_here = heads_kv * group_size
    local_blocks = cache_rows // BLOCK
    qblocks = query_count // BLOCK

    local_block = pattern - shard_index * local_blocks
    in_shard = (local_block >= 0) & (local_block < local_blocks)
    slot_rank = jnp.cumsum(in_shard.astype(jnp.int32), axis=1) - 1
    slot_ids = jnp.arange(CAP, dtype=jnp.int32)
    picked = in_shard[:, :, None] & (slot_rank[:, :, None] == slot_ids[None, None, :])
    chosen = jnp.sum(jnp.where(picked, local_block[:, :, None], 0), axis=1).astype(jnp.int32)
    live = jnp.any(picked, axis=1).astype(jnp.int32)

    parts = heads_kv
    outs = [
        local_attention(queries, cached_keys, chosen, live, cached_values, part, 1)
        for part in range(parts)
    ]
    mixed_parts = [out[0] for out in outs]
    top = jnp.concatenate([out[1] for out in outs], axis=1)
    total = jnp.concatenate([out[2] for out in outs], axis=1)

    def by_row(stat):
        stat = stat.reshape(qblocks, heads_kv, group_size, BLOCK).transpose(0, 3, 1, 2)
        return stat.reshape(query_count, heads_here)

    stats = jnp.concatenate([by_row(top), by_row(total)], axis=1)
    rows_here = query_count // ctx_n
    own = lax.dynamic_slice_in_dim(stats, shard_index * rows_here, rows_here, axis=0)
    by_shift = [own]
    for shift in range(1, ctx_n):
        target = lax.rem(shard_index + shift, ctx_n)
        chunk = lax.dynamic_slice_in_dim(stats, target * rows_here, rows_here, axis=0)
        pairs = [(src, (src + shift) % ctx_n) for src in range(ctx_n)]
        by_shift.append(lax.ppermute(chunk, "ctx", perm=pairs))
    sources = lax.rem(shard_index - jnp.arange(ctx_n, dtype=jnp.int32) + ctx_n, ctx_n)
    got_stats = jnp.take(jnp.stack(by_shift), sources, axis=0)
    got_stats = got_stats.reshape(ctx_n, rows_here, 2, heads_here)
    got_top, got_total = got_stats[:, :, 0], got_stats[:, :, 1]
    row_peak = got_top.max(axis=0)
    rescale = jnp.exp(got_top - row_peak[None])
    row_norm = jnp.sum(got_total * rescale, axis=0)
    half_heads = heads_here // parts
    half_width = query_width // parts
    pieces = []
    for part, mixed in enumerate(mixed_parts):
        splits = 2 if part == parts - 1 and half_heads % 2 == 0 else 1
        piece_heads = half_heads // splits
        for split in range(splits):
            first = part * half_heads + split * piece_heads
            columns = slice(split * piece_heads * HEAD_DIM, (split + 1) * piece_heads * HEAD_DIM)
            pieces.append((mixed if splits == 1 else mixed[:, columns], first, piece_heads))
    terms = []
    for mixed, first, piece_heads in pieces:
        heads = slice(first, first + piece_heads)
        piece_width = piece_heads * HEAD_DIM
        got_mixed = lax.all_to_all(mixed, "ctx", split_axis=0, concat_axis=0, tiled=True)
        got_mixed = got_mixed.reshape(ctx_n, -1, piece_heads, HEAD_DIM).astype(jnp.float32)
        summed = jnp.sum(got_mixed * rescale[:, :, heads, None], axis=0)
        attended = (summed / row_norm[:, heads, None]).reshape(rows_here, piece_width).astype(jnp.bfloat16)
        terms.append((lax.all_gather(attended, "ctx", axis=0, tiled=True),
                      out_weight[first * HEAD_DIM:first * HEAD_DIM + piece_width]))

    def project(columns):
        total_out = None
        for rows, weight in terms:
            term = jnp.dot(rows, columns(weight), preferred_element_type=jnp.float32)
            total_out = term if total_out is None else total_out + term
        return total_out

    heads_n = lax.axis_size("head")
    share = out_weight.shape[1] // heads_n
    if heads_n == 2:
        sent = project(lambda w: lax.dynamic_slice_in_dim(w, (1 - head_index) * share, share, axis=1))
        got = lax.ppermute(sent.astype(jnp.bfloat16), "head", perm=[(0, 1), (1, 0)])
        kept = project(lambda w: lax.dynamic_slice_in_dim(w, head_index * share, share, axis=1))
        return (kept + got.astype(jnp.float32)).astype(jnp.bfloat16)
    partial_out = project(lambda w: w)
    pieces = partial_out.reshape(query_count, heads_n, share).transpose(1, 0, 2)
    got = lax.all_to_all(pieces.astype(jnp.bfloat16), "head", 0, 0, tiled=True)
    return got.astype(jnp.float32).sum(axis=0).astype(jnp.bfloat16)


def solution(mesh):
    return jax.shard_map(
        shards,
        mesh=mesh,
        in_specs=(
            P(("groups", "rep"), "head"),
            P(("groups", "ctx"), "head"),
            P(("groups", "ctx"), "head"),
            P(("groups", "rep"), None),
            P("head", "ctx"),
        ),
        out_specs=P(("groups", "rep"), ("ctx", "head")),
        check_vma=False,
    )
```

```python
import functools

import jax
import jax.numpy as jnp
from jax import lax
from jax.experimental import pallas as pl
from jax.experimental.pallas import tpu as pltpu
from jax.sharding import PartitionSpec as P

HEADS = 64
KV_HEADS = 8
HEAD_DIM = 128
BLOCK = 128
CAP = 8


def attend_kernel(kv_first, chosen_ref, live_ref, q_ref, k_hbm, v_hbm, o_ref, m_ref, l_ref, kbuf, vbuf, sem):
    b = pl.program_id(0)
    steps = pl.num_programs(0)
    heads_kv = m_ref.shape[1]
    group_size = q_ref.shape[1] // (heads_kv * HEAD_DIM)

    cols = pl.ds(kv_first * HEAD_DIM, heads_kv * HEAD_DIM)

    def block_copies(step, slot):
        copies = []
        for j in range(CAP):
            rows = pl.ds(pl.multiple_of(chosen_ref[step, j] * BLOCK, BLOCK), BLOCK)
            dst = pl.ds(j * BLOCK, BLOCK)
            copies.append(pltpu.make_async_copy(k_hbm.at[rows, cols], kbuf.at[slot, dst], sem.at[slot, 0, j]))
            copies.append(pltpu.make_async_copy(v_hbm.at[rows, cols], vbuf.at[slot, dst], sem.at[slot, 1, j]))
        return copies

    slot = b % 2

    @pl.when(b == 0)
    def _():
        for c in block_copies(b, slot):
            c.start()

    @pl.when(b + 1 < steps)
    def _():
        for c in block_copies(b + 1, 1 - slot):
            c.start()

    for c in block_copies(b, slot):
        c.wait()

    key_slot = lax.broadcasted_iota(jnp.int32, (1, CAP * BLOCK), 1) // BLOCK
    live_keys = key_slot < 0
    for j in range(CAP):
        live_keys = live_keys | ((key_slot == j) & (live_ref[b, j] > 0))
    for kv in range(heads_kv):
        base = kv * group_size * HEAD_DIM
        stacked = jnp.concatenate(
            [q_ref[:, base + g * HEAD_DIM:base + (g + 1) * HEAD_DIM] for g in range(group_size)], axis=0
        )
        column = kv * HEAD_DIM
        keys = kbuf[slot, :, column:column + HEAD_DIM]
        scores = lax.dot_general(
            stacked, keys, (((1,), (1,)), ((), ())), preferred_element_type=jnp.float32
        ) * (HEAD_DIM ** (-0.5))
        scores = jnp.where(live_keys, scores, jnp.float32(-1e30))
        top = jnp.max(scores, axis=1, keepdims=True)
        weights = jnp.exp(scores - top)
        total = jnp.sum(weights, axis=1, keepdims=True)
        values = vbuf[slot, :, column:column + HEAD_DIM]
        mixed = jnp.dot(weights.astype(jnp.bfloat16), values, preferred_element_type=jnp.float32)
        for g in range(group_size):
            o_ref[:, base + g * HEAD_DIM:base + (g + 1) * HEAD_DIM] = (
                mixed[g * BLOCK:(g + 1) * BLOCK].astype(o_ref.dtype)
            )
        m_ref[0, kv] = jnp.transpose(jnp.broadcast_to(top, (top.shape[0], 128)))[0:1]
        l_ref[0, kv] = jnp.transpose(jnp.broadcast_to(total, (total.shape[0], 128)))[0:1]


def local_attention(queries, cached_keys, chosen, live, cached_values, kv_first, heads_kv):
    query_count = queries.shape[0]
    cache_width = cached_keys.shape[1]
    group_size = HEADS // KV_HEADS
    query_width = heads_kv * group_size * HEAD_DIM
    part = kv_first // heads_kv
    qblocks = query_count // BLOCK
    stat_shape = jax.ShapeDtypeStruct((qblocks, heads_kv, 1, group_size * BLOCK), jnp.float32)
    stat_spec = pl.BlockSpec((1, heads_kv, 1, group_size * BLOCK), lambda b, c, v: (b, 0, 0, 0))
    flops = 4 * query_count * heads_kv * group_size * CAP * BLOCK * HEAD_DIM
    return pl.pallas_call(
        functools.partial(attend_kernel, kv_first),
        out_shape=(jax.ShapeDtypeStruct((query_count, query_width), jnp.bfloat16), stat_shape, stat_shape),
        grid_spec=pltpu.PrefetchScalarGridSpec(
            num_scalar_prefetch=2,
            grid=(qblocks,),
            in_specs=[
                pl.BlockSpec((BLOCK, query_width), lambda b, c, v: (b, part)),
                pl.BlockSpec(memory_space=pl.ANY),
                pl.BlockSpec(memory_space=pl.ANY),
            ],
            out_specs=[pl.BlockSpec((BLOCK, query_width), lambda b, c, v: (b, 0)), stat_spec, stat_spec],
            scratch_shapes=[
                pltpu.VMEM((2, CAP * BLOCK, heads_kv * HEAD_DIM), jnp.bfloat16),
                pltpu.VMEM((2, CAP * BLOCK, heads_kv * HEAD_DIM), jnp.bfloat16),
                pltpu.SemaphoreType.DMA((2, 2, CAP)),
            ],
        ),
        compiler_params=pltpu.CompilerParams(dimension_semantics=("arbitrary",)),
        cost_estimate=pl.CostEstimate(
            flops=flops,
            transcendentals=query_count * heads_kv * group_size * CAP * BLOCK,
            bytes_accessed=2 * query_count * query_width + 4 * qblocks * CAP * BLOCK * heads_kv * HEAD_DIM,
        ),
    )(chosen, live, queries, cached_keys, cached_values)


def shards(queries, cached_keys, cached_values, pattern, out_weight):
    shard_index = lax.axis_index("ctx")
    head_index = lax.axis_index("head")
    ctx_n = lax.axis_size("ctx")
    query_count, query_width = queries.shape
    cache_rows, cache_width = cached_keys.shape
    heads_kv = cache_width // HEAD_DIM
    group_size = HEADS // KV_HEADS
    heads_here = heads_kv * group_size
    local_blocks = cache_rows // BLOCK
    qblocks = query_count // BLOCK

    local_block = pattern - shard_index * local_blocks
    in_shard = (local_block >= 0) & (local_block < local_blocks)
    slot_rank = jnp.cumsum(in_shard.astype(jnp.int32), axis=1) - 1
    slot_ids = jnp.arange(CAP, dtype=jnp.int32)
    picked = in_shard[:, :, None] & (slot_rank[:, :, None] == slot_ids[None, None, :])
    chosen = jnp.sum(jnp.where(picked, local_block[:, :, None], 0), axis=1).astype(jnp.int32)
    live = jnp.any(picked, axis=1).astype(jnp.int32)

    parts = heads_kv
    outs = [
        local_attention(queries, cached_keys, chosen, live, cached_values, part, 1)
        for part in range(parts)
    ]
    mixed_parts = [out[0] for out in outs]
    top = jnp.concatenate([out[1] for out in outs], axis=1)
    total = jnp.concatenate([out[2] for out in outs], axis=1)

    def by_row(stat):
        stat = stat.reshape(qblocks, heads_kv, group_size, BLOCK).transpose(0, 3, 1, 2)
        return stat.reshape(query_count, heads_here)

    stats = jnp.concatenate([by_row(top), by_row(total)], axis=1)
    rows_here = query_count // ctx_n
    own = lax.dynamic_slice_in_dim(stats, shard_index * rows_here, rows_here, axis=0)
    by_shift = [own]
    for shift in range(1, ctx_n):
        target = lax.rem(shard_index + shift, ctx_n)
        chunk = lax.dynamic_slice_in_dim(stats, target * rows_here, rows_here, axis=0)
        pairs = [(src, (src + shift) % ctx_n) for src in range(ctx_n)]
        by_shift.append(lax.ppermute(chunk, "ctx", perm=pairs))
    sources = lax.rem(shard_index - jnp.arange(ctx_n, dtype=jnp.int32) + ctx_n, ctx_n)
    got_stats = jnp.take(jnp.stack(by_shift), sources, axis=0)
    got_stats = got_stats.reshape(ctx_n, rows_here, 2, heads_here)
    got_top, got_total = got_stats[:, :, 0], got_stats[:, :, 1]
    row_peak = got_top.max(axis=0)
    rescale = jnp.exp(got_top - row_peak[None])
    row_norm = jnp.sum(got_total * rescale, axis=0)
    half_heads = heads_here // parts
    half_width = query_width // parts
    pieces = []
    for part, mixed in enumerate(mixed_parts):
        tail = half_heads // 4 if part == parts - 1 and half_heads % 4 == 0 else 0
        sizes = [half_heads - tail, tail] if tail else [half_heads]
        offset = 0
        for piece_heads in sizes:
            first = part * half_heads + offset
            columns = slice(offset * HEAD_DIM, (offset + piece_heads) * HEAD_DIM)
            pieces.append((mixed if len(sizes) == 1 else mixed[:, columns], first, piece_heads))
            offset += piece_heads
    terms = []
    for mixed, first, piece_heads in pieces:
        heads = slice(first, first + piece_heads)
        piece_width = piece_heads * HEAD_DIM
        got_mixed = lax.all_to_all(mixed, "ctx", split_axis=0, concat_axis=0, tiled=True)
        got_mixed = got_mixed.reshape(ctx_n, -1, piece_heads, HEAD_DIM).astype(jnp.float32)
        summed = jnp.sum(got_mixed * rescale[:, :, heads, None], axis=0)
        attended = (summed / row_norm[:, heads, None]).reshape(rows_here, piece_width).astype(jnp.bfloat16)
        terms.append((lax.all_gather(attended, "ctx", axis=0, tiled=True),
                      out_weight[first * HEAD_DIM:first * HEAD_DIM + piece_width]))

    def project(columns):
        total_out = None
        for rows, weight in terms:
            term = jnp.dot(rows, columns(weight), preferred_element_type=jnp.float32)
            total_out = term if total_out is None else total_out + term
        return total_out

    heads_n = lax.axis_size("head")
    share = out_weight.shape[1] // heads_n
    if heads_n == 2:
        sent = project(lambda w: lax.dynamic_slice_in_dim(w, (1 - head_index) * share, share, axis=1))
        got = lax.ppermute(sent.astype(jnp.bfloat16), "head", perm=[(0, 1), (1, 0)])
        kept = project(lambda w: lax.dynamic_slice_in_dim(w, head_index * share, share, axis=1))
        return (kept + got.astype(jnp.float32)).astype(jnp.bfloat16)
    partial_out = project(lambda w: w)
    pieces = partial_out.reshape(query_count, heads_n, share).transpose(1, 0, 2)
    got = lax.all_to_all(pieces.astype(jnp.bfloat16), "head", 0, 0, tiled=True)
    return got.astype(jnp.float32).sum(axis=0).astype(jnp.bfloat16)


def solution(mesh):
    return jax.shard_map(
        shards,
        mesh=mesh,
        in_specs=(
            P(("groups", "rep"), "head"),
            P(("groups", "ctx"), "head"),
            P(("groups", "ctx"), "head"),
            P(("groups", "rep"), None),
            P("head", "ctx"),
        ),
        out_specs=P(("groups", "rep"), ("ctx", "head")),
        check_vma=False,
    )
```

```python
import functools

import jax
import jax.numpy as jnp
from jax import lax
from jax.experimental import pallas as pl
from jax.experimental.pallas import tpu as pltpu
from jax.sharding import PartitionSpec as P

HEADS = 64
KV_HEADS = 8
HEAD_DIM = 128
BLOCK = 128
CAP = 8


def attend_kernel(kv_first, chosen_ref, live_ref, q_ref, k_hbm, v_hbm, o_ref, m_ref, l_ref, kbuf, vbuf, sem):
    b = pl.program_id(0)
    steps = pl.num_programs(0)
    heads_kv = m_ref.shape[1]
    group_size = q_ref.shape[1] // (heads_kv * HEAD_DIM)

    cols = pl.ds(kv_first * HEAD_DIM, heads_kv * HEAD_DIM)

    def block_copies(step, slot):
        copies = []
        for j in range(CAP):
            rows = pl.ds(pl.multiple_of(chosen_ref[step, j] * BLOCK, BLOCK), BLOCK)
            dst = pl.ds(j * BLOCK, BLOCK)
            copies.append(pltpu.make_async_copy(k_hbm.at[rows, cols], kbuf.at[slot, dst], sem.at[slot, 0, j]))
            copies.append(pltpu.make_async_copy(v_hbm.at[rows, cols], vbuf.at[slot, dst], sem.at[slot, 1, j]))
        return copies

    slot = b % 2

    @pl.when(b == 0)
    def _():
        for c in block_copies(b, slot):
            c.start()

    @pl.when(b + 1 < steps)
    def _():
        for c in block_copies(b + 1, 1 - slot):
            c.start()

    for c in block_copies(b, slot):
        c.wait()

    key_slot = lax.broadcasted_iota(jnp.int32, (1, CAP * BLOCK), 1) // BLOCK
    live_keys = key_slot < 0
    for j in range(CAP):
        live_keys = live_keys | ((key_slot == j) & (live_ref[b, j] > 0))
    for kv in range(heads_kv):
        base = kv * group_size * HEAD_DIM
        stacked = jnp.concatenate(
            [q_ref[:, base + g * HEAD_DIM:base + (g + 1) * HEAD_DIM] for g in range(group_size)], axis=0
        )
        column = kv * HEAD_DIM
        keys = kbuf[slot, :, column:column + HEAD_DIM]
        scores = lax.dot_general(
            stacked, keys, (((1,), (1,)), ((), ())), preferred_element_type=jnp.float32
        ) * (HEAD_DIM ** (-0.5))
        scores = jnp.where(live_keys, scores, jnp.float32(-1e30))
        top = jnp.max(scores, axis=1, keepdims=True)
        weights = jnp.exp(scores - top)
        total = jnp.sum(weights, axis=1, keepdims=True)
        values = vbuf[slot, :, column:column + HEAD_DIM]
        mixed = jnp.dot(weights.astype(jnp.bfloat16), values, preferred_element_type=jnp.float32)
        for g in range(group_size):
            o_ref[:, base + g * HEAD_DIM:base + (g + 1) * HEAD_DIM] = (
                mixed[g * BLOCK:(g + 1) * BLOCK].astype(o_ref.dtype)
            )
        m_ref[0, kv] = jnp.transpose(jnp.broadcast_to(top, (top.shape[0], 128)))[0:1]
        l_ref[0, kv] = jnp.transpose(jnp.broadcast_to(total, (total.shape[0], 128)))[0:1]


def local_attention(queries, cached_keys, chosen, live, cached_values, kv_first, heads_kv):
    query_count = queries.shape[0]
    cache_width = cached_keys.shape[1]
    group_size = HEADS // KV_HEADS
    query_width = heads_kv * group_size * HEAD_DIM
    part = kv_first // heads_kv
    qblocks = query_count // BLOCK
    stat_shape = jax.ShapeDtypeStruct((qblocks, heads_kv, 1, group_size * BLOCK), jnp.float32)
    stat_spec = pl.BlockSpec((1, heads_kv, 1, group_size * BLOCK), lambda b, c, v: (b, 0, 0, 0))
    flops = 4 * query_count * heads_kv * group_size * CAP * BLOCK * HEAD_DIM
    return pl.pallas_call(
        functools.partial(attend_kernel, kv_first),
        out_shape=(jax.ShapeDtypeStruct((query_count, query_width), jnp.bfloat16), stat_shape, stat_shape),
        grid_spec=pltpu.PrefetchScalarGridSpec(
            num_scalar_prefetch=2,
            grid=(qblocks,),
            in_specs=[
                pl.BlockSpec((BLOCK, query_width), lambda b, c, v: (b, part)),
                pl.BlockSpec(memory_space=pl.ANY),
                pl.BlockSpec(memory_space=pl.ANY),
            ],
            out_specs=[pl.BlockSpec((BLOCK, query_width), lambda b, c, v: (b, 0)), stat_spec, stat_spec],
            scratch_shapes=[
                pltpu.VMEM((2, CAP * BLOCK, heads_kv * HEAD_DIM), jnp.bfloat16),
                pltpu.VMEM((2, CAP * BLOCK, heads_kv * HEAD_DIM), jnp.bfloat16),
                pltpu.SemaphoreType.DMA((2, 2, CAP)),
            ],
        ),
        compiler_params=pltpu.CompilerParams(dimension_semantics=("arbitrary",)),
        cost_estimate=pl.CostEstimate(
            flops=flops,
            transcendentals=query_count * heads_kv * group_size * CAP * BLOCK,
            bytes_accessed=2 * query_count * query_width + 4 * qblocks * CAP * BLOCK * heads_kv * HEAD_DIM,
        ),
    )(chosen, live, queries, cached_keys, cached_values)


def shards(queries, cached_keys, cached_values, pattern, out_weight):
    shard_index = lax.axis_index("ctx")
    head_index = lax.axis_index("head")
    ctx_n = lax.axis_size("ctx")
    query_count, query_width = queries.shape
    cache_rows, cache_width = cached_keys.shape
    heads_kv = cache_width // HEAD_DIM
    group_size = HEADS // KV_HEADS
    heads_here = heads_kv * group_size
    local_blocks = cache_rows // BLOCK
    qblocks = query_count // BLOCK

    local_block = pattern - shard_index * local_blocks
    in_shard = (local_block >= 0) & (local_block < local_blocks)
    slot_rank = jnp.cumsum(in_shard.astype(jnp.int32), axis=1) - 1
    slot_ids = jnp.arange(CAP, dtype=jnp.int32)
    picked = in_shard[:, :, None] & (slot_rank[:, :, None] == slot_ids[None, None, :])
    chosen = jnp.sum(jnp.where(picked, local_block[:, :, None], 0), axis=1).astype(jnp.int32)
    live = jnp.any(picked, axis=1).astype(jnp.int32)

    per_call = 2 if heads_kv % 2 == 0 else 1
    parts = heads_kv // per_call
    outs = [
        local_attention(queries, cached_keys, chosen, live, cached_values, part * per_call, per_call)
        for part in range(parts)
    ]
    mixed_parts = [out[0] for out in outs]
    top = jnp.concatenate([out[1] for out in outs], axis=1)
    total = jnp.concatenate([out[2] for out in outs], axis=1)

    def by_row(stat):
        stat = stat.reshape(qblocks, heads_kv, group_size, BLOCK).transpose(0, 3, 1, 2)
        return stat.reshape(query_count, heads_here)

    stats = jnp.concatenate([by_row(top), by_row(total)], axis=1)
    rows_here = query_count // ctx_n
    own = lax.dynamic_slice_in_dim(stats, shard_index * rows_here, rows_here, axis=0)
    by_shift = [own]
    for shift in range(1, ctx_n):
        target = lax.rem(shard_index + shift, ctx_n)
        chunk = lax.dynamic_slice_in_dim(stats, target * rows_here, rows_here, axis=0)
        pairs = [(src, (src + shift) % ctx_n) for src in range(ctx_n)]
        by_shift.append(lax.ppermute(chunk, "ctx", perm=pairs))
    sources = lax.rem(shard_index - jnp.arange(ctx_n, dtype=jnp.int32) + ctx_n, ctx_n)
    got_stats = jnp.take(jnp.stack(by_shift), sources, axis=0)
    got_stats = got_stats.reshape(ctx_n, rows_here, 2, heads_here)
    got_top, got_total = got_stats[:, :, 0], got_stats[:, :, 1]
    row_peak = got_top.max(axis=0)
    rescale = jnp.exp(got_top - row_peak[None])
    row_norm = jnp.sum(got_total * rescale, axis=0)
    half_heads = heads_here // parts
    half_width = query_width // parts
    pieces = []
    for part, mixed in enumerate(mixed_parts):
        splits = 2 if part == parts - 1 and half_heads % 2 == 0 else 1
        piece_heads = half_heads // splits
        for split in range(splits):
            first = part * half_heads + split * piece_heads
            columns = slice(split * piece_heads * HEAD_DIM, (split + 1) * piece_heads * HEAD_DIM)
            pieces.append((mixed if splits == 1 else mixed[:, columns], first, piece_heads))
    terms = []
    for mixed, first, piece_heads in pieces:
        heads = slice(first, first + piece_heads)
        piece_width = piece_heads * HEAD_DIM
        got_mixed = lax.all_to_all(mixed, "ctx", split_axis=0, concat_axis=0, tiled=True)
        got_mixed = got_mixed.reshape(ctx_n, -1, piece_heads, HEAD_DIM).astype(jnp.float32)
        summed = jnp.sum(got_mixed * rescale[:, :, heads, None], axis=0)
        attended = (summed / row_norm[:, heads, None]).reshape(rows_here, piece_width).astype(jnp.bfloat16)
        terms.append((lax.all_gather(attended, "ctx", axis=0, tiled=True),
                      out_weight[first * HEAD_DIM:first * HEAD_DIM + piece_width]))

    def project(columns):
        total_out = None
        for rows, weight in terms:
            term = jnp.dot(rows, columns(weight), preferred_element_type=jnp.float32)
            total_out = term if total_out is None else total_out + term
        return total_out

    heads_n = lax.axis_size("head")
    share = out_weight.shape[1] // heads_n
    if heads_n == 2:
        sent = project(lambda w: lax.dynamic_slice_in_dim(w, (1 - head_index) * share, share, axis=1))
        got = lax.ppermute(sent.astype(jnp.bfloat16), "head", perm=[(0, 1), (1, 0)])
        kept = project(lambda w: lax.dynamic_slice_in_dim(w, head_index * share, share, axis=1))
        return (kept + got.astype(jnp.float32)).astype(jnp.bfloat16)
    partial_out = project(lambda w: w)
    pieces = partial_out.reshape(query_count, heads_n, share).transpose(1, 0, 2)
    got = lax.all_to_all(pieces.astype(jnp.bfloat16), "head", 0, 0, tiled=True)
    return got.astype(jnp.float32).sum(axis=0).astype(jnp.bfloat16)


def solution(mesh):
    return jax.shard_map(
        shards,
        mesh=mesh,
        in_specs=(
            P(("groups", "rep"), "head"),
            P(("groups", "ctx"), "head"),
            P(("groups", "ctx"), "head"),
            P(("groups", "rep"), None),
            P("head", "ctx"),
        ),
        out_specs=P(("groups", "rep"), ("ctx", "head")),
        check_vma=False,
    )
```

```python
import functools

import jax
import jax.numpy as jnp
from jax import lax
from jax.experimental import pallas as pl
from jax.experimental.pallas import tpu as pltpu
from jax.sharding import PartitionSpec as P

HEADS = 64
KV_HEADS = 8
HEAD_DIM = 128
BLOCK = 128
CAP = 8


def attend_kernel(kv_first, chosen_ref, live_ref, q_ref, k_hbm, v_hbm, o_ref, m_ref, l_ref, kbuf, vbuf, sem):
    b = pl.program_id(0)
    steps = pl.num_programs(0)
    heads_kv = m_ref.shape[1]
    group_size = q_ref.shape[1] // (heads_kv * HEAD_DIM)

    cols = pl.ds(kv_first * HEAD_DIM, heads_kv * HEAD_DIM)

    def block_copies(step, slot):
        copies = []
        for j in range(CAP):
            rows = pl.ds(pl.multiple_of(chosen_ref[step, j] * BLOCK, BLOCK), BLOCK)
            dst = pl.ds(j * BLOCK, BLOCK)
            copies.append(pltpu.make_async_copy(k_hbm.at[rows, cols], kbuf.at[slot, dst], sem.at[slot, 0, j]))
            copies.append(pltpu.make_async_copy(v_hbm.at[rows, cols], vbuf.at[slot, dst], sem.at[slot, 1, j]))
        return copies

    slot = b % 2

    @pl.when(b == 0)
    def _():
        for c in block_copies(b, slot):
            c.start()

    @pl.when(b + 1 < steps)
    def _():
        for c in block_copies(b + 1, 1 - slot):
            c.start()

    for c in block_copies(b, slot):
        c.wait()

    key_slot = lax.broadcasted_iota(jnp.int32, (1, CAP * BLOCK), 1) // BLOCK
    live_keys = key_slot < 0
    for j in range(CAP):
        live_keys = live_keys | ((key_slot == j) & (live_ref[b, j] > 0))
    for kv in range(heads_kv):
        base = kv * group_size * HEAD_DIM
        stacked = jnp.concatenate(
            [q_ref[:, base + g * HEAD_DIM:base + (g + 1) * HEAD_DIM] for g in range(group_size)], axis=0
        )
        column = kv * HEAD_DIM
        keys = kbuf[slot, :, column:column + HEAD_DIM]
        scores = lax.dot_general(
            stacked, keys, (((1,), (1,)), ((), ())), preferred_element_type=jnp.float32
        ) * (HEAD_DIM ** (-0.5))
        scores = jnp.where(live_keys, scores, jnp.float32(-1e30))
        top = jnp.max(scores, axis=1, keepdims=True)
        weights = jnp.exp(scores - top)
        total = jnp.sum(weights, axis=1, keepdims=True)
        values = vbuf[slot, :, column:column + HEAD_DIM]
        mixed = jnp.dot(weights.astype(jnp.bfloat16), values, preferred_element_type=jnp.float32)
        for g in range(group_size):
            o_ref[:, base + g * HEAD_DIM:base + (g + 1) * HEAD_DIM] = (
                mixed[g * BLOCK:(g + 1) * BLOCK].astype(o_ref.dtype)
            )
        m_ref[0, kv] = jnp.transpose(jnp.broadcast_to(top, (top.shape[0], 128)))[0:1]
        l_ref[0, kv] = jnp.transpose(jnp.broadcast_to(total, (total.shape[0], 128)))[0:1]


def local_attention(queries, cached_keys, chosen, live, cached_values, kv_first, heads_kv):
    query_count = queries.shape[0]
    cache_width = cached_keys.shape[1]
    group_size = HEADS // KV_HEADS
    query_width = heads_kv * group_size * HEAD_DIM
    part = kv_first // heads_kv
    qblocks = query_count // BLOCK
    stat_shape = jax.ShapeDtypeStruct((qblocks, heads_kv, 1, group_size * BLOCK), jnp.float32)
    stat_spec = pl.BlockSpec((1, heads_kv, 1, group_size * BLOCK), lambda b, c, v: (b, 0, 0, 0))
    flops = 4 * query_count * heads_kv * group_size * CAP * BLOCK * HEAD_DIM
    return pl.pallas_call(
        functools.partial(attend_kernel, kv_first),
        out_shape=(jax.ShapeDtypeStruct((query_count, query_width), jnp.bfloat16), stat_shape, stat_shape),
        grid_spec=pltpu.PrefetchScalarGridSpec(
            num_scalar_prefetch=2,
            grid=(qblocks,),
            in_specs=[
                pl.BlockSpec((BLOCK, query_width), lambda b, c, v: (b, part)),
                pl.BlockSpec(memory_space=pl.ANY),
                pl.BlockSpec(memory_space=pl.ANY),
            ],
            out_specs=[pl.BlockSpec((BLOCK, query_width), lambda b, c, v: (b, 0)), stat_spec, stat_spec],
            scratch_shapes=[
                pltpu.VMEM((2, CAP * BLOCK, heads_kv * HEAD_DIM), jnp.bfloat16),
                pltpu.VMEM((2, CAP * BLOCK, heads_kv * HEAD_DIM), jnp.bfloat16),
                pltpu.SemaphoreType.DMA((2, 2, CAP)),
            ],
        ),
        compiler_params=pltpu.CompilerParams(dimension_semantics=("arbitrary",)),
        cost_estimate=pl.CostEstimate(
            flops=flops,
            transcendentals=query_count * heads_kv * group_size * CAP * BLOCK,
            bytes_accessed=2 * query_count * query_width + 4 * qblocks * CAP * BLOCK * heads_kv * HEAD_DIM,
        ),
    )(chosen, live, queries, cached_keys, cached_values)


def shards(queries, cached_keys, cached_values, pattern, out_weight):
    shard_index = lax.axis_index("ctx")
    head_index = lax.axis_index("head")
    ctx_n = lax.axis_size("ctx")
    query_count, query_width = queries.shape
    cache_rows, cache_width = cached_keys.shape
    heads_kv = cache_width // HEAD_DIM
    group_size = HEADS // KV_HEADS
    heads_here = heads_kv * group_size
    local_blocks = cache_rows // BLOCK
    qblocks = query_count // BLOCK

    local_block = pattern - shard_index * local_blocks
    in_shard = (local_block >= 0) & (local_block < local_blocks)
    slot_rank = jnp.cumsum(in_shard.astype(jnp.int32), axis=1) - 1
    slot_ids = jnp.arange(CAP, dtype=jnp.int32)
    picked = in_shard[:, :, None] & (slot_rank[:, :, None] == slot_ids[None, None, :])
    chosen = jnp.sum(jnp.where(picked, local_block[:, :, None], 0), axis=1).astype(jnp.int32)
    live = jnp.any(picked, axis=1).astype(jnp.int32)

    per_call = 2 if heads_kv % 2 == 0 else 1
    parts = heads_kv // per_call
    outs = [
        local_attention(queries, cached_keys, chosen, live, cached_values, part * per_call, per_call)
        for part in range(parts)
    ]
    mixed_parts = [out[0] for out in outs]
    top = jnp.concatenate([out[1] for out in outs], axis=1)
    total = jnp.concatenate([out[2] for out in outs], axis=1)

    def by_row(stat):
        stat = stat.reshape(qblocks, heads_kv, group_size, BLOCK).transpose(0, 3, 1, 2)
        return stat.reshape(query_count, heads_here)

    stats = jnp.concatenate([by_row(top), by_row(total)], axis=1)
    rows_here = query_count // ctx_n
    own = lax.dynamic_slice_in_dim(stats, shard_index * rows_here, rows_here, axis=0)
    by_shift = [own]
    for shift in range(1, ctx_n):
        target = lax.rem(shard_index + shift, ctx_n)
        chunk = lax.dynamic_slice_in_dim(stats, target * rows_here, rows_here, axis=0)
        pairs = [(src, (src + shift) % ctx_n) for src in range(ctx_n)]
        by_shift.append(lax.ppermute(chunk, "ctx", perm=pairs))
    sources = lax.rem(shard_index - jnp.arange(ctx_n, dtype=jnp.int32) + ctx_n, ctx_n)
    got_stats = jnp.take(jnp.stack(by_shift), sources, axis=0)
    got_stats = got_stats.reshape(ctx_n, rows_here, 2, heads_here)
    got_top, got_total = got_stats[:, :, 0], got_stats[:, :, 1]
    row_peak = got_top.max(axis=0)
    rescale = jnp.exp(got_top - row_peak[None])
    row_norm = jnp.sum(got_total * rescale, axis=0)
    half_heads = heads_here // parts
    half_width = query_width // parts
    pieces = []
    for part, mixed in enumerate(mixed_parts):
        splits = 4 if part == parts - 1 and half_heads % 4 == 0 else 1
        piece_heads = half_heads // splits
        for split in range(splits):
            first = part * half_heads + split * piece_heads
            columns = slice(split * piece_heads * HEAD_DIM, (split + 1) * piece_heads * HEAD_DIM)
            pieces.append((mixed if splits == 1 else mixed[:, columns], first, piece_heads))
    terms = []
    for mixed, first, piece_heads in pieces:
        heads = slice(first, first + piece_heads)
        piece_width = piece_heads * HEAD_DIM
        got_mixed = lax.all_to_all(mixed, "ctx", split_axis=0, concat_axis=0, tiled=True)
        got_mixed = got_mixed.reshape(ctx_n, -1, piece_heads, HEAD_DIM).astype(jnp.float32)
        summed = jnp.sum(got_mixed * rescale[:, :, heads, None], axis=0)
        attended = (summed / row_norm[:, heads, None]).reshape(rows_here, piece_width).astype(jnp.bfloat16)
        terms.append((lax.all_gather(attended, "ctx", axis=0, tiled=True),
                      out_weight[first * HEAD_DIM:first * HEAD_DIM + piece_width]))

    def project(columns):
        total_out = None
        for rows, weight in terms:
            term = jnp.dot(rows, columns(weight), preferred_element_type=jnp.float32)
            total_out = term if total_out is None else total_out + term
        return total_out

    heads_n = lax.axis_size("head")
    share = out_weight.shape[1] // heads_n
    if heads_n == 2:
        sent = project(lambda w: lax.dynamic_slice_in_dim(w, (1 - head_index) * share, share, axis=1))
        got = lax.ppermute(sent.astype(jnp.bfloat16), "head", perm=[(0, 1), (1, 0)])
        kept = project(lambda w: lax.dynamic_slice_in_dim(w, head_index * share, share, axis=1))
        return (kept + got.astype(jnp.float32)).astype(jnp.bfloat16)
    partial_out = project(lambda w: w)
    pieces = partial_out.reshape(query_count, heads_n, share).transpose(1, 0, 2)
    got = lax.all_to_all(pieces.astype(jnp.bfloat16), "head", 0, 0, tiled=True)
    return got.astype(jnp.float32).sum(axis=0).astype(jnp.bfloat16)


def solution(mesh):
    return jax.shard_map(
        shards,
        mesh=mesh,
        in_specs=(
            P(("groups", "rep"), "head"),
            P(("groups", "ctx"), "head"),
            P(("groups", "ctx"), "head"),
            P(("groups", "rep"), None),
            P("head", "ctx"),
        ),
        out_specs=P(("groups", "rep"), ("ctx", "head")),
        check_vma=False,
    )
```

```python
import functools

import jax
import jax.numpy as jnp
from jax import lax
from jax.experimental import pallas as pl
from jax.experimental.pallas import tpu as pltpu
from jax.sharding import PartitionSpec as P

HEADS = 64
KV_HEADS = 8
HEAD_DIM = 128
BLOCK = 128
CAP = 8


def attend_kernel(kv_first, chosen_ref, live_ref, q_ref, k_hbm, v_hbm, o_ref, m_ref, l_ref, kbuf, vbuf, sem):
    b = pl.program_id(0)
    steps = pl.num_programs(0)
    heads_kv = m_ref.shape[1]
    group_size = q_ref.shape[1] // (heads_kv * HEAD_DIM)

    cols = pl.ds(kv_first * HEAD_DIM, heads_kv * HEAD_DIM)

    def block_copies(step, slot):
        copies = []
        for j in range(CAP):
            rows = pl.ds(pl.multiple_of(chosen_ref[step, j] * BLOCK, BLOCK), BLOCK)
            dst = pl.ds(j * BLOCK, BLOCK)
            copies.append(pltpu.make_async_copy(k_hbm.at[rows, cols], kbuf.at[slot, dst], sem.at[slot, 0, j]))
            copies.append(pltpu.make_async_copy(v_hbm.at[rows, cols], vbuf.at[slot, dst], sem.at[slot, 1, j]))
        return copies

    slot = b % 2

    @pl.when(b == 0)
    def _():
        for c in block_copies(b, slot):
            c.start()

    @pl.when(b + 1 < steps)
    def _():
        for c in block_copies(b + 1, 1 - slot):
            c.start()

    for c in block_copies(b, slot):
        c.wait()

    key_slot = lax.broadcasted_iota(jnp.int32, (1, CAP * BLOCK), 1) // BLOCK
    live_keys = key_slot < 0
    for j in range(CAP):
        live_keys = live_keys | ((key_slot == j) & (live_ref[b, j] > 0))
    for kv in range(heads_kv):
        base = kv * group_size * HEAD_DIM
        stacked = jnp.concatenate(
            [q_ref[:, base + g * HEAD_DIM:base + (g + 1) * HEAD_DIM] for g in range(group_size)], axis=0
        )
        column = kv * HEAD_DIM
        keys = kbuf[slot, :, column:column + HEAD_DIM]
        scores = lax.dot_general(
            stacked, keys, (((1,), (1,)), ((), ())), preferred_element_type=jnp.float32
        ) * (HEAD_DIM ** (-0.5))
        scores = jnp.where(live_keys, scores, jnp.float32(-1e30))
        top = jnp.max(scores, axis=1, keepdims=True)
        weights = jnp.exp(scores - top)
        total = jnp.sum(weights, axis=1, keepdims=True)
        values = vbuf[slot, :, column:column + HEAD_DIM]
        mixed = jnp.dot(weights.astype(jnp.bfloat16), values, preferred_element_type=jnp.float32)
        for g in range(group_size):
            o_ref[:, base + g * HEAD_DIM:base + (g + 1) * HEAD_DIM] = (
                mixed[g * BLOCK:(g + 1) * BLOCK].astype(o_ref.dtype)
            )
        m_ref[0, kv] = jnp.transpose(jnp.broadcast_to(top, (top.shape[0], 128)))[0:1]
        l_ref[0, kv] = jnp.transpose(jnp.broadcast_to(total, (total.shape[0], 128)))[0:1]


def local_attention(queries, cached_keys, chosen, live, cached_values, kv_first, heads_kv):
    query_count = queries.shape[0]
    cache_width = cached_keys.shape[1]
    group_size = HEADS // KV_HEADS
    query_width = heads_kv * group_size * HEAD_DIM
    part = kv_first // heads_kv
    qblocks = query_count // BLOCK
    stat_shape = jax.ShapeDtypeStruct((qblocks, heads_kv, 1, group_size * BLOCK), jnp.float32)
    stat_spec = pl.BlockSpec((1, heads_kv, 1, group_size * BLOCK), lambda b, c, v: (b, 0, 0, 0))
    flops = 4 * query_count * heads_kv * group_size * CAP * BLOCK * HEAD_DIM
    return pl.pallas_call(
        functools.partial(attend_kernel, kv_first),
        out_shape=(jax.ShapeDtypeStruct((query_count, query_width), jnp.bfloat16), stat_shape, stat_shape),
        grid_spec=pltpu.PrefetchScalarGridSpec(
            num_scalar_prefetch=2,
            grid=(qblocks,),
            in_specs=[
                pl.BlockSpec((BLOCK, query_width), lambda b, c, v: (b, part)),
                pl.BlockSpec(memory_space=pl.ANY),
                pl.BlockSpec(memory_space=pl.ANY),
            ],
            out_specs=[pl.BlockSpec((BLOCK, query_width), lambda b, c, v: (b, 0)), stat_spec, stat_spec],
            scratch_shapes=[
                pltpu.VMEM((2, CAP * BLOCK, heads_kv * HEAD_DIM), jnp.bfloat16),
                pltpu.VMEM((2, CAP * BLOCK, heads_kv * HEAD_DIM), jnp.bfloat16),
                pltpu.SemaphoreType.DMA((2, 2, CAP)),
            ],
        ),
        compiler_params=pltpu.CompilerParams(dimension_semantics=("arbitrary",)),
        cost_estimate=pl.CostEstimate(
            flops=flops,
            transcendentals=query_count * heads_kv * group_size * CAP * BLOCK,
            bytes_accessed=2 * query_count * query_width + 4 * qblocks * CAP * BLOCK * heads_kv * HEAD_DIM,
        ),
    )(chosen, live, queries, cached_keys, cached_values)


def shards(queries, cached_keys, cached_values, pattern, out_weight):
    shard_index = lax.axis_index("ctx")
    head_index = lax.axis_index("head")
    ctx_n = lax.axis_size("ctx")
    query_count, query_width = queries.shape
    cache_rows, cache_width = cached_keys.shape
    heads_kv = cache_width // HEAD_DIM
    group_size = HEADS // KV_HEADS
    heads_here = heads_kv * group_size
    local_blocks = cache_rows // BLOCK
    qblocks = query_count // BLOCK

    local_block = pattern - shard_index * local_blocks
    in_shard = (local_block >= 0) & (local_block < local_blocks)
    slot_rank = jnp.cumsum(in_shard.astype(jnp.int32), axis=1) - 1
    slot_ids = jnp.arange(CAP, dtype=jnp.int32)
    picked = in_shard[:, :, None] & (slot_rank[:, :, None] == slot_ids[None, None, :])
    chosen = jnp.sum(jnp.where(picked, local_block[:, :, None], 0), axis=1).astype(jnp.int32)
    live = jnp.any(picked, axis=1).astype(jnp.int32)

    parts = heads_kv
    outs = [
        local_attention(queries, cached_keys, chosen, live, cached_values, part, 1)
        for part in range(parts)
    ]
    mixed_parts = [out[0] for out in outs]
    top = jnp.concatenate([out[1] for out in outs], axis=1)
    total = jnp.concatenate([out[2] for out in outs], axis=1)

    def by_row(stat):
        stat = stat.reshape(qblocks, heads_kv, group_size, BLOCK).transpose(0, 3, 1, 2)
        return stat.reshape(query_count, heads_here)

    stats = jnp.concatenate([by_row(top), by_row(total)], axis=1)
    rows_here = query_count // ctx_n
    own = lax.dynamic_slice_in_dim(stats, shard_index * rows_here, rows_here, axis=0)
    by_shift = [own]
    for shift in range(1, ctx_n):
        target = lax.rem(shard_index + shift, ctx_n)
        chunk = lax.dynamic_slice_in_dim(stats, target * rows_here, rows_here, axis=0)
        pairs = [(src, (src + shift) % ctx_n) for src in range(ctx_n)]
        by_shift.append(lax.ppermute(chunk, "ctx", perm=pairs))
    sources = lax.rem(shard_index - jnp.arange(ctx_n, dtype=jnp.int32) + ctx_n, ctx_n)
    got_stats = jnp.take(jnp.stack(by_shift), sources, axis=0)
    got_stats = got_stats.reshape(ctx_n, rows_here, 2, heads_here)
    got_top, got_total = got_stats[:, :, 0], got_stats[:, :, 1]
    row_peak = got_top.max(axis=0)
    rescale = jnp.exp(got_top - row_peak[None])
    row_norm = jnp.sum(got_total * rescale, axis=0)
    half_heads = heads_here // parts
    half_width = query_width // parts
    pieces = []
    for part, mixed in enumerate(mixed_parts):
        splits = 2 if part >= parts - 2 and half_heads % 2 == 0 else 1
        piece_heads = half_heads // splits
        for split in range(splits):
            first = part * half_heads + split * piece_heads
            columns = slice(split * piece_heads * HEAD_DIM, (split + 1) * piece_heads * HEAD_DIM)
            pieces.append((mixed if splits == 1 else mixed[:, columns], first, piece_heads))
    terms = []
    for mixed, first, piece_heads in pieces:
        heads = slice(first, first + piece_heads)
        piece_width = piece_heads * HEAD_DIM
        got_mixed = lax.all_to_all(mixed, "ctx", split_axis=0, concat_axis=0, tiled=True)
        got_mixed = got_mixed.reshape(ctx_n, -1, piece_heads, HEAD_DIM).astype(jnp.float32)
        summed = jnp.sum(got_mixed * rescale[:, :, heads, None], axis=0)
        attended = (summed / row_norm[:, heads, None]).reshape(rows_here, piece_width).astype(jnp.bfloat16)
        terms.append((lax.all_gather(attended, "ctx", axis=0, tiled=True),
                      out_weight[first * HEAD_DIM:first * HEAD_DIM + piece_width]))

    def project(columns):
        total_out = None
        for rows, weight in terms:
            term = jnp.dot(rows, columns(weight), preferred_element_type=jnp.float32)
            total_out = term if total_out is None else total_out + term
        return total_out

    heads_n = lax.axis_size("head")
    share = out_weight.shape[1] // heads_n
    if heads_n == 2:
        sent = project(lambda w: lax.dynamic_slice_in_dim(w, (1 - head_index) * share, share, axis=1))
        got = lax.ppermute(sent.astype(jnp.bfloat16), "head", perm=[(0, 1), (1, 0)])
        kept = project(lambda w: lax.dynamic_slice_in_dim(w, head_index * share, share, axis=1))
        return (kept + got.astype(jnp.float32)).astype(jnp.bfloat16)
    partial_out = project(lambda w: w)
    pieces = partial_out.reshape(query_count, heads_n, share).transpose(1, 0, 2)
    got = lax.all_to_all(pieces.astype(jnp.bfloat16), "head", 0, 0, tiled=True)
    return got.astype(jnp.float32).sum(axis=0).astype(jnp.bfloat16)


def solution(mesh):
    return jax.shard_map(
        shards,
        mesh=mesh,
        in_specs=(
            P(("groups", "rep"), "head"),
            P(("groups", "ctx"), "head"),
            P(("groups", "ctx"), "head"),
            P(("groups", "rep"), None),
            P("head", "ctx"),
        ),
        out_specs=P(("groups", "rep"), ("ctx", "head")),
        check_vma=False,
    )
```

```python
import functools

import jax
import jax.numpy as jnp
from jax import lax
from jax.experimental import pallas as pl
from jax.experimental.pallas import tpu as pltpu
from jax.sharding import PartitionSpec as P

HEADS = 64
KV_HEADS = 8
HEAD_DIM = 128
BLOCK = 128
CAP = 8


def attend_kernel(kv_first, chosen_ref, live_ref, q_ref, k_hbm, v_hbm, o_ref, m_ref, l_ref, kbuf, vbuf, sem):
    b = pl.program_id(0)
    steps = pl.num_programs(0)
    heads_kv = m_ref.shape[1]
    group_size = q_ref.shape[1] // (heads_kv * HEAD_DIM)

    cols = pl.ds(kv_first * HEAD_DIM, heads_kv * HEAD_DIM)

    def block_copies(step, slot):
        copies = []
        for j in range(CAP):
            rows = pl.ds(pl.multiple_of(chosen_ref[step, j] * BLOCK, BLOCK), BLOCK)
            dst = pl.ds(j * BLOCK, BLOCK)
            copies.append(pltpu.make_async_copy(k_hbm.at[rows, cols], kbuf.at[slot, dst], sem.at[slot, 0, j]))
            copies.append(pltpu.make_async_copy(v_hbm.at[rows, cols], vbuf.at[slot, dst], sem.at[slot, 1, j]))
        return copies

    slot = b % 2

    @pl.when(b == 0)
    def _():
        for c in block_copies(b, slot):
            c.start()

    @pl.when(b + 1 < steps)
    def _():
        for c in block_copies(b + 1, 1 - slot):
            c.start()

    for c in block_copies(b, slot):
        c.wait()

    key_slot = lax.broadcasted_iota(jnp.int32, (1, CAP * BLOCK), 1) // BLOCK
    live_keys = key_slot < 0
    for j in range(CAP):
        live_keys = live_keys | ((key_slot == j) & (live_ref[b, j] > 0))
    for kv in range(heads_kv):
        base = kv * group_size * HEAD_DIM
        stacked = jnp.concatenate(
            [q_ref[:, base + g * HEAD_DIM:base + (g + 1) * HEAD_DIM] for g in range(group_size)], axis=0
        )
        column = kv * HEAD_DIM
        keys = kbuf[slot, :, column:column + HEAD_DIM]
        scores = lax.dot_general(
            stacked, keys, (((1,), (1,)), ((), ())), preferred_element_type=jnp.float32
        ) * (HEAD_DIM ** (-0.5))
        scores = jnp.where(live_keys, scores, jnp.float32(-1e30))
        top = jnp.max(scores, axis=1, keepdims=True)
        weights = jnp.exp(scores - top)
        total = jnp.sum(weights, axis=1, keepdims=True)
        values = vbuf[slot, :, column:column + HEAD_DIM]
        mixed = jnp.dot(weights.astype(jnp.bfloat16), values, preferred_element_type=jnp.float32)
        for g in range(group_size):
            o_ref[:, base + g * HEAD_DIM:base + (g + 1) * HEAD_DIM] = (
                mixed[g * BLOCK:(g + 1) * BLOCK].astype(o_ref.dtype)
            )
        m_ref[0, kv] = jnp.transpose(jnp.broadcast_to(top, (top.shape[0], 128)))[0:1]
        l_ref[0, kv] = jnp.transpose(jnp.broadcast_to(total, (total.shape[0], 128)))[0:1]


def local_attention(queries, cached_keys, chosen, live, cached_values, kv_first, heads_kv):
    query_count = queries.shape[0]
    cache_width = cached_keys.shape[1]
    group_size = HEADS // KV_HEADS
    query_width = heads_kv * group_size * HEAD_DIM
    part = kv_first // heads_kv
    qblocks = query_count // BLOCK
    stat_shape = jax.ShapeDtypeStruct((qblocks, heads_kv, 1, group_size * BLOCK), jnp.float32)
    stat_spec = pl.BlockSpec((1, heads_kv, 1, group_size * BLOCK), lambda b, c, v: (b, 0, 0, 0))
    flops = 4 * query_count * heads_kv * group_size * CAP * BLOCK * HEAD_DIM
    return pl.pallas_call(
        functools.partial(attend_kernel, kv_first),
        out_shape=(jax.ShapeDtypeStruct((query_count, query_width), jnp.bfloat16), stat_shape, stat_shape),
        grid_spec=pltpu.PrefetchScalarGridSpec(
            num_scalar_prefetch=2,
            grid=(qblocks,),
            in_specs=[
                pl.BlockSpec((BLOCK, query_width), lambda b, c, v: (b, part)),
                pl.BlockSpec(memory_space=pl.ANY),
                pl.BlockSpec(memory_space=pl.ANY),
            ],
            out_specs=[pl.BlockSpec((BLOCK, query_width), lambda b, c, v: (b, 0)), stat_spec, stat_spec],
            scratch_shapes=[
                pltpu.VMEM((2, CAP * BLOCK, heads_kv * HEAD_DIM), jnp.bfloat16),
                pltpu.VMEM((2, CAP * BLOCK, heads_kv * HEAD_DIM), jnp.bfloat16),
                pltpu.SemaphoreType.DMA((2, 2, CAP)),
            ],
        ),
        compiler_params=pltpu.CompilerParams(dimension_semantics=("arbitrary",)),
        cost_estimate=pl.CostEstimate(
            flops=flops,
            transcendentals=query_count * heads_kv * group_size * CAP * BLOCK,
            bytes_accessed=2 * query_count * query_width + 4 * qblocks * CAP * BLOCK * heads_kv * HEAD_DIM,
        ),
    )(chosen, live, queries, cached_keys, cached_values)


def shards(queries, cached_keys, cached_values, pattern, out_weight):
    shard_index = lax.axis_index("ctx")
    head_index = lax.axis_index("head")
    ctx_n = lax.axis_size("ctx")
    query_count, query_width = queries.shape
    cache_rows, cache_width = cached_keys.shape
    heads_kv = cache_width // HEAD_DIM
    group_size = HEADS // KV_HEADS
    heads_here = heads_kv * group_size
    local_blocks = cache_rows // BLOCK
    qblocks = query_count // BLOCK

    local_block = pattern - shard_index * local_blocks
    in_shard = (local_block >= 0) & (local_block < local_blocks)
    slot_rank = jnp.cumsum(in_shard.astype(jnp.int32), axis=1) - 1
    slot_ids = jnp.arange(CAP, dtype=jnp.int32)
    picked = in_shard[:, :, None] & (slot_rank[:, :, None] == slot_ids[None, None, :])
    chosen = jnp.sum(jnp.where(picked, local_block[:, :, None], 0), axis=1).astype(jnp.int32)
    live = jnp.any(picked, axis=1).astype(jnp.int32)

    parts = heads_kv
    outs = [
        local_attention(queries, cached_keys, chosen, live, cached_values, part, 1)
        for part in range(parts)
    ]
    mixed_parts = [out[0] for out in outs]
    top = jnp.concatenate([out[1] for out in outs], axis=1)
    total = jnp.concatenate([out[2] for out in outs], axis=1)

    def by_row(stat):
        stat = stat.reshape(qblocks, heads_kv, group_size, BLOCK).transpose(0, 3, 1, 2)
        return stat.reshape(query_count, heads_here)

    stats = jnp.concatenate([by_row(top), by_row(total)], axis=1)
    rows_here = query_count // ctx_n
    own = lax.dynamic_slice_in_dim(stats, shard_index * rows_here, rows_here, axis=0)
    by_shift = [own]
    for shift in range(1, ctx_n):
        target = lax.rem(shard_index + shift, ctx_n)
        chunk = lax.dynamic_slice_in_dim(stats, target * rows_here, rows_here, axis=0)
        pairs = [(src, (src + shift) % ctx_n) for src in range(ctx_n)]
        by_shift.append(lax.ppermute(chunk, "ctx", perm=pairs))
    sources = lax.rem(shard_index - jnp.arange(ctx_n, dtype=jnp.int32) + ctx_n, ctx_n)
    got_stats = jnp.take(jnp.stack(by_shift), sources, axis=0)
    got_stats = got_stats.reshape(ctx_n, rows_here, 2, heads_here)
    got_top, got_total = got_stats[:, :, 0], got_stats[:, :, 1]
    row_peak = got_top.max(axis=0)
    rescale = jnp.exp(got_top - row_peak[None])
    row_norm = jnp.sum(got_total * rescale, axis=0)
    half_heads = heads_here // parts
    half_width = query_width // parts
    pieces = []
    merged = 2 if parts == 4 else 0
    if merged:
        pieces.append((jnp.concatenate(mixed_parts[:merged], axis=1), 0, merged * half_heads))
    for part, mixed in enumerate(mixed_parts):
        if part < merged:
            continue
        splits = 2 if part == parts - 1 and half_heads % 2 == 0 else 1
        piece_heads = half_heads // splits
        for split in range(splits):
            first = part * half_heads + split * piece_heads
            columns = slice(split * piece_heads * HEAD_DIM, (split + 1) * piece_heads * HEAD_DIM)
            pieces.append((mixed if splits == 1 else mixed[:, columns], first, piece_heads))
    terms = []
    for mixed, first, piece_heads in pieces:
        heads = slice(first, first + piece_heads)
        piece_width = piece_heads * HEAD_DIM
        got_mixed = lax.all_to_all(mixed, "ctx", split_axis=0, concat_axis=0, tiled=True)
        got_mixed = got_mixed.reshape(ctx_n, -1, piece_heads, HEAD_DIM).astype(jnp.float32)
        summed = jnp.sum(got_mixed * rescale[:, :, heads, None], axis=0)
        attended = (summed / row_norm[:, heads, None]).reshape(rows_here, piece_width).astype(jnp.bfloat16)
        terms.append((lax.all_gather(attended, "ctx", axis=0, tiled=True),
                      out_weight[first * HEAD_DIM:first * HEAD_DIM + piece_width]))

    def project(columns):
        total_out = None
        for rows, weight in terms:
            term = jnp.dot(rows, columns(weight), preferred_element_type=jnp.float32)
            total_out = term if total_out is None else total_out + term
        return total_out

    heads_n = lax.axis_size("head")
    share = out_weight.shape[1] // heads_n
    if heads_n == 2:
        sent = project(lambda w: lax.dynamic_slice_in_dim(w, (1 - head_index) * share, share, axis=1))
        got = lax.ppermute(sent.astype(jnp.bfloat16), "head", perm=[(0, 1), (1, 0)])
        kept = project(lambda w: lax.dynamic_slice_in_dim(w, head_index * share, share, axis=1))
        return (kept + got.astype(jnp.float32)).astype(jnp.bfloat16)
    partial_out = project(lambda w: w)
    pieces = partial_out.reshape(query_count, heads_n, share).transpose(1, 0, 2)
    got = lax.all_to_all(pieces.astype(jnp.bfloat16), "head", 0, 0, tiled=True)
    return got.astype(jnp.float32).sum(axis=0).astype(jnp.bfloat16)


def solution(mesh):
    return jax.shard_map(
        shards,
        mesh=mesh,
        in_specs=(
            P(("groups", "rep"), "head"),
            P(("groups", "ctx"), "head"),
            P(("groups", "ctx"), "head"),
            P(("groups", "rep"), None),
            P("head", "ctx"),
        ),
        out_specs=P(("groups", "rep"), ("ctx", "head")),
        check_vma=False,
    )
```

```python
import functools

import jax
import jax.numpy as jnp
from jax import lax
from jax.experimental import pallas as pl
from jax.experimental.pallas import tpu as pltpu
from jax.sharding import PartitionSpec as P

HEADS = 64
KV_HEADS = 8
HEAD_DIM = 128
BLOCK = 128
CAP = 8


def attend_kernel(kv_first, chosen_ref, live_ref, q_ref, k_hbm, v_hbm, o_ref, m_ref, l_ref, kbuf, vbuf, sem):
    b = pl.program_id(0)
    steps = pl.num_programs(0)
    heads_kv = m_ref.shape[1]
    group_size = q_ref.shape[1] // (heads_kv * HEAD_DIM)

    cols = pl.ds(kv_first * HEAD_DIM, heads_kv * HEAD_DIM)

    def block_copies(step, slot):
        copies = []
        for j in range(CAP):
            rows = pl.ds(pl.multiple_of(chosen_ref[step, j] * BLOCK, BLOCK), BLOCK)
            dst = pl.ds(j * BLOCK, BLOCK)
            copies.append(pltpu.make_async_copy(k_hbm.at[rows, cols], kbuf.at[slot, dst], sem.at[slot, 0, j]))
            copies.append(pltpu.make_async_copy(v_hbm.at[rows, cols], vbuf.at[slot, dst], sem.at[slot, 1, j]))
        return copies

    slot = b % 2

    @pl.when(b == 0)
    def _():
        for c in block_copies(b, slot):
            c.start()

    @pl.when(b + 1 < steps)
    def _():
        for c in block_copies(b + 1, 1 - slot):
            c.start()

    for c in block_copies(b, slot):
        c.wait()

    key_slot = lax.broadcasted_iota(jnp.int32, (1, CAP * BLOCK), 1) // BLOCK
    live_keys = key_slot < 0
    for j in range(CAP):
        live_keys = live_keys | ((key_slot == j) & (live_ref[b, j] > 0))
    for kv in range(heads_kv):
        base = kv * group_size * HEAD_DIM
        stacked = jnp.concatenate(
            [q_ref[:, base + g * HEAD_DIM:base + (g + 1) * HEAD_DIM] for g in range(group_size)], axis=0
        )
        column = kv * HEAD_DIM
        keys = kbuf[slot, :, column:column + HEAD_DIM]
        scores = lax.dot_general(
            stacked, keys, (((1,), (1,)), ((), ())), preferred_element_type=jnp.float32
        ) * (HEAD_DIM ** (-0.5))
        scores = jnp.where(live_keys, scores, jnp.float32(-1e30))
        top = jnp.max(scores, axis=1, keepdims=True)
        weights = jnp.exp(scores - top)
        total = jnp.sum(weights, axis=1, keepdims=True)
        values = vbuf[slot, :, column:column + HEAD_DIM]
        mixed = jnp.dot(weights.astype(jnp.bfloat16), values, preferred_element_type=jnp.float32)
        for g in range(group_size):
            o_ref[:, base + g * HEAD_DIM:base + (g + 1) * HEAD_DIM] = (
                mixed[g * BLOCK:(g + 1) * BLOCK].astype(o_ref.dtype)
            )
        m_ref[0, kv] = jnp.transpose(jnp.broadcast_to(top, (top.shape[0], 128)))[0:1]
        l_ref[0, kv] = jnp.transpose(jnp.broadcast_to(total, (total.shape[0], 128)))[0:1]


def local_attention(queries, cached_keys, chosen, live, cached_values, kv_first, heads_kv):
    query_count = queries.shape[0]
    cache_width = cached_keys.shape[1]
    group_size = HEADS // KV_HEADS
    query_width = heads_kv * group_size * HEAD_DIM
    part = kv_first // heads_kv
    qblocks = query_count // BLOCK
    stat_shape = jax.ShapeDtypeStruct((qblocks, heads_kv, 1, group_size * BLOCK), jnp.float32)
    stat_spec = pl.BlockSpec((1, heads_kv, 1, group_size * BLOCK), lambda b, c, v: (b, 0, 0, 0))
    flops = 4 * query_count * heads_kv * group_size * CAP * BLOCK * HEAD_DIM
    return pl.pallas_call(
        functools.partial(attend_kernel, kv_first),
        out_shape=(jax.ShapeDtypeStruct((query_count, query_width), jnp.bfloat16), stat_shape, stat_shape),
        grid_spec=pltpu.PrefetchScalarGridSpec(
            num_scalar_prefetch=2,
            grid=(qblocks,),
            in_specs=[
                pl.BlockSpec((BLOCK, query_width), lambda b, c, v: (b, part)),
                pl.BlockSpec(memory_space=pl.ANY),
                pl.BlockSpec(memory_space=pl.ANY),
            ],
            out_specs=[pl.BlockSpec((BLOCK, query_width), lambda b, c, v: (b, 0)), stat_spec, stat_spec],
            scratch_shapes=[
                pltpu.VMEM((2, CAP * BLOCK, heads_kv * HEAD_DIM), jnp.bfloat16),
                pltpu.VMEM((2, CAP * BLOCK, heads_kv * HEAD_DIM), jnp.bfloat16),
                pltpu.SemaphoreType.DMA((2, 2, CAP)),
            ],
        ),
        compiler_params=pltpu.CompilerParams(dimension_semantics=("arbitrary",)),
        cost_estimate=pl.CostEstimate(
            flops=flops,
            transcendentals=query_count * heads_kv * group_size * CAP * BLOCK,
            bytes_accessed=2 * query_count * query_width + 4 * qblocks * CAP * BLOCK * heads_kv * HEAD_DIM,
        ),
    )(chosen, live, queries, cached_keys, cached_values)


def shards(queries, cached_keys, cached_values, pattern, out_weight):
    shard_index = lax.axis_index("ctx")
    head_index = lax.axis_index("head")
    ctx_n = lax.axis_size("ctx")
    query_count, query_width = queries.shape
    cache_rows, cache_width = cached_keys.shape
    heads_kv = cache_width // HEAD_DIM
    group_size = HEADS // KV_HEADS
    heads_here = heads_kv * group_size
    local_blocks = cache_rows // BLOCK
    qblocks = query_count // BLOCK

    local_block = pattern - shard_index * local_blocks
    in_shard = (local_block >= 0) & (local_block < local_blocks)
    slot_rank = jnp.cumsum(in_shard.astype(jnp.int32), axis=1) - 1
    slot_ids = jnp.arange(CAP, dtype=jnp.int32)
    picked = in_shard[:, :, None] & (slot_rank[:, :, None] == slot_ids[None, None, :])
    chosen = jnp.sum(jnp.where(picked, local_block[:, :, None], 0), axis=1).astype(jnp.int32)
    live = jnp.any(picked, axis=1).astype(jnp.int32)

    parts = heads_kv
    outs = [
        local_attention(queries, cached_keys, chosen, live, cached_values, part, 1)
        for part in range(parts)
    ]
    mixed_parts = [out[0] for out in outs]
    top = jnp.concatenate([out[1] for out in outs], axis=1)
    total = jnp.concatenate([out[2] for out in outs], axis=1)

    def by_row(stat):
        stat = stat.reshape(qblocks, heads_kv, group_size, BLOCK).transpose(0, 3, 1, 2)
        return stat.reshape(query_count, heads_here)

    stats = jnp.concatenate([by_row(top), by_row(total)], axis=1)
    rows_here = query_count // ctx_n
    own = lax.dynamic_slice_in_dim(stats, shard_index * rows_here, rows_here, axis=0)
    by_shift = [own]
    for shift in range(1, ctx_n):
        target = lax.rem(shard_index + shift, ctx_n)
        chunk = lax.dynamic_slice_in_dim(stats, target * rows_here, rows_here, axis=0)
        pairs = [(src, (src + shift) % ctx_n) for src in range(ctx_n)]
        by_shift.append(lax.ppermute(chunk, "ctx", perm=pairs))
    sources = lax.rem(shard_index - jnp.arange(ctx_n, dtype=jnp.int32) + ctx_n, ctx_n)
    got_stats = jnp.take(jnp.stack(by_shift), sources, axis=0)
    got_stats = got_stats.reshape(ctx_n, rows_here, 2, heads_here)
    got_top, got_total = got_stats[:, :, 0], got_stats[:, :, 1]
    row_peak = got_top.max(axis=0)
    rescale = jnp.exp(got_top - row_peak[None])
    row_norm = jnp.sum(got_total * rescale, axis=0)
    half_heads = heads_here // parts
    half_width = query_width // parts
    pieces = []
    for part, mixed in enumerate(mixed_parts):
        splits = 2 if part == parts - 1 and half_heads % 2 == 0 else 1
        piece_heads = half_heads // splits
        for split in range(splits):
            first = part * half_heads + split * piece_heads
            columns = slice(split * piece_heads * HEAD_DIM, (split + 1) * piece_heads * HEAD_DIM)
            pieces.append((mixed if splits == 1 else mixed[:, columns], first, piece_heads))
    terms = []
    for mixed, first, piece_heads in pieces:
        heads = slice(first, first + piece_heads)
        piece_width = piece_heads * HEAD_DIM
        got_mixed = lax.all_to_all(mixed, "ctx", split_axis=0, concat_axis=0, tiled=True)
        got_mixed = got_mixed.reshape(ctx_n, -1, piece_heads, HEAD_DIM).astype(jnp.float32)
        summed = jnp.sum(got_mixed * rescale[:, :, heads, None], axis=0)
        attended = (summed / row_norm[:, heads, None]).reshape(rows_here, piece_width).astype(jnp.bfloat16)
        terms.append((lax.all_gather(attended, "ctx", axis=0, tiled=True),
                      out_weight[first * HEAD_DIM:first * HEAD_DIM + piece_width]))

    def project(columns):
        total_out = None
        for rows, weight in terms:
            term = jnp.dot(rows, columns(weight), preferred_element_type=jnp.float32)
            total_out = term if total_out is None else total_out + term
        return total_out

    heads_n = lax.axis_size("head")
    share = out_weight.shape[1] // heads_n
    if heads_n == 2:
        sent = project(lambda w: lax.dynamic_slice_in_dim(w, (1 - head_index) * share, share, axis=1))
        halves = [sent[:, :share // 2], sent[:, share // 2:]]
        got = jnp.concatenate(
            [lax.ppermute(half.astype(jnp.bfloat16), "head", perm=[(0, 1), (1, 0)]) for half in halves], axis=1
        )
        kept = project(lambda w: lax.dynamic_slice_in_dim(w, head_index * share, share, axis=1))
        return (kept + got.astype(jnp.float32)).astype(jnp.bfloat16)
    partial_out = project(lambda w: w)
    pieces = partial_out.reshape(query_count, heads_n, share).transpose(1, 0, 2)
    got = lax.all_to_all(pieces.astype(jnp.bfloat16), "head", 0, 0, tiled=True)
    return got.astype(jnp.float32).sum(axis=0).astype(jnp.bfloat16)


def solution(mesh):
    return jax.shard_map(
        shards,
        mesh=mesh,
        in_specs=(
            P(("groups", "rep"), "head"),
            P(("groups", "ctx"), "head"),
            P(("groups", "ctx"), "head"),
            P(("groups", "rep"), None),
            P("head", "ctx"),
        ),
        out_specs=P(("groups", "rep"), ("ctx", "head")),
        check_vma=False,
    )
```

```python
import functools

import jax
import jax.numpy as jnp
from jax import lax
from jax.experimental import pallas as pl
from jax.experimental.pallas import tpu as pltpu
from jax.sharding import PartitionSpec as P

HEADS = 64
KV_HEADS = 8
HEAD_DIM = 128
BLOCK = 128
CAP = 8


def attend_kernel(kv_first, chosen_ref, live_ref, q_ref, k_hbm, v_hbm, o_ref, m_ref, l_ref, kbuf, vbuf, sem):
    b = pl.program_id(0)
    steps = pl.num_programs(0)
    heads_kv = m_ref.shape[1]
    group_size = q_ref.shape[1] // (heads_kv * HEAD_DIM)

    cols = pl.ds(kv_first * HEAD_DIM, heads_kv * HEAD_DIM)

    def block_copies(step, slot):
        copies = []
        for j in range(CAP):
            rows = pl.ds(pl.multiple_of(chosen_ref[step, j] * BLOCK, BLOCK), BLOCK)
            dst = pl.ds(j * BLOCK, BLOCK)
            copies.append(pltpu.make_async_copy(k_hbm.at[rows, cols], kbuf.at[slot, dst], sem.at[slot, 0, j]))
            copies.append(pltpu.make_async_copy(v_hbm.at[rows, cols], vbuf.at[slot, dst], sem.at[slot, 1, j]))
        return copies

    slot = b % 2

    @pl.when(b == 0)
    def _():
        for c in block_copies(b, slot):
            c.start()

    @pl.when(b + 1 < steps)
    def _():
        for c in block_copies(b + 1, 1 - slot):
            c.start()

    for c in block_copies(b, slot):
        c.wait()

    key_slot = lax.broadcasted_iota(jnp.int32, (1, CAP * BLOCK), 1) // BLOCK
    live_keys = key_slot < 0
    for j in range(CAP):
        live_keys = live_keys | ((key_slot == j) & (live_ref[b, j] > 0))
    for kv in range(heads_kv):
        base = kv * group_size * HEAD_DIM
        stacked = jnp.concatenate(
            [q_ref[:, base + g * HEAD_DIM:base + (g + 1) * HEAD_DIM] for g in range(group_size)], axis=0
        )
        column = kv * HEAD_DIM
        keys = kbuf[slot, :, column:column + HEAD_DIM]
        scores = lax.dot_general(
            stacked, keys, (((1,), (1,)), ((), ())), preferred_element_type=jnp.float32
        ) * (HEAD_DIM ** (-0.5))
        scores = jnp.where(live_keys, scores, jnp.float32(-1e30))
        top = jnp.max(scores, axis=1, keepdims=True)
        weights = jnp.exp(scores - top)
        total = jnp.sum(weights, axis=1, keepdims=True)
        values = vbuf[slot, :, column:column + HEAD_DIM]
        mixed = jnp.dot(weights.astype(jnp.bfloat16), values, preferred_element_type=jnp.float32)
        for g in range(group_size):
            o_ref[:, base + g * HEAD_DIM:base + (g + 1) * HEAD_DIM] = (
                mixed[g * BLOCK:(g + 1) * BLOCK].astype(o_ref.dtype)
            )
        m_ref[0, kv] = jnp.transpose(jnp.broadcast_to(top, (top.shape[0], 128)))[0:1]
        l_ref[0, kv] = jnp.transpose(jnp.broadcast_to(total, (total.shape[0], 128)))[0:1]


def local_attention(queries, cached_keys, chosen, live, cached_values, kv_first, heads_kv):
    query_count = queries.shape[0]
    cache_width = cached_keys.shape[1]
    group_size = HEADS // KV_HEADS
    query_width = heads_kv * group_size * HEAD_DIM
    part = kv_first // heads_kv
    qblocks = query_count // BLOCK
    stat_shape = jax.ShapeDtypeStruct((qblocks, heads_kv, 1, group_size * BLOCK), jnp.float32)
    stat_spec = pl.BlockSpec((1, heads_kv, 1, group_size * BLOCK), lambda b, c, v: (b, 0, 0, 0))
    flops = 4 * query_count * heads_kv * group_size * CAP * BLOCK * HEAD_DIM
    return pl.pallas_call(
        functools.partial(attend_kernel, kv_first),
        out_shape=(jax.ShapeDtypeStruct((query_count, query_width), jnp.bfloat16), stat_shape, stat_shape),
        grid_spec=pltpu.PrefetchScalarGridSpec(
            num_scalar_prefetch=2,
            grid=(qblocks,),
            in_specs=[
                pl.BlockSpec((BLOCK, query_width), lambda b, c, v: (b, part)),
                pl.BlockSpec(memory_space=pl.ANY),
                pl.BlockSpec(memory_space=pl.ANY),
            ],
            out_specs=[pl.BlockSpec((BLOCK, query_width), lambda b, c, v: (b, 0)), stat_spec, stat_spec],
            scratch_shapes=[
                pltpu.VMEM((2, CAP * BLOCK, heads_kv * HEAD_DIM), jnp.bfloat16),
                pltpu.VMEM((2, CAP * BLOCK, heads_kv * HEAD_DIM), jnp.bfloat16),
                pltpu.SemaphoreType.DMA((2, 2, CAP)),
            ],
        ),
        compiler_params=pltpu.CompilerParams(dimension_semantics=("arbitrary",)),
        cost_estimate=pl.CostEstimate(
            flops=flops,
            transcendentals=query_count * heads_kv * group_size * CAP * BLOCK,
            bytes_accessed=2 * query_count * query_width + 4 * qblocks * CAP * BLOCK * heads_kv * HEAD_DIM,
        ),
    )(chosen, live, queries, cached_keys, cached_values)


def shards(queries, cached_keys, cached_values, pattern, out_weight):
    shard_index = lax.axis_index("ctx")
    head_index = lax.axis_index("head")
    ctx_n = lax.axis_size("ctx")
    query_count, query_width = queries.shape
    cache_rows, cache_width = cached_keys.shape
    heads_kv = cache_width // HEAD_DIM
    group_size = HEADS // KV_HEADS
    heads_here = heads_kv * group_size
    local_blocks = cache_rows // BLOCK
    qblocks = query_count // BLOCK

    local_block = pattern - shard_index * local_blocks
    in_shard = (local_block >= 0) & (local_block < local_blocks)
    slot_rank = jnp.cumsum(in_shard.astype(jnp.int32), axis=1) - 1
    slot_ids = jnp.arange(CAP, dtype=jnp.int32)
    picked = in_shard[:, :, None] & (slot_rank[:, :, None] == slot_ids[None, None, :])
    chosen = jnp.sum(jnp.where(picked, local_block[:, :, None], 0), axis=1).astype(jnp.int32)
    live = jnp.any(picked, axis=1).astype(jnp.int32)

    parts = heads_kv
    calls = [(0, parts - 1), (parts - 1, 1)] if parts > 1 else [(0, 1)]
    outs = [
        local_attention(queries, cached_keys, chosen, live, cached_values, first, count)
        for first, count in calls
    ]
    mixed_parts = []
    for out, (first, count) in zip(outs, calls):
        width = out[0].shape[1] // count
        mixed_parts += [out[0][:, index * width:(index + 1) * width] for index in range(count)]
    top = jnp.concatenate([out[1] for out in outs], axis=1)
    total = jnp.concatenate([out[2] for out in outs], axis=1)

    def by_row(stat):
        stat = stat.reshape(qblocks, heads_kv, group_size, BLOCK).transpose(0, 3, 1, 2)
        return stat.reshape(query_count, heads_here)

    stats = jnp.concatenate([by_row(top), by_row(total)], axis=1)
    rows_here = query_count // ctx_n
    own = lax.dynamic_slice_in_dim(stats, shard_index * rows_here, rows_here, axis=0)
    by_shift = [own]
    for shift in range(1, ctx_n):
        target = lax.rem(shard_index + shift, ctx_n)
        chunk = lax.dynamic_slice_in_dim(stats, target * rows_here, rows_here, axis=0)
        pairs = [(src, (src + shift) % ctx_n) for src in range(ctx_n)]
        by_shift.append(lax.ppermute(chunk, "ctx", perm=pairs))
    sources = lax.rem(shard_index - jnp.arange(ctx_n, dtype=jnp.int32) + ctx_n, ctx_n)
    got_stats = jnp.take(jnp.stack(by_shift), sources, axis=0)
    got_stats = got_stats.reshape(ctx_n, rows_here, 2, heads_here)
    got_top, got_total = got_stats[:, :, 0], got_stats[:, :, 1]
    row_peak = got_top.max(axis=0)
    rescale = jnp.exp(got_top - row_peak[None])
    row_norm = jnp.sum(got_total * rescale, axis=0)
    half_heads = heads_here // parts
    half_width = query_width // parts
    pieces = []
    for part, mixed in enumerate(mixed_parts):
        splits = 2 if part == parts - 1 and half_heads % 2 == 0 else 1
        piece_heads = half_heads // splits
        for split in range(splits):
            first = part * half_heads + split * piece_heads
            columns = slice(split * piece_heads * HEAD_DIM, (split + 1) * piece_heads * HEAD_DIM)
            pieces.append((mixed if splits == 1 else mixed[:, columns], first, piece_heads))
    terms = []
    for mixed, first, piece_heads in pieces:
        heads = slice(first, first + piece_heads)
        piece_width = piece_heads * HEAD_DIM
        got_mixed = lax.all_to_all(mixed, "ctx", split_axis=0, concat_axis=0, tiled=True)
        got_mixed = got_mixed.reshape(ctx_n, -1, piece_heads, HEAD_DIM).astype(jnp.float32)
        summed = jnp.sum(got_mixed * rescale[:, :, heads, None], axis=0)
        attended = (summed / row_norm[:, heads, None]).reshape(rows_here, piece_width).astype(jnp.bfloat16)
        terms.append((lax.all_gather(attended, "ctx", axis=0, tiled=True),
                      out_weight[first * HEAD_DIM:first * HEAD_DIM + piece_width]))

    def project(columns):
        total_out = None
        for rows, weight in terms:
            term = jnp.dot(rows, columns(weight), preferred_element_type=jnp.float32)
            total_out = term if total_out is None else total_out + term
        return total_out

    heads_n = lax.axis_size("head")
    share = out_weight.shape[1] // heads_n
    if heads_n == 2:
        sent = project(lambda w: lax.dynamic_slice_in_dim(w, (1 - head_index) * share, share, axis=1))
        got = lax.ppermute(sent.astype(jnp.bfloat16), "head", perm=[(0, 1), (1, 0)])
        kept = project(lambda w: lax.dynamic_slice_in_dim(w, head_index * share, share, axis=1))
        return (kept + got.astype(jnp.float32)).astype(jnp.bfloat16)
    partial_out = project(lambda w: w)
    pieces = partial_out.reshape(query_count, heads_n, share).transpose(1, 0, 2)
    got = lax.all_to_all(pieces.astype(jnp.bfloat16), "head", 0, 0, tiled=True)
    return got.astype(jnp.float32).sum(axis=0).astype(jnp.bfloat16)


def solution(mesh):
    return jax.shard_map(
        shards,
        mesh=mesh,
        in_specs=(
            P(("groups", "rep"), "head"),
            P(("groups", "ctx"), "head"),
            P(("groups", "ctx"), "head"),
            P(("groups", "rep"), None),
            P("head", "ctx"),
        ),
        out_specs=P(("groups", "rep"), ("ctx", "head")),
        check_vma=False,
    )
```
